32 devices in a mesh: node: 8 (over y, x, core), hub: 4 (over z).
Axes of the slice: x: 2, y: 2, z: 4, core: 2. Of those that a mesh axis runs over, the one named last changes fastest.
Arguments:
- seed_scores: bfloat16 [32768, 128], P(('node', 'hub')), may hold values from -10 to 10
- seed_mask: int32 [32768], P(('node', 'hub')), may hold values 0 or 1
- band_offsets: int32 [256, 10], P(('node', 'hub')), may hold values from -2 to 2
- band_tiles: bfloat16 [256, 10, 128, 128], P(('node', 'hub')), may hold values from 5e-05 to 1
- hub_blocks: int32 [256, 6], P(('node', 'hub')), may hold values from 0 to 31
- hub_tiles: bfloat16 [256, 6, 128, 128], P(('node', 'hub')), may hold values from 5e-05 to 1
- hub_rows: int32 [4096], P(('node', 'hub')), may hold values from 0 to 1023
Outputs:
- labels: float32 [32768, 128], P(('node', 'hub'))
The draws below stay inside these ranges and needn't reach their ends.
All inputs are finite; a program needn't handle non-finite values. No bound on the sum of `seed_mask` on one device may be relied on, other than what follows from the above.
Results may differ from the reference program's by a relative error of at most 0.00041.
Values may be sent and summed in bfloat16 or wider, within the bound.
No kernel may reach another device: no remote copies, remote signals or barrier semaphores. Data moves between devices by JAX's collectives and lax.ppermute only.
A program may use at most 64 MiB of HBM per device.

```python
import jax
import jax.numpy as jnp
from jax import lax

C = 128
BLK = 128
NB_DEV = 8
BW = 2
K_BAND = 10
HB = 6
H = 4096
ITERS = 3
ROWS_DEV = 1024
NBLK = 256
N = 32768
HBLK = 32
HUB_DEV = 128


def draw_seed_scores(key, part):
    first_key, second_key = jax.random.split(key)
    offsets = jnp.clip(jax.random.normal(first_key, (N // BLK, C), jnp.float32) * 1.5, -4.0, 4.0)
    noise = jnp.clip(jax.random.normal(second_key, (N, C), jnp.float32), -6.0, 6.0)
    return (jnp.repeat(offsets, BLK, axis=0) + noise).astype(jnp.bfloat16)


def sparse_weights(key, dimensions, fraction):
    row_key, entry_key = jax.random.split(key)
    row_dims = dimensions[:-1] + (1,)
    factor = jnp.exp(jax.random.uniform(row_key, row_dims, jnp.float32, -2.0, 0.0))
    uniforms = jax.random.uniform(entry_key, dimensions, jnp.float32, 0.0, 1.0)
    smaller = 0.0005 * jnp.exp(jnp.log(10.0) * jnp.clip((uniforms - fraction) / (1.0 - fraction), 0.0, 1.0))
    weights = jnp.where(uniforms < fraction, 1.0, smaller)
    return (factor * weights).astype(jnp.bfloat16)


def draw_band_tiles(key, part):
    return sparse_weights(jax.random.fold_in(key, 11), (NBLK, K_BAND, BLK, BLK), 1.0 / 80.0)


def draw_hub_tiles(key, part):
    return sparse_weights(jax.random.fold_in(key, 12), (NBLK, HB, BLK, BLK), 1.0 / 32.0)


def with_ends(drawn, stream_key, low, top_value):
    shape = drawn.shape
    place = [jax.random.randint(jax.random.fold_in(stream_key, axis), (), 0, shape[axis]) for axis in range(len(shape))]
    drawn = drawn.at[tuple(place)].set(low)
    longest = shape.index(max(shape))
    place[longest] = (place[longest] + 1) % shape[longest]
    return drawn.at[tuple(place)].set(top_value)


def setup_inputs(seed: int = 0) -> dict:
    key_of = jax.random.split(jax.random.key(seed), 8)
    return {
        "seed_scores": draw_seed_scores(jax.random.fold_in(key_of[7], 71), 0),
        "seed_mask": with_ends((jax.random.randint(key_of[1], (N,), 0, 2) < 1).astype(jnp.int32), jax.random.fold_in(key_of[1], 1), 0, 1),
        "band_offsets": with_ends(jax.random.randint(key_of[2], (NBLK, K_BAND), -BW, BW + 1), jax.random.fold_in(key_of[2], 1), -BW, BW).astype(jnp.int32),
        "band_tiles": draw_band_tiles(jax.random.fold_in(key_of[7], 71), 0),
        "hub_blocks": with_ends(jax.random.randint(key_of[4], (NBLK, HB), 0, HBLK), jax.random.fold_in(key_of[4], 1), 0, HBLK - 1).astype(jnp.int32),
        "hub_tiles": draw_hub_tiles(jax.random.fold_in(key_of[7], 71), 0),
        "hub_rows": with_ends(jax.random.randint(key_of[6], (H,), 0, ROWS_DEV), jax.random.fold_in(key_of[6], 1), 0, ROWS_DEV - 1).astype(jnp.int32),
    }


spread_weight = 0.8


def reference(seed_scores, seed_mask, band_offsets, band_tiles, hub_blocks, hub_tiles, hub_rows):
    seeds = seed_mask.astype(jnp.float32)[:, None] * seed_scores.astype(jnp.float32)
    owners = (jnp.arange(H, dtype=jnp.int32) // HUB_DEV) * (NB_DEV * BLK) + hub_rows
    groups = NBLK // NB_DEV
    labels = seeds
    for step in range(ITERS):
        current = labels.astype(jnp.bfloat16)
        blocked = current.reshape(NBLK, BLK, C)
        border = jnp.zeros((BW, BLK, C), jnp.bfloat16)
        padded = jnp.concatenate([border, blocked, border], 0)
        hub_labels = current[owners].reshape(HBLK, BLK, C)

        def one_group(group):
            first = group * NB_DEV
            tiles = lax.dynamic_slice_in_dim(band_tiles, first, NB_DEV, 0)
            offsets = lax.dynamic_slice_in_dim(band_offsets, first, NB_DEV, 0)
            htiles = lax.dynamic_slice_in_dim(hub_tiles, first, NB_DEV, 0)
            hindex = lax.dynamic_slice_in_dim(hub_blocks, first, NB_DEV, 0)
            neighbour = first + jnp.arange(NB_DEV, dtype=jnp.int32)[:, None] + BW + offsets
            near = padded[neighbour]
            tiles32 = tiles.astype(jnp.float32)
            htiles32 = htiles.astype(jnp.float32)
            band = jnp.einsum('bkij,bkjc->bic', tiles32, near.astype(jnp.float32))
            hubs = jnp.einsum('bhij,bhjc->bic', htiles32, hub_labels[hindex].astype(jnp.float32))
            degree = jnp.sum(tiles32, axis=(1, 3)) + jnp.sum(htiles32, axis=(1, 3))
            return (band + hubs) / degree[..., None]

        gathered = lax.map(one_group, jnp.arange(groups, dtype=jnp.int32)).reshape(N, C)
        labels = spread_weight * gathered + (1.0 - spread_weight) * seeds
    return labels
```

```python
import jax
import jax.numpy as jnp
import numpy as np
from jax import lax
from jax.sharding import PartitionSpec as P

BW = 2
ITERS = 3
AXES = ("node", "hub")
ROUNDS_32 = ((1, 2, 3), (8, 16, 24), (4,))


spread_weight = 0.8


def extended_2(block, sides, width):
    for axis, dim in sides:
        count = lax.axis_size(axis)
        forward = [(i, i + 1) for i in range(count - 1)]
        backward = [(target, source) for source, target in forward]
        low = lax.ppermute(
            lax.slice_in_dim(block, block.shape[dim] - width, None, axis=dim), axis, forward
        )
        high = lax.ppermute(lax.slice_in_dim(block, 0, width, axis=dim), axis, backward)
        block = jnp.concatenate([low, block, high], axis=dim)
    return block


def band_product(extended, tiles, offsets):
    neighbour = jnp.arange(offsets.shape[0], dtype=jnp.int32)[:, None] + BW + offsets
    return jnp.einsum(
        "bkij,bkjc->bic", tiles, extended[neighbour], preferred_element_type=jnp.float32
    )


def xor_rounds(count):
    if count == 32:
        return ROUNDS_32
    return None


def hub_gather(owned, block_rows, hub_blocks):
    count = lax.axis_size(AXES)
    rounds = xor_rounds(count)
    if rounds is None or owned.shape[0] != block_rows:
        hub_all = lax.all_gather(owned, AXES, axis=0, tiled=True)
        return hub_all.reshape(-1, block_rows, owned.shape[1]), hub_blocks
    me = lax.axis_index(AXES)
    buf = owned[None]
    offs = [0]
    for group in rounds:
        recvs = [lax.ppermute(buf, AXES, [(i, i ^ m) for i in range(count)]) for m in group]
        buf = jnp.concatenate([buf] + recvs, 0)
        offs = offs + [o ^ m for m in group for o in offs]
    assert sorted(offs) == list(range(count))
    where = np.zeros(count, np.int32)
    for p, o in enumerate(offs):
        where[o] = p
    return buf, jnp.asarray(where)[hub_blocks ^ me]


def body(seed_scores, seed_mask, band_offsets, band_tiles, hub_blocks, hub_tiles, hub_rows):
    blocks = band_offsets.shape[0]
    block_rows = band_tiles.shape[2]
    classes = seed_scores.shape[1]
    seeds = seed_mask.astype(jnp.float32)[:, None] * seed_scores.astype(jnp.float32)
    degree = jnp.sum(band_tiles, axis=(1, 3), dtype=jnp.float32) + jnp.sum(
        hub_tiles, axis=(1, 3), dtype=jnp.float32
    )
    rim_rows = BW * block_rows
    labels = seeds
    for step in range(ITERS):
        current = labels.astype(jnp.bfloat16)
        owned = current[hub_rows]
        hub_labels, hub_index = hub_gather(owned, block_rows, hub_blocks)
        hub_part = jnp.einsum(
            "bhij,bhjc->bic", hub_tiles, hub_labels[hub_index], preferred_element_type=jnp.float32
        )
        extended = extended_2(current, ((AXES, 0),), rim_rows)
        extended = extended.reshape(blocks + 2 * BW, block_rows, classes)
        band_part = band_product(extended, band_tiles, band_offsets)
        gathered = ((band_part + hub_part) / degree[..., None]).reshape(-1, classes)
        labels = spread_weight * gathered + (1.0 - spread_weight) * seeds
    return labels


def solution(mesh):
    placed = (
        P(AXES, None),
        P(AXES),
        P(AXES, None),
        P(AXES, None, None, None),
        P(AXES, None),
        P(AXES, None, None, None),
        P(AXES),
    )
    return jax.shard_map(
        body, mesh=mesh, in_specs=placed, out_specs=P(AXES, None), check_vma=False
    )
```

```python
import functools

import jax
import jax.numpy as jnp
import numpy as np
from jax import lax
from jax.experimental import pallas as pl
from jax.experimental.pallas import tpu as pltpu
from jax.sharding import PartitionSpec as P

BW = 2
ITERS = 3
AXES = ("node", "hub")
ROUNDS_32 = ((1, 2, 3), (8, 16, 24), (4,))


spread_weight = 0.8


def rims(block, width):
    count = lax.axis_size(AXES)
    forward = [(i, i + 1) for i in range(count - 1)]
    backward = [(target, source) for source, target in forward]
    low = lax.ppermute(lax.slice_in_dim(block, block.shape[0] - width, None, axis=0), AXES, forward)
    high = lax.ppermute(lax.slice_in_dim(block, 0, width, axis=0), AXES, backward)
    return low, high


def xor_rounds(count):
    if count == 32:
        return ROUNDS_32
    return None


def hub_gather(owned, block_rows, hub_blocks):
    count = lax.axis_size(AXES)
    rounds = xor_rounds(count)
    if rounds is None or owned.shape[0] != block_rows:
        hub_all = lax.all_gather(owned, AXES, axis=0, tiled=True)
        return [hub_all.reshape(-1, block_rows, owned.shape[1])], hub_blocks
    me = lax.axis_index(AXES)
    buf = owned[None]
    offs = [0]
    pieces = [buf]
    for r, group in enumerate(rounds):
        recvs = [lax.ppermute(buf, AXES, [(i, i ^ m) for i in range(count)]) for m in group]
        offs = offs + [o ^ m for m in group for o in offs]
        pieces = [buf] + recvs
        if r + 1 < len(rounds):
            buf = jnp.concatenate(pieces, 0)
    assert sorted(offs) == list(range(count))
    where = np.zeros(count, np.int32)
    for p, o in enumerate(offs):
        where[o] = p
    return pieces, jnp.asarray(where)[hub_blocks ^ me]


def spread_kernel(n_hub, off_ref, hidx_ref, cur_hbm, low_hbm, high_hbm, *rest):
    hub_hbm = rest[:n_hub]
    bt_hbm, ht_hbm, deg_ref, seeds_ref, out_ref, cur_out_ref, ext, hub, bt, ht, sem = rest[n_hub:]
    blocks, k_band, rows = bt.shape[0], bt.shape[1], bt.shape[2]
    k_hub = ht.shape[1]
    width = low_hbm.shape[0]
    own = cur_hbm.shape[0]
    copies = [
        pltpu.make_async_copy(low_hbm, ext.at[pl.ds(0, width)], sem.at[0]),
        pltpu.make_async_copy(cur_hbm, ext.at[pl.ds(width, own)], sem.at[1]),
        pltpu.make_async_copy(high_hbm, ext.at[pl.ds(width + own, width)], sem.at[2]),
    ]
    at = 0
    for i, piece in enumerate(hub_hbm):
        n = piece.shape[0]
        copies.append(pltpu.make_async_copy(piece, hub.at[pl.ds(at, n)], sem.at[3 + i]))
        at += n
    first = 3 + n_hub
    band_copies = [
        pltpu.make_async_copy(bt_hbm.at[b], bt.at[b], sem.at[first + b]) for b in range(blocks)
    ]
    hub_copies = [
        pltpu.make_async_copy(ht_hbm.at[b], ht.at[b], sem.at[first + blocks + b])
        for b in range(blocks)
    ]
    for b in range(blocks):
        band_copies[b].start()
        if b == 0:
            for c in copies:
                c.start()
        hub_copies[b].start()
    for c in copies:
        c.wait()
    for b in range(blocks):
        band_copies[b].wait()
        acc = jnp.zeros((rows, cur_out_ref.shape[1]), jnp.float32)
        for k in range(k_band):
            n = b + BW + off_ref[b * k_band + k]
            start = pl.multiple_of(n * rows, rows)
            acc = acc + jnp.dot(bt[b, k], ext[pl.ds(start, rows), :], preferred_element_type=jnp.float32)
        band = acc
        hub_copies[b].wait()
        acc = jnp.zeros_like(band)
        for h in range(k_hub):
            p = hidx_ref[b * k_hub + h]
            acc = acc + jnp.dot(ht[b, h], hub[p], preferred_element_type=jnp.float32)
        gathered = (band + acc) / deg_ref[pl.ds(b * rows, rows), :]
        labels = spread_weight * gathered + (1.0 - spread_weight) * seeds_ref[pl.ds(b * rows, rows), :]
        out_ref[pl.ds(b * rows, rows), :] = labels
        cur_out_ref[pl.ds(b * rows, rows), :] = labels.astype(cur_out_ref.dtype)


def spread(band_offsets, hub_index, current, low, high, hub_pieces, band_tiles, hub_tiles, degree, seeds):
    blocks, k_band, rows, _ = band_tiles.shape
    k_hub = hub_tiles.shape[1]
    classes = current.shape[1]
    n_hub_blocks = sum(p.shape[0] for p in hub_pieces)
    smem = pl.BlockSpec(memory_space=pltpu.SMEM)
    anyspace = pl.BlockSpec(memory_space=pl.ANY)
    vmem = pl.BlockSpec(memory_space=pltpu.VMEM)
    n_hub = len(hub_pieces)
    return pl.pallas_call(
        functools.partial(spread_kernel, n_hub),
        in_specs=[smem, smem] + [anyspace] * (3 + n_hub + 2) + [vmem, vmem],
        out_specs=[vmem, vmem],
        out_shape=[
            jax.ShapeDtypeStruct(seeds.shape, jnp.float32),
            jax.ShapeDtypeStruct(current.shape, current.dtype),
        ],
        scratch_shapes=[
            pltpu.VMEM((low.shape[0] + current.shape[0] + high.shape[0], classes), current.dtype),
            pltpu.VMEM((n_hub_blocks, rows, classes), current.dtype),
            pltpu.VMEM(band_tiles.shape, band_tiles.dtype),
            pltpu.VMEM(hub_tiles.shape, hub_tiles.dtype),
            pltpu.SemaphoreType.DMA((3 + n_hub + 2 * blocks,)),
        ],
    )(
        band_offsets.reshape(-1),
        hub_index.reshape(-1),
        current,
        low,
        high,
        *hub_pieces,
        band_tiles,
        hub_tiles,
        degree,
        seeds,
    )


def body(seed_scores, seed_mask, band_offsets, band_tiles, hub_blocks, hub_tiles, hub_rows):
    block_rows = band_tiles.shape[2]
    seeds = seed_mask.astype(jnp.float32)[:, None] * seed_scores.astype(jnp.float32)
    degree = jnp.sum(band_tiles, axis=(1, 3), dtype=jnp.float32) + jnp.sum(
        hub_tiles, axis=(1, 3), dtype=jnp.float32
    )
    degree = degree.reshape(-1, 1)
    rim_rows = BW * block_rows
    current = seeds.astype(jnp.bfloat16)
    for step in range(ITERS):
        owned = current[hub_rows]
        hub_pieces, hub_index = hub_gather(owned, block_rows, hub_blocks)
        low, high = rims(current, rim_rows)
        labels, current = spread(
            band_offsets, hub_index, current, low, high, hub_pieces, band_tiles, hub_tiles, degree, seeds
        )
    return labels


def solution(mesh):
    placed = (
        P(AXES, None),
        P(AXES),
        P(AXES, None),
        P(AXES, None, None, None),
        P(AXES, None),
        P(AXES, None, None, None),
        P(AXES),
    )
    return jax.shard_map(
        body, mesh=mesh, in_specs=placed, out_specs=P(AXES, None), check_vma=False
    )
```

```python
import functools

import jax
import jax.numpy as jnp
import numpy as np
from jax import lax
from jax.experimental import pallas as pl
from jax.experimental.pallas import tpu as pltpu
from jax.sharding import PartitionSpec as P

BW = 2
ITERS = 3
AXES = ("node", "hub")
ROUNDS_32 = ((1, 2, 3), (8, 16, 24), (4,))


spread_weight = 0.8


def rims(block, width):
    count = lax.axis_size(AXES)
    forward = [(i, i + 1) for i in range(count - 1)]
    backward = [(target, source) for source, target in forward]
    low = lax.ppermute(lax.slice_in_dim(block, block.shape[0] - width, None, axis=0), AXES, forward)
    high = lax.ppermute(lax.slice_in_dim(block, 0, width, axis=0), AXES, backward)
    return low, high


def xor_rounds(count):
    if count == 32:
        return ROUNDS_32
    return None


def hub_gather(owned, block_rows, hub_blocks):
    count = lax.axis_size(AXES)
    hub_all = lax.all_gather(owned, AXES, axis=0, tiled=True)
    return [hub_all.reshape(-1, block_rows, owned.shape[1])], hub_blocks


def exchange(current, owned, block_rows, hub_blocks, width):
    count = lax.axis_size(AXES)
    rounds = xor_rounds(count)
    if rounds is None or owned.shape[0] != block_rows or lax.axis_size("hub") != 4:
        hub_pieces, hub_index = hub_gather(owned, block_rows, hub_blocks)
        low, high = rims(current, width)
        return hub_pieces, hub_index, low, high
    me = lax.axis_index(AXES)
    z = lax.axis_index("hub")
    top = current[current.shape[0] - width:]
    bottom = current[:width]
    rim1 = jnp.where(z % 2 == 0, top, bottom)
    rim3 = jnp.where(z == 1, top, bottom)
    rimc = jnp.where(z == 3, top, bottom)
    pairs = lambda m: [(i, i ^ m) for i in range(count)]
    r1 = lax.ppermute(jnp.concatenate([owned, rim1], 0), AXES, pairs(1))
    r2 = lax.ppermute(owned, AXES, pairs(2))
    r3 = lax.ppermute(jnp.concatenate([owned, rim3], 0), AXES, pairs(3))
    groups = count // 4
    cross = [(4 * g + 3, 4 * g + 4) for g in range(groups - 1)]
    cross += [(4 * g + 4, 4 * g + 3) for g in range(groups - 1)]
    rc = lax.ppermute(rimc, AXES, cross)
    rows = owned.shape[0]
    low = jnp.where(z == 0, rc, jnp.where(z == 2, r3[rows:], r1[rows:]))
    high = jnp.where(z == 3, rc, jnp.where(z == 1, r3[rows:], r1[rows:]))
    pieces = [owned[None], r1[None, :rows], r2[None], r3[None, :rows]]
    offs = [0, 1, 2, 3]
    assert tuple(rounds[0]) == (1, 2, 3)
    buf = jnp.concatenate(pieces, 0)
    for r, group in enumerate(rounds[1:]):
        recvs = [lax.ppermute(buf, AXES, [(i, i ^ m) for i in range(count)]) for m in group]
        offs = offs + [o ^ m for m in group for o in offs]
        pieces = [buf] + recvs
        if r + 2 < len(rounds):
            buf = jnp.concatenate(pieces, 0)
    assert sorted(offs) == list(range(count))
    where = np.zeros(count, np.int32)
    for p, o in enumerate(offs):
        where[o] = p
    return pieces, jnp.asarray(where)[hub_blocks ^ me], low, high


def spread_kernel(n_hub, off_ref, hidx_ref, cur_hbm, low_hbm, high_hbm, *rest):
    hub_hbm = rest[:n_hub]
    bt_hbm, ht_hbm, deg_ref, seeds_ref, out_ref, cur_out_ref, ext, hub, bt, ht, sem = rest[n_hub:]
    blocks, k_band, rows = bt.shape[0], bt.shape[1], bt.shape[2]
    k_hub = ht.shape[1]
    width = low_hbm.shape[0]
    own = cur_hbm.shape[0]
    copies = [
        pltpu.make_async_copy(low_hbm, ext.at[pl.ds(0, width)], sem.at[0]),
        pltpu.make_async_copy(cur_hbm, ext.at[pl.ds(width, own)], sem.at[1]),
        pltpu.make_async_copy(high_hbm, ext.at[pl.ds(width + own, width)], sem.at[2]),
    ]
    at = 0
    for i, piece in enumerate(hub_hbm):
        n = piece.shape[0]
        copies.append(pltpu.make_async_copy(piece, hub.at[pl.ds(at, n)], sem.at[3 + i]))
        at += n
    first = 3 + n_hub
    band_copies = [
        pltpu.make_async_copy(bt_hbm.at[b], bt.at[b], sem.at[first + b]) for b in range(blocks)
    ]
    hub_copies = [
        pltpu.make_async_copy(ht_hbm.at[b], ht.at[b], sem.at[first + blocks + b])
        for b in range(blocks)
    ]
    for b in range(blocks):
        band_copies[b].start()
        if b == 0:
            for c in copies:
                c.start()
        hub_copies[b].start()
    for c in copies:
        c.wait()
    for b in range(blocks):
        band_copies[b].wait()
        acc = jnp.zeros((rows, cur_out_ref.shape[1]), jnp.float32)
        for k in range(k_band):
            n = b + BW + off_ref[b * k_band + k]
            start = pl.multiple_of(n * rows, rows)
            acc = acc + jnp.dot(bt[b, k], ext[pl.ds(start, rows), :], preferred_element_type=jnp.float32)
        band = acc
        hub_copies[b].wait()
        acc = jnp.zeros_like(band)
        for h in range(k_hub):
            p = hidx_ref[b * k_hub + h]
            acc = acc + jnp.dot(ht[b, h], hub[p], preferred_element_type=jnp.float32)
        gathered = (band + acc) / deg_ref[pl.ds(b * rows, rows), :]
        labels = spread_weight * gathered + (1.0 - spread_weight) * seeds_ref[pl.ds(b * rows, rows), :]
        out_ref[pl.ds(b * rows, rows), :] = labels
        cur_out_ref[pl.ds(b * rows, rows), :] = labels.astype(cur_out_ref.dtype)


def spread(band_offsets, hub_index, current, low, high, hub_pieces, band_tiles, hub_tiles, degree, seeds):
    blocks, k_band, rows, _ = band_tiles.shape
    k_hub = hub_tiles.shape[1]
    classes = current.shape[1]
    n_hub_blocks = sum(p.shape[0] for p in hub_pieces)
    smem = pl.BlockSpec(memory_space=pltpu.SMEM)
    anyspace = pl.BlockSpec(memory_space=pl.ANY)
    vmem = pl.BlockSpec(memory_space=pltpu.VMEM)
    n_hub = len(hub_pieces)
    return pl.pallas_call(
        functools.partial(spread_kernel, n_hub),
        in_specs=[smem, smem] + [anyspace] * (3 + n_hub + 2) + [vmem, vmem],
        out_specs=[vmem, vmem],
        out_shape=[
            jax.ShapeDtypeStruct(seeds.shape, jnp.float32),
            jax.ShapeDtypeStruct(current.shape, current.dtype),
        ],
        scratch_shapes=[
            pltpu.VMEM((low.shape[0] + current.shape[0] + high.shape[0], classes), current.dtype),
            pltpu.VMEM((n_hub_blocks, rows, classes), current.dtype),
            pltpu.VMEM(band_tiles.shape, band_tiles.dtype),
            pltpu.VMEM(hub_tiles.shape, hub_tiles.dtype),
            pltpu.SemaphoreType.DMA((3 + n_hub + 2 * blocks,)),
        ],
    )(
        band_offsets.reshape(-1),
        hub_index.reshape(-1),
        current,
        low,
        high,
        *hub_pieces,
        band_tiles,
        hub_tiles,
        degree,
        seeds,
    )


def body(seed_scores, seed_mask, band_offsets, band_tiles, hub_blocks, hub_tiles, hub_rows):
    block_rows = band_tiles.shape[2]
    seeds = seed_mask.astype(jnp.float32)[:, None] * seed_scores.astype(jnp.float32)
    degree = jnp.sum(band_tiles, axis=(1, 3), dtype=jnp.float32) + jnp.sum(
        hub_tiles, axis=(1, 3), dtype=jnp.float32
    )
    degree = degree.reshape(-1, 1)
    rim_rows = BW * block_rows
    current = seeds.astype(jnp.bfloat16)
    for step in range(ITERS):
        owned = current[hub_rows]
        hub_pieces, hub_index, low, high = exchange(current, owned, block_rows, hub_blocks, rim_rows)
        labels, current = spread(
            band_offsets, hub_index, current, low, high, hub_pieces, band_tiles, hub_tiles, degree, seeds
        )
    return labels


def solution(mesh):
    placed = (
        P(AXES, None),
        P(AXES),
        P(AXES, None),
        P(AXES, None, None, None),
        P(AXES, None),
        P(AXES, None, None, None),
        P(AXES),
    )
    return jax.shard_map(
        body, mesh=mesh, in_specs=placed, out_specs=P(AXES, None), check_vma=False
    )
```

```python
import functools

import jax
import jax.numpy as jnp
import numpy as np
from jax import lax
from jax.experimental import pallas as pl
from jax.experimental.pallas import tpu as pltpu
from jax.sharding import PartitionSpec as P

BW = 2
ITERS = 3
AXES = ("node", "hub")
ROUNDS_32 = ((1, 2, 3), (8, 16, 24), (4,))


spread_weight = 0.8

SMEM = pl.BlockSpec(memory_space=pltpu.SMEM)
ANY = pl.BlockSpec(memory_space=pl.ANY)
VMEM = pl.BlockSpec(memory_space=pltpu.VMEM)


def fast_path(owned, block_rows):
    count = lax.axis_size(AXES)
    return count == 32 and owned.shape[0] == block_rows and lax.axis_size("hub") == 4


def payloads(current, owned, z, width):
    top = current[current.shape[0] - width:]
    bottom = current[:width]
    p1 = jnp.concatenate([owned, jnp.where(z % 2 == 0, top, bottom)], 0)
    p3 = jnp.concatenate([owned, jnp.where(z == 1, top, bottom)], 0)
    pc = jnp.where(z == 3, top, bottom)
    return p1, p3, pc


def exchange(current, owned, p1, p3, pc, hub_blocks, width, block_rows, middle):
    count = lax.axis_size(AXES)
    if not fast_path(owned, block_rows):
        forward = [(i, i + 1) for i in range(count - 1)]
        backward = [(target, source) for source, target in forward]
        low = lax.ppermute(current[current.shape[0] - width:], AXES, forward)
        high = lax.ppermute(current[:width], AXES, backward)
        hub_all = lax.all_gather(owned, AXES, axis=0, tiled=True)
        return middle((low, high)), [hub_all.reshape(-1, block_rows, owned.shape[1])], hub_blocks
    me = lax.axis_index(AXES)
    pairs = lambda m: [(i, i ^ m) for i in range(count)]
    r1 = lax.ppermute(p1, AXES, pairs(1))
    r2 = lax.ppermute(owned, AXES, pairs(2))
    r3 = lax.ppermute(p3, AXES, pairs(3))
    groups = count // 4
    cross = [(4 * g + 3, 4 * g + 4) for g in range(groups - 1)]
    cross += [(4 * g + 4, 4 * g + 3) for g in range(groups - 1)]
    rc = lax.ppermute(pc, AXES, cross)
    rows = block_rows
    buf = jnp.concatenate([owned[None], r1[None, :rows], r2[None], r3[None, :rows]], 0)
    offs = [0, 1, 2, 3]
    rounds = ROUNDS_32
    pieces = [buf]
    done = None
    for r, group in enumerate(rounds[1:]):
        recvs = [lax.ppermute(buf, AXES, pairs(m)) for m in group]
        if done is None:
            done, recvs = lax.optimization_barrier((middle((r1, r3, rc)), recvs))
        offs = offs + [o ^ m for m in group for o in offs]
        pieces = [buf] + recvs
        if r + 2 < len(rounds):
            buf = jnp.concatenate(pieces, 0)
    assert sorted(offs) == list(range(count))
    where = np.zeros(count, np.int32)
    for p, o in enumerate(offs):
        where[o] = p
    return done, pieces, jnp.asarray(where)[hub_blocks ^ me]


def band_kernel(fast, n_own, z_ref, off_ref, cur_hbm, *rest):
    if fast:
        r1_hbm, r3_hbm, rc_hbm, bt_hbm, out_ref, ext, bt, sem = rest
    else:
        low_hbm, high_hbm, bt_hbm, out_ref, ext, bt, sem = rest
    blocks, k_band, rows = bt.shape[0], bt.shape[1], bt.shape[2]
    own = cur_hbm.shape[0]
    width = (ext.shape[0] - own) // 2
    low_dst = ext.at[pl.ds(0, width)]
    high_dst = ext.at[pl.ds(width + own, width)]
    mid = pltpu.make_async_copy(cur_hbm, ext.at[pl.ds(width, own)], sem.at[1])
    band_copies = [pltpu.make_async_copy(bt_hbm.at[b], bt.at[b], sem.at[3 + b]) for b in range(blocks)]
    band_copies[0].start()
    mid.start()
    if fast:
        z = z_ref[0]
        low_r1 = pltpu.make_async_copy(r1_hbm.at[pl.ds(n_own, width)], low_dst, sem.at[0])
        low_r3 = pltpu.make_async_copy(r3_hbm.at[pl.ds(n_own, width)], low_dst, sem.at[0])
        low_rc = pltpu.make_async_copy(rc_hbm, low_dst, sem.at[0])
        high_r1 = pltpu.make_async_copy(r1_hbm.at[pl.ds(n_own, width)], high_dst, sem.at[2])
        high_r3 = pltpu.make_async_copy(r3_hbm.at[pl.ds(n_own, width)], high_dst, sem.at[2])
        high_rc = pltpu.make_async_copy(rc_hbm, high_dst, sem.at[2])

        @pl.when(z == 0)
        def _():
            low_rc.start()
            high_r1.start()

        @pl.when(z == 1)
        def _():
            low_r1.start()
            high_r3.start()

        @pl.when(z == 2)
        def _():
            low_r3.start()
            high_r1.start()

        @pl.when(z == 3)
        def _():
            low_r1.start()
            high_rc.start()

        low_wait, high_wait = low_rc, high_rc
    else:
        low_wait = pltpu.make_async_copy(low_hbm, low_dst, sem.at[0])
        high_wait = pltpu.make_async_copy(high_hbm, high_dst, sem.at[2])
        low_wait.start()
        high_wait.start()
    for b in range(1, blocks):
        band_copies[b].start()
    mid.wait()
    low_wait.wait()
    high_wait.wait()
    for b in range(blocks):
        band_copies[b].wait()
        acc = jnp.zeros((rows, out_ref.shape[1]), jnp.float32)
        for k in range(k_band):
            n = b + BW + off_ref[b * k_band + k]
            start = pl.multiple_of(n * rows, rows)
            acc = acc + jnp.dot(bt[b, k], ext[pl.ds(start, rows), :], preferred_element_type=jnp.float32)
        out_ref[pl.ds(b * rows, rows), :] = acc


def band_call(z, band_offsets, current, rim_sources, band_tiles, fast, n_own, width):
    blocks, k_band, rows, _ = band_tiles.shape
    classes = current.shape[1]
    flops = 2 * blocks * k_band * rows * rows * classes
    bytes_accessed = band_tiles.size * 2 + current.size * 2 * 2 + current.size * 4
    return pl.pallas_call(
        functools.partial(band_kernel, fast, n_own),
        cost_estimate=pl.CostEstimate(flops=flops, transcendentals=0, bytes_accessed=bytes_accessed),
        in_specs=[SMEM, SMEM] + [ANY] * (1 + len(rim_sources) + 1),
        out_specs=VMEM,
        out_shape=jax.ShapeDtypeStruct(current.shape, jnp.float32),
        scratch_shapes=[
            pltpu.VMEM((current.shape[0] + 2 * width, classes), current.dtype),
            pltpu.VMEM(band_tiles.shape, band_tiles.dtype),
            pltpu.SemaphoreType.DMA((3 + blocks,)),
        ],
    )(z, band_offsets.reshape(-1), current, *rim_sources, band_tiles)


def hub_kernel(n_hub, width, z_ref, hidx_ref, rows_ref, *rest):
    hub_hbm = rest[:n_hub]
    (ht_hbm, band_ref, deg_ref, seeds_ref,
     out_ref, cur_ref, owned_ref, p1_ref, p3_ref, pc_ref,
     hub, ht, own32, sem) = rest[n_hub:]
    blocks, k_hub, rows = ht.shape[0], ht.shape[1], ht.shape[2]
    own = cur_ref.shape[0]
    n_own = owned_ref.shape[0]
    hub_copies = [pltpu.make_async_copy(ht_hbm.at[b], ht.at[b], sem.at[n_hub + b]) for b in range(blocks)]
    hub_copies[0].start()
    copies = []
    at = 0
    for i, piece in enumerate(hub_hbm):
        n = piece.shape[0]
        copies.append(pltpu.make_async_copy(piece, hub.at[pl.ds(at, n)], sem.at[i]))
        at += n
    for c in copies:
        c.start()
    for b in range(1, blocks):
        hub_copies[b].start()
    for c in copies:
        c.wait()
    for b in range(blocks):
        hub_copies[b].wait()
        acc = jnp.zeros((rows, out_ref.shape[1]), jnp.float32)
        for h in range(k_hub):
            p = hidx_ref[b * k_hub + h]
            acc = acc + jnp.dot(ht[b, h], hub[p], preferred_element_type=jnp.float32)
        gathered = (band_ref[pl.ds(b * rows, rows), :] + acc) / deg_ref[pl.ds(b * rows, rows), :]
        labels = spread_weight * gathered + (1.0 - spread_weight) * seeds_ref[pl.ds(b * rows, rows), :]
        out_ref[pl.ds(b * rows, rows), :] = labels
        cur_ref[pl.ds(b * rows, rows), :] = labels.astype(cur_ref.dtype)

    def pick(j, carry):
        own32[pl.ds(j, 1), :] = out_ref[pl.ds(rows_ref[j], 1), :]
        return carry

    lax.fori_loop(0, n_own, pick, 0)
    owned = own32[...].astype(owned_ref.dtype)
    owned_ref[...] = owned
    p1_ref[pl.ds(0, n_own), :] = owned
    p3_ref[pl.ds(0, n_own), :] = owned
    z = z_ref[0]
    top = cur_ref[pl.ds(own - width, width), :]
    bottom = cur_ref[pl.ds(0, width), :]
    p1_ref[pl.ds(n_own, width), :] = jnp.where(z % 2 == 0, top, bottom)
    p3_ref[pl.ds(n_own, width), :] = jnp.where(z == 1, top, bottom)
    pc_ref[...] = jnp.where(z == 3, top, bottom)


def hub_call(z, hub_index, hub_rows, hub_pieces, hub_tiles, band, degree, seeds, width):
    blocks, k_hub, rows, _ = hub_tiles.shape
    classes = seeds.shape[1]
    n_hub = len(hub_pieces)
    n_hub_blocks = sum(p.shape[0] for p in hub_pieces)
    n_own = hub_rows.shape[0]
    bf = jnp.bfloat16
    flops = 2 * blocks * k_hub * rows * rows * classes
    bytes_accessed = hub_tiles.size * 2 + n_hub_blocks * rows * classes * 2 + seeds.size * 4 * 4
    return pl.pallas_call(
        functools.partial(hub_kernel, n_hub, width),
        cost_estimate=pl.CostEstimate(flops=flops, transcendentals=0, bytes_accessed=bytes_accessed),
        in_specs=[SMEM, SMEM, SMEM] + [ANY] * (n_hub + 1) + [VMEM, VMEM, VMEM],
        out_specs=[VMEM] * 6,
        out_shape=[
            jax.ShapeDtypeStruct(seeds.shape, jnp.float32),
            jax.ShapeDtypeStruct(seeds.shape, bf),
            jax.ShapeDtypeStruct((n_own, classes), bf),
            jax.ShapeDtypeStruct((n_own + width, classes), bf),
            jax.ShapeDtypeStruct((n_own + width, classes), bf),
            jax.ShapeDtypeStruct((width, classes), bf),
        ],
        scratch_shapes=[
            pltpu.VMEM((n_hub_blocks, rows, classes), bf),
            pltpu.VMEM(hub_tiles.shape, hub_tiles.dtype),
            pltpu.VMEM((n_own, classes), jnp.float32),
            pltpu.SemaphoreType.DMA((n_hub + blocks,)),
        ],
    )(z, hub_index.reshape(-1), hub_rows, *hub_pieces, hub_tiles, band, degree, seeds)


def body(seed_scores, seed_mask, band_offsets, band_tiles, hub_blocks, hub_tiles, hub_rows):
    block_rows = band_tiles.shape[2]
    seeds = seed_mask.astype(jnp.float32)[:, None] * seed_scores.astype(jnp.float32)
    degree = jnp.sum(band_tiles, axis=(1, 3), dtype=jnp.float32) + jnp.sum(
        hub_tiles, axis=(1, 3), dtype=jnp.float32
    )
    degree = degree.reshape(-1, 1)
    width = BW * block_rows
    z = lax.axis_index("hub").astype(jnp.int32).reshape(1)
    current = seeds.astype(jnp.bfloat16)
    owned = current[hub_rows]
    p1, p3, pc = payloads(current, owned, z[0], width)
    fast = fast_path(owned, block_rows)
    for step in range(ITERS):
        middle = functools.partial(
            band_call, z, band_offsets, current, band_tiles=band_tiles, fast=fast, n_own=owned.shape[0], width=width
        )
        band, hub_pieces, hub_index = exchange(
            current, owned, p1, p3, pc, hub_blocks, width, block_rows, lambda rims: middle(rims)
        )
        labels, current, owned, p1, p3, pc = hub_call(
            z, hub_index, hub_rows, hub_pieces, hub_tiles, band, degree, seeds, width
        )
    return labels


def solution(mesh):
    placed = (
        P(AXES, None),
        P(AXES),
        P(AXES, None),
        P(AXES, None, None, None),
        P(AXES, None),
        P(AXES, None, None, None),
        P(AXES),
    )
    return jax.shard_map(
        body, mesh=mesh, in_specs=placed, out_specs=P(AXES, None), check_vma=False
    )
```

```python
import functools

import jax
import jax.numpy as jnp
import numpy as np
from jax import lax
from jax.experimental import pallas as pl
from jax.experimental.pallas import tpu as pltpu
from jax.sharding import PartitionSpec as P

BW = 2
ITERS = 3
AXES = ("node", "hub")
ROUNDS_32 = ((1, 2, 3), (8, 16, 24), (4,))


spread_weight = 0.8

SMEM = pl.BlockSpec(memory_space=pltpu.SMEM)
ANY = pl.BlockSpec(memory_space=pl.ANY)
VMEM = pl.BlockSpec(memory_space=pltpu.VMEM)


def rims(current, width):
    count = lax.axis_size(AXES)
    forward = [(i, i + 1) for i in range(count - 1)]
    backward = [(target, source) for source, target in forward]
    low = lax.ppermute(current[current.shape[0] - width:], AXES, forward)
    high = lax.ppermute(current[:width], AXES, backward)
    return low, high


def positions(hub_blocks, owned, block_rows):
    count = lax.axis_size(AXES)
    if count != 32 or owned.shape[0] != block_rows:
        return hub_blocks
    offs = [0]
    for group in ROUNDS_32:
        offs = offs + [o ^ m for m in group for o in offs]
    assert sorted(offs) == list(range(count))
    where = np.zeros(count, np.int32)
    for p, o in enumerate(offs):
        where[o] = p
    return jnp.asarray(where)[hub_blocks ^ lax.axis_index(AXES)]


def hub_exchange(owned, block_rows, middle, after=lambda done: done):
    count = lax.axis_size(AXES)
    classes = owned.shape[1]
    if count != 32 or owned.shape[0] != block_rows:
        done = after(middle())
        hub_all = lax.all_gather(owned, AXES, axis=0, tiled=True)
        return done, [hub_all]
    pairs = lambda m: [(i, i ^ m) for i in range(count)]
    buf = owned[None]
    done = None
    pieces = [buf]
    for r, group in enumerate(ROUNDS_32):
        recvs = [lax.ppermute(buf, AXES, pairs(m)) for m in group]
        if r == 0:
            done, recvs = lax.optimization_barrier((middle(), recvs))
        elif r == 1:
            done, recvs = lax.optimization_barrier((after(done), recvs))
        pieces = [buf] + recvs
        if r + 1 < len(ROUNDS_32):
            buf = jnp.concatenate(pieces, 0)
    return done, [p.reshape(-1, classes) for p in pieces]


def load_ext_hub(cur_hbm, low_hbm, high_hbm, hub_hbm, ext, hub, sem):
    width = low_hbm.shape[0]
    own = cur_hbm.shape[0]
    copies = [
        pltpu.make_async_copy(low_hbm, ext.at[pl.ds(0, width)], sem.at[0]),
        pltpu.make_async_copy(cur_hbm, ext.at[pl.ds(width, own)], sem.at[1]),
        pltpu.make_async_copy(high_hbm, ext.at[pl.ds(width + own, width)], sem.at[2]),
    ]
    at = 0
    for i, piece in enumerate(hub_hbm):
        n = piece.shape[0]
        copies.append(pltpu.make_async_copy(piece, hub.at[pl.ds(at, n)], sem.at[3 + i]))
        at += n
    return copies


def full_kernel(n_hub, off_ref, hidx_ref, cur_hbm, low_hbm, high_hbm, *rest):
    hub_hbm = rest[:n_hub]
    (bt_hbm, ht_hbm, deg_ref, seeds_ref, out_ref, cur_ref, top_ref, bottom_ref,
     ext, hub, bt, ht, sem) = rest[n_hub:]
    blocks, k_band, rows = bt.shape[0], bt.shape[1], bt.shape[2]
    k_hub = ht.shape[1]
    width = top_ref.shape[0]
    own = cur_ref.shape[0]
    copies = load_ext_hub(cur_hbm, low_hbm, high_hbm, hub_hbm, ext, hub, sem)
    first = 3 + n_hub
    band_copies = [pltpu.make_async_copy(bt_hbm.at[b], bt.at[b], sem.at[first + b]) for b in range(blocks)]
    hub_copies = [
        pltpu.make_async_copy(ht_hbm.at[b], ht.at[b], sem.at[first + blocks + b]) for b in range(blocks)
    ]
    band_copies[0].start()
    for c in copies:
        c.start()
    hub_copies[0].start()
    for b in range(1, blocks):
        band_copies[b].start()
        hub_copies[b].start()
    for c in copies:
        c.wait()
    for b in range(blocks):
        band_copies[b].wait()
        band = jnp.zeros((rows, cur_ref.shape[1]), jnp.float32)
        for k in range(k_band):
            n = b + BW + off_ref[b * k_band + k]
            start = pl.multiple_of(n * rows, rows)
            band = band + jnp.dot(bt[b, k], ext[pl.ds(start, rows), :], preferred_element_type=jnp.float32)
        hub_copies[b].wait()
        acc = jnp.zeros_like(band)
        for h in range(k_hub):
            start = pl.multiple_of(hidx_ref[b * k_hub + h] * rows, rows)
            acc = acc + jnp.dot(ht[b, h], hub[pl.ds(start, rows), :], preferred_element_type=jnp.float32)
        gathered = (band + acc) / deg_ref[pl.ds(b * rows, rows), :]
        labels = spread_weight * gathered + (1.0 - spread_weight) * seeds_ref[pl.ds(b * rows, rows), :]
        out_ref[pl.ds(b * rows, rows), :] = labels
        cur_ref[pl.ds(b * rows, rows), :] = labels.astype(cur_ref.dtype)
    top_ref[...] = cur_ref[pl.ds(own - width, width), :]
    bottom_ref[...] = cur_ref[pl.ds(0, width), :]


def full_call(band_offsets, hub_index, current, low, high, hub_pieces, band_tiles, hub_tiles, degree, seeds):
    blocks, k_band, rows, _ = band_tiles.shape
    classes = current.shape[1]
    width = low.shape[0]
    n_hub = len(hub_pieces)
    bf = current.dtype
    return pl.pallas_call(
        functools.partial(full_kernel, n_hub),
        in_specs=[SMEM, SMEM] + [ANY] * (3 + n_hub + 2) + [VMEM, VMEM],
        out_specs=[VMEM] * 4,
        out_shape=[
            jax.ShapeDtypeStruct(seeds.shape, jnp.float32),
            jax.ShapeDtypeStruct(current.shape, bf),
            jax.ShapeDtypeStruct((width, classes), bf),
            jax.ShapeDtypeStruct((width, classes), bf),
        ],
        scratch_shapes=[
            pltpu.VMEM((current.shape[0] + 2 * width, classes), bf),
            pltpu.VMEM((sum(p.shape[0] for p in hub_pieces), classes), bf),
            pltpu.VMEM(band_tiles.shape, band_tiles.dtype),
            pltpu.VMEM(hub_tiles.shape, hub_tiles.dtype),
            pltpu.SemaphoreType.DMA((3 + n_hub + 2 * blocks,)),
        ],
    )(
        band_offsets.reshape(-1), hub_index.reshape(-1), current, low, high, *hub_pieces,
        band_tiles, hub_tiles, degree, seeds,
    )


def early_kernel(n_hub, cur_hbm, low_hbm, high_hbm, *rest):
    hub_hbm = rest[:n_hub]
    rb_hi, rb_lo, rh_hi, rh_lo, deg_ref, seeds_ref, owned_ref, ext, hub, sem = rest[n_hub:]
    copies = load_ext_hub(cur_hbm, low_hbm, high_hbm, hub_hbm, ext, hub, sem)
    for c in copies:
        c.start()
    for c in copies:
        c.wait()
    f32 = jnp.float32
    band = jnp.dot(rb_hi[...], ext[...], preferred_element_type=f32) + jnp.dot(
        rb_lo[...], ext[...], preferred_element_type=f32
    )
    hubs = jnp.dot(rh_hi[...], hub[...], preferred_element_type=f32) + jnp.dot(
        rh_lo[...], hub[...], preferred_element_type=f32
    )
    gathered = (band + hubs) / deg_ref[...]
    labels = spread_weight * gathered + (1.0 - spread_weight) * seeds_ref[...]
    owned_ref[...] = labels.astype(owned_ref.dtype)


def early_call(current, low, high, hub_pieces, weights, deg_rows, seeds_rows):
    classes = current.shape[1]
    width = low.shape[0]
    n_hub = len(hub_pieces)
    bf = current.dtype
    return pl.pallas_call(
        functools.partial(early_kernel, n_hub),
        in_specs=[ANY] * (3 + n_hub) + [VMEM] * 6,
        out_specs=VMEM,
        out_shape=jax.ShapeDtypeStruct(seeds_rows.shape, bf),
        scratch_shapes=[
            pltpu.VMEM((current.shape[0] + 2 * width, classes), bf),
            pltpu.VMEM((sum(p.shape[0] for p in hub_pieces), classes), bf),
            pltpu.SemaphoreType.DMA((3 + n_hub,)),
        ],
    )(current, low, high, *hub_pieces, *weights, deg_rows, seeds_rows)


def split16(x):
    hi = x.astype(jnp.bfloat16)
    lo = (x - hi.astype(jnp.float32)).astype(jnp.bfloat16)
    return hi, lo


def row_weights(hub_rows, band_offsets, band_tiles, hub_tiles, hub_index, n_hub_blocks):
    blocks, k_band, rows, _ = band_tiles.shape
    b = hub_rows // rows
    i = hub_rows % rows
    hi = lax.Precision.HIGHEST
    band_rows = band_tiles[b, :, i, :].astype(jnp.float32)
    near = b[:, None] + BW + band_offsets[b]
    pick = (near[:, :, None] == jnp.arange(blocks + 2 * BW)[None, None, :]).astype(jnp.float32)
    rb = jnp.einsum("jkn,jkc->jnc", pick, band_rows, precision=hi).reshape(hub_rows.shape[0], -1)
    hub_rows_w = hub_tiles[b, :, i, :].astype(jnp.float32)
    where = hub_index[b]
    pick = (where[:, :, None] == jnp.arange(n_hub_blocks)[None, None, :]).astype(jnp.float32)
    rh = jnp.einsum("jhp,jhc->jpc", pick, hub_rows_w, precision=hi).reshape(hub_rows.shape[0], -1)
    return split16(rb) + split16(rh)


def send_rims(done):
    labels, current, top, bottom = done
    count = lax.axis_size(AXES)
    forward = [(i, i + 1) for i in range(count - 1)]
    backward = [(target, source) for source, target in forward]
    return labels, current, lax.ppermute(top, AXES, forward), lax.ppermute(bottom, AXES, backward)


def body(seed_scores, seed_mask, band_offsets, band_tiles, hub_blocks, hub_tiles, hub_rows):
    block_rows = band_tiles.shape[2]
    seeds = seed_mask.astype(jnp.float32)[:, None] * seed_scores.astype(jnp.float32)
    degree = jnp.sum(band_tiles, axis=(1, 3), dtype=jnp.float32) + jnp.sum(
        hub_tiles, axis=(1, 3), dtype=jnp.float32
    )
    degree = degree.reshape(-1, 1)
    width = BW * block_rows
    current = seeds.astype(jnp.bfloat16)
    owned = current[hub_rows]
    hub_index = positions(hub_blocks, owned, block_rows)
    n_hub_blocks = lax.axis_size(AXES) * owned.shape[0] // block_rows
    weights = row_weights(hub_rows, band_offsets, band_tiles, hub_tiles, hub_index, n_hub_blocks)
    deg_rows = degree[hub_rows]
    seeds_rows = seeds[hub_rows]
    low, high = rims(current, width)
    _, hub_pieces = hub_exchange(owned, block_rows, lambda: None)
    for step in range(ITERS - 1):
        owned = early_call(current, low, high, hub_pieces, weights, deg_rows, seeds_rows)
        full = functools.partial(
            full_call, band_offsets, hub_index, current, low, high, hub_pieces, band_tiles, hub_tiles,
            degree, seeds,
        )
        (labels, current, low, high), hub_pieces = hub_exchange(owned, block_rows, full, send_rims)
    labels, _, _, _ = full_call(
        band_offsets, hub_index, current, low, high, hub_pieces, band_tiles, hub_tiles, degree, seeds
    )
    return labels


def solution(mesh):
    placed = (
        P(AXES, None),
        P(AXES),
        P(AXES, None),
        P(AXES, None, None, None),
        P(AXES, None),
        P(AXES, None, None, None),
        P(AXES),
    )
    return jax.shard_map(
        body, mesh=mesh, in_specs=placed, out_specs=P(AXES, None), check_vma=False
    )
```

```python
import functools

import jax
import jax.numpy as jnp
import numpy as np
from jax import lax
from jax.experimental import pallas as pl
from jax.experimental.pallas import tpu as pltpu
from jax.sharding import PartitionSpec as P

BW = 2
ITERS = 3
AXES = ("node", "hub")
ROUNDS_32 = ((1, 2, 3), (8, 16, 24), (4,))


spread_weight = 0.8

SMEM = pl.BlockSpec(memory_space=pltpu.SMEM)
ANY = pl.BlockSpec(memory_space=pl.ANY)
VMEM = pl.BlockSpec(memory_space=pltpu.VMEM)


def fast_path(owned, block_rows):
    count = lax.axis_size(AXES)
    return count == 32 and owned.shape[0] == block_rows and lax.axis_size("hub") == 4


def payloads(current, owned, z, width):
    top = current[current.shape[0] - width:]
    bottom = current[:width]
    p1 = jnp.concatenate([owned, jnp.where(z % 2 == 0, top, bottom)], 0)
    p3 = jnp.concatenate([owned, jnp.where(z == 1, top, bottom)], 0)
    pc = jnp.where(z == 3, top, bottom)
    return p1, p3, pc


def exchange(current, owned, p1, p3, pc, hub_blocks, width, block_rows, middle):
    count = lax.axis_size(AXES)
    if not fast_path(owned, block_rows):
        forward = [(i, i + 1) for i in range(count - 1)]
        backward = [(target, source) for source, target in forward]
        low = lax.ppermute(current[current.shape[0] - width:], AXES, forward)
        high = lax.ppermute(current[:width], AXES, backward)
        hub_all = lax.all_gather(owned, AXES, axis=0, tiled=True)
        return middle((low, high)), [hub_all.reshape(-1, block_rows, owned.shape[1])], hub_blocks
    me = lax.axis_index(AXES)
    pairs = lambda m: [(i, i ^ m) for i in range(count)]
    r1 = lax.ppermute(p1, AXES, pairs(1))
    r2 = lax.ppermute(owned, AXES, pairs(2))
    r3 = lax.ppermute(p3, AXES, pairs(3))
    groups = count // 4
    cross = [(4 * g + 3, 4 * g + 4) for g in range(groups - 1)]
    cross += [(4 * g + 4, 4 * g + 3) for g in range(groups - 1)]
    rc = lax.ppermute(pc, AXES, cross)
    rows = block_rows
    buf = jnp.concatenate([owned[None], r1[None, :rows], r2[None], r3[None, :rows]], 0)
    offs = [0, 1, 2, 3]
    rounds = ROUNDS_32
    pieces = [buf]
    done = None
    for r, group in enumerate(rounds[1:]):
        recvs = [lax.ppermute(buf, AXES, pairs(m)) for m in group]
        if done is None:
            done, recvs = lax.optimization_barrier((middle((r1, r3, rc)), recvs))
        offs = offs + [o ^ m for m in group for o in offs]
        pieces = [buf] + recvs
        if r + 2 < len(rounds):
            buf = jnp.concatenate(pieces, 0)
    assert sorted(offs) == list(range(count))
    where = np.zeros(count, np.int32)
    for p, o in enumerate(offs):
        where[o] = p
    return done, pieces, jnp.asarray(where)[hub_blocks ^ me]


def band_kernel(fast, n_own, z_ref, off_ref, cur_hbm, *rest):
    if fast:
        r1_hbm, r3_hbm, rc_hbm, bt_hbm, out_ref, ext, bt, sem = rest
    else:
        low_hbm, high_hbm, bt_hbm, out_ref, ext, bt, sem = rest
    blocks, k_band, rows = bt.shape[0], bt.shape[1], bt.shape[2]
    own = cur_hbm.shape[0]
    width = (ext.shape[0] - own) // 2
    low_dst = ext.at[pl.ds(0, width)]
    high_dst = ext.at[pl.ds(width + own, width)]
    mid = pltpu.make_async_copy(cur_hbm, ext.at[pl.ds(width, own)], sem.at[1])
    band_copies = [pltpu.make_async_copy(bt_hbm.at[b], bt.at[b], sem.at[3 + b]) for b in range(blocks)]
    band_copies[0].start()
    mid.start()
    if fast:
        z = z_ref[0]
        low_r1 = pltpu.make_async_copy(r1_hbm.at[pl.ds(n_own, width)], low_dst, sem.at[0])
        low_r3 = pltpu.make_async_copy(r3_hbm.at[pl.ds(n_own, width)], low_dst, sem.at[0])
        low_rc = pltpu.make_async_copy(rc_hbm, low_dst, sem.at[0])
        high_r1 = pltpu.make_async_copy(r1_hbm.at[pl.ds(n_own, width)], high_dst, sem.at[2])
        high_r3 = pltpu.make_async_copy(r3_hbm.at[pl.ds(n_own, width)], high_dst, sem.at[2])
        high_rc = pltpu.make_async_copy(rc_hbm, high_dst, sem.at[2])

        @pl.when(z == 0)
        def _():
            low_rc.start()
            high_r1.start()

        @pl.when(z == 1)
        def _():
            low_r1.start()
            high_r3.start()

        @pl.when(z == 2)
        def _():
            low_r3.start()
            high_r1.start()

        @pl.when(z == 3)
        def _():
            low_r1.start()
            high_rc.start()

        low_wait, high_wait = low_rc, high_rc
    else:
        low_wait = pltpu.make_async_copy(low_hbm, low_dst, sem.at[0])
        high_wait = pltpu.make_async_copy(high_hbm, high_dst, sem.at[2])
        low_wait.start()
        high_wait.start()
    for b in range(1, blocks):
        band_copies[b].start()
    mid.wait()
    low_wait.wait()
    high_wait.wait()
    for b in range(blocks):
        band_copies[b].wait()
        acc = jnp.zeros((rows, out_ref.shape[1]), jnp.float32)
        for k in range(k_band):
            n = b + BW + off_ref[b * k_band + k]
            start = pl.multiple_of(n * rows, rows)
            acc = acc + jnp.dot(bt[b, k], ext[pl.ds(start, rows), :], preferred_element_type=jnp.float32)
        out_ref[pl.ds(b * rows, rows), :] = acc


def band_call(z, band_offsets, current, rim_sources, band_tiles, fast, n_own, width):
    blocks, k_band, rows, _ = band_tiles.shape
    classes = current.shape[1]
    flops = 2 * blocks * k_band * rows * rows * classes
    bytes_accessed = band_tiles.size * 2 + current.size * 2 * 2 + current.size * 4
    return pl.pallas_call(
        functools.partial(band_kernel, fast, n_own),
        cost_estimate=pl.CostEstimate(flops=flops, transcendentals=0, bytes_accessed=bytes_accessed),
        in_specs=[SMEM, SMEM] + [ANY] * (1 + len(rim_sources) + 1),
        out_specs=VMEM,
        out_shape=jax.ShapeDtypeStruct(current.shape, jnp.float32),
        scratch_shapes=[
            pltpu.VMEM((current.shape[0] + 2 * width, classes), current.dtype),
            pltpu.VMEM(band_tiles.shape, band_tiles.dtype),
            pltpu.SemaphoreType.DMA((3 + blocks,)),
        ],
    )(z, band_offsets.reshape(-1), current, *rim_sources, band_tiles)


def hub_kernel(n_hub, width, z_ref, hidx_ref, *rest):
    hub_hbm = rest[:n_hub]
    (ht_hbm, band_hbm, deg_hbm, seeds_hbm, pick_ref,
     out_ref, cur_ref, owned_ref, p1_ref, p3_ref, pc_ref,
     hub, ht, band, deg, seeds, sem) = rest[n_hub:]
    blocks, k_hub, rows = ht.shape[0], ht.shape[1], ht.shape[2]
    own = cur_ref.shape[0]
    n_own = owned_ref.shape[0]
    per_block = []
    for b in range(blocks):
        span = pl.ds(b * rows, rows)
        per_block.append([
            pltpu.make_async_copy(ht_hbm.at[b], ht.at[b], sem.at[n_hub + 4 * b]),
            pltpu.make_async_copy(band_hbm.at[span], band.at[span], sem.at[n_hub + 4 * b + 1]),
            pltpu.make_async_copy(deg_hbm.at[span], deg.at[span], sem.at[n_hub + 4 * b + 2]),
            pltpu.make_async_copy(seeds_hbm.at[span], seeds.at[span], sem.at[n_hub + 4 * b + 3]),
        ])
    for c in per_block[0]:
        c.start()
    copies = []
    at = 0
    for i, piece in enumerate(hub_hbm):
        n = piece.shape[0]
        copies.append(pltpu.make_async_copy(piece, hub.at[pl.ds(at, n)], sem.at[i]))
        at += n
    for c in copies:
        c.start()
    for b in range(1, blocks):
        for c in per_block[b]:
            c.start()
    for c in copies:
        c.wait()
    for b in range(blocks):
        for c in per_block[b]:
            c.wait()
        span = pl.ds(b * rows, rows)
        acc = jnp.zeros((rows, out_ref.shape[1]), jnp.float32)
        for h in range(k_hub):
            p = hidx_ref[b * k_hub + h]
            acc = acc + jnp.dot(ht[b, h], hub[p], preferred_element_type=jnp.float32)
        gathered = (band[span] + acc) / deg[span]
        labels = spread_weight * gathered + (1.0 - spread_weight) * seeds[span]
        out_ref[span, :] = labels
        cur_ref[span, :] = labels.astype(cur_ref.dtype)
    owned = jnp.dot(pick_ref[...], cur_ref[...], preferred_element_type=jnp.float32).astype(owned_ref.dtype)
    owned_ref[...] = owned
    p1_ref[pl.ds(0, n_own), :] = owned
    p3_ref[pl.ds(0, n_own), :] = owned
    z = z_ref[0]
    top = cur_ref[pl.ds(own - width, width), :]
    bottom = cur_ref[pl.ds(0, width), :]
    p1_ref[pl.ds(n_own, width), :] = jnp.where(z % 2 == 0, top, bottom)
    p3_ref[pl.ds(n_own, width), :] = jnp.where(z == 1, top, bottom)
    pc_ref[...] = jnp.where(z == 3, top, bottom)


def hub_call(z, hub_index, pick, hub_pieces, hub_tiles, band, degree, seeds, width):
    blocks, k_hub, rows, _ = hub_tiles.shape
    classes = seeds.shape[1]
    n_hub = len(hub_pieces)
    n_hub_blocks = sum(p.shape[0] for p in hub_pieces)
    n_own = pick.shape[0]
    bf = jnp.bfloat16
    flops = 2 * blocks * k_hub * rows * rows * classes
    bytes_accessed = hub_tiles.size * 2 + n_hub_blocks * rows * classes * 2 + seeds.size * 4 * 4
    return pl.pallas_call(
        functools.partial(hub_kernel, n_hub, width),
        cost_estimate=pl.CostEstimate(flops=flops, transcendentals=0, bytes_accessed=bytes_accessed),
        in_specs=[SMEM, SMEM] + [ANY] * (n_hub + 4) + [VMEM],
        out_specs=[VMEM] * 6,
        out_shape=[
            jax.ShapeDtypeStruct(seeds.shape, jnp.float32),
            jax.ShapeDtypeStruct(seeds.shape, bf),
            jax.ShapeDtypeStruct((n_own, classes), bf),
            jax.ShapeDtypeStruct((n_own + width, classes), bf),
            jax.ShapeDtypeStruct((n_own + width, classes), bf),
            jax.ShapeDtypeStruct((width, classes), bf),
        ],
        scratch_shapes=[
            pltpu.VMEM((n_hub_blocks, rows, classes), bf),
            pltpu.VMEM(hub_tiles.shape, hub_tiles.dtype),
            pltpu.VMEM(seeds.shape, jnp.float32),
            pltpu.VMEM(degree.shape, jnp.float32),
            pltpu.VMEM(seeds.shape, jnp.float32),
            pltpu.SemaphoreType.DMA((n_hub + 4 * blocks,)),
        ],
    )(z, hub_index.reshape(-1), *hub_pieces, hub_tiles, band, degree, seeds, pick)


def body(seed_scores, seed_mask, band_offsets, band_tiles, hub_blocks, hub_tiles, hub_rows):
    block_rows = band_tiles.shape[2]
    seeds = seed_mask.astype(jnp.float32)[:, None] * seed_scores.astype(jnp.float32)
    degree = jnp.sum(band_tiles, axis=(1, 3), dtype=jnp.float32) + jnp.sum(
        hub_tiles, axis=(1, 3), dtype=jnp.float32
    )
    degree = degree.reshape(-1, 1)
    width = BW * block_rows
    z = lax.axis_index("hub").astype(jnp.int32).reshape(1)
    current = seeds.astype(jnp.bfloat16)
    owned = current[hub_rows]
    p1, p3, pc = payloads(current, owned, z[0], width)
    fast = fast_path(owned, block_rows)
    pick = (hub_rows[:, None] == jnp.arange(current.shape[0], dtype=hub_rows.dtype)[None, :]).astype(jnp.bfloat16)
    for step in range(ITERS):
        middle = functools.partial(
            band_call, z, band_offsets, current, band_tiles=band_tiles, fast=fast, n_own=owned.shape[0], width=width
        )
        band, hub_pieces, hub_index = exchange(
            current, owned, p1, p3, pc, hub_blocks, width, block_rows, lambda rims: middle(rims)
        )
        labels, current, owned, p1, p3, pc = hub_call(
            z, hub_index, pick, hub_pieces, hub_tiles, band, degree, seeds, width
        )
    return labels


def solution(mesh):
    placed = (
        P(AXES, None),
        P(AXES),
        P(AXES, None),
        P(AXES, None, None, None),
        P(AXES, None),
        P(AXES, None, None, None),
        P(AXES),
    )
    return jax.shard_map(
        body, mesh=mesh, in_specs=placed, out_specs=P(AXES, None), check_vma=False
    )
```

```python
import functools

import jax
import jax.numpy as jnp
import numpy as np
from jax import lax
from jax.experimental import pallas as pl
from jax.experimental.pallas import tpu as pltpu
from jax.sharding import PartitionSpec as P

BW = 2
ITERS = 3
AXES = ("node", "hub")
ROUNDS_32 = ((1, 2, 3), (8, 16, 24), (4,))


spread_weight = 0.8

SMEM = pl.BlockSpec(memory_space=pltpu.SMEM)
ANY = pl.BlockSpec(memory_space=pl.ANY)
VMEM = pl.BlockSpec(memory_space=pltpu.VMEM)


def fast_path(owned, block_rows):
    count = lax.axis_size(AXES)
    return count == 32 and owned.shape[0] == block_rows and lax.axis_size("hub") == 4


def payloads(current, owned, z, width):
    top = current[current.shape[0] - width:]
    bottom = current[:width]
    p1 = jnp.concatenate([owned, jnp.where(z % 2 == 0, top, bottom)], 0)
    p3 = jnp.concatenate([owned, jnp.where(z == 1, top, bottom)], 0)
    pc = jnp.where(z == 3, top, bottom)
    return p1, p3, pc


def exchange(current, owned, p1, p3, pc, hub_blocks, width, block_rows, middle):
    count = lax.axis_size(AXES)
    if not fast_path(owned, block_rows):
        forward = [(i, i + 1) for i in range(count - 1)]
        backward = [(target, source) for source, target in forward]
        low = lax.ppermute(current[current.shape[0] - width:], AXES, forward)
        high = lax.ppermute(current[:width], AXES, backward)
        hub_all = lax.all_gather(owned, AXES, axis=0, tiled=True)
        return middle((low, high)), [hub_all.reshape(-1, block_rows, owned.shape[1])], hub_blocks
    me = lax.axis_index(AXES)
    pairs = lambda m: [(i, i ^ m) for i in range(count)]
    r3 = lax.ppermute(p3, AXES, pairs(3))
    r2 = lax.ppermute(owned, AXES, pairs(2))
    r1 = lax.ppermute(p1, AXES, pairs(1))
    groups = count // 4
    cross = [(4 * g + 3, 4 * g + 4) for g in range(groups - 1)]
    cross += [(4 * g + 4, 4 * g + 3) for g in range(groups - 1)]
    rc = lax.ppermute(pc, AXES, cross)
    rows = block_rows
    buf = jnp.concatenate([owned[None], r1[None, :rows], r2[None], r3[None, :rows]], 0)
    offs = [0, 1, 2, 3]
    rounds = ROUNDS_32
    pieces = [buf]
    done = None
    for r, group in enumerate(rounds[1:]):
        sent = {m: lax.ppermute(buf, AXES, pairs(m)) for m in sorted(group, key=lambda m: -m)}
        recvs = [sent[m] for m in group]
        if done is None:
            done, recvs = lax.optimization_barrier((middle((r1, r3, rc)), recvs))
        offs = offs + [o ^ m for m in group for o in offs]
        pieces = [buf] + recvs
        if r + 2 < len(rounds):
            buf = jnp.concatenate(pieces, 0)
    assert sorted(offs) == list(range(count))
    where = np.zeros(count, np.int32)
    for p, o in enumerate(offs):
        where[o] = p
    return done, pieces, jnp.asarray(where)[hub_blocks ^ me]


def band_kernel(fast, n_own, z_ref, off_ref, cur_hbm, *rest):
    if fast:
        r1_hbm, r3_hbm, rc_hbm, bt_hbm, out_ref, ext, bt, sem = rest
    else:
        low_hbm, high_hbm, bt_hbm, out_ref, ext, bt, sem = rest
    blocks, k_band, rows = bt.shape[0], bt.shape[1], bt.shape[2]
    own = cur_hbm.shape[0]
    width = (ext.shape[0] - own) // 2
    low_dst = ext.at[pl.ds(0, width)]
    high_dst = ext.at[pl.ds(width + own, width)]
    mid = pltpu.make_async_copy(cur_hbm, ext.at[pl.ds(width, own)], sem.at[1])
    band_copies = [pltpu.make_async_copy(bt_hbm.at[b], bt.at[b], sem.at[3 + b]) for b in range(blocks)]
    band_copies[0].start()
    mid.start()
    if fast:
        z = z_ref[0]
        low_r1 = pltpu.make_async_copy(r1_hbm.at[pl.ds(n_own, width)], low_dst, sem.at[0])
        low_r3 = pltpu.make_async_copy(r3_hbm.at[pl.ds(n_own, width)], low_dst, sem.at[0])
        low_rc = pltpu.make_async_copy(rc_hbm, low_dst, sem.at[0])
        high_r1 = pltpu.make_async_copy(r1_hbm.at[pl.ds(n_own, width)], high_dst, sem.at[2])
        high_r3 = pltpu.make_async_copy(r3_hbm.at[pl.ds(n_own, width)], high_dst, sem.at[2])
        high_rc = pltpu.make_async_copy(rc_hbm, high_dst, sem.at[2])

        @pl.when(z == 0)
        def _():
            low_rc.start()
            high_r1.start()

        @pl.when(z == 1)
        def _():
            low_r1.start()
            high_r3.start()

        @pl.when(z == 2)
        def _():
            low_r3.start()
            high_r1.start()

        @pl.when(z == 3)
        def _():
            low_r1.start()
            high_rc.start()

        low_wait, high_wait = low_rc, high_rc
    else:
        low_wait = pltpu.make_async_copy(low_hbm, low_dst, sem.at[0])
        high_wait = pltpu.make_async_copy(high_hbm, high_dst, sem.at[2])
        low_wait.start()
        high_wait.start()
    for b in range(1, blocks):
        band_copies[b].start()
    mid.wait()
    low_wait.wait()
    high_wait.wait()
    for b in range(blocks):
        band_copies[b].wait()
        acc = jnp.zeros((rows, out_ref.shape[1]), jnp.float32)
        for k in range(k_band):
            n = b + BW + off_ref[b * k_band + k]
            start = pl.multiple_of(n * rows, rows)
            acc = acc + jnp.dot(bt[b, k], ext[pl.ds(start, rows), :], preferred_element_type=jnp.float32)
        out_ref[pl.ds(b * rows, rows), :] = acc


def band_call(z, band_offsets, current, rim_sources, band_tiles, fast, n_own, width):
    blocks, k_band, rows, _ = band_tiles.shape
    classes = current.shape[1]
    flops = 2 * blocks * k_band * rows * rows * classes
    bytes_accessed = band_tiles.size * 2 + current.size * 2 * 2 + current.size * 4
    return pl.pallas_call(
        functools.partial(band_kernel, fast, n_own),
        cost_estimate=pl.CostEstimate(flops=flops, transcendentals=0, bytes_accessed=bytes_accessed),
        in_specs=[SMEM, SMEM] + [ANY] * (1 + len(rim_sources) + 1),
        out_specs=VMEM,
        out_shape=jax.ShapeDtypeStruct(current.shape, jnp.float32),
        scratch_shapes=[
            pltpu.VMEM((current.shape[0] + 2 * width, classes), current.dtype),
            pltpu.VMEM(band_tiles.shape, band_tiles.dtype),
            pltpu.SemaphoreType.DMA((3 + blocks,)),
        ],
    )(z, band_offsets.reshape(-1), current, *rim_sources, band_tiles)


def hub_kernel(n_hub, width, z_ref, hidx_ref, *rest):
    hub_hbm = rest[:n_hub]
    (ht_hbm, band_hbm, deg_hbm, seeds_hbm, pick_ref,
     out_ref, cur_ref, owned_ref, p1_ref, p3_ref, pc_ref,
     hub, ht, band, deg, seeds, sem) = rest[n_hub:]
    blocks, k_hub, rows = ht.shape[0], ht.shape[1], ht.shape[2]
    own = cur_ref.shape[0]
    n_own = owned_ref.shape[0]
    per_block = []
    for b in range(blocks):
        span = pl.ds(b * rows, rows)
        per_block.append([
            pltpu.make_async_copy(ht_hbm.at[b], ht.at[b], sem.at[n_hub + 4 * b]),
            pltpu.make_async_copy(band_hbm.at[span], band.at[span], sem.at[n_hub + 4 * b + 1]),
            pltpu.make_async_copy(deg_hbm.at[span], deg.at[span], sem.at[n_hub + 4 * b + 2]),
            pltpu.make_async_copy(seeds_hbm.at[span], seeds.at[span], sem.at[n_hub + 4 * b + 3]),
        ])
    for c in per_block[0]:
        c.start()
    copies = []
    at = 0
    for i, piece in enumerate(hub_hbm):
        n = piece.shape[0]
        copies.append(pltpu.make_async_copy(piece, hub.at[pl.ds(at, n)], sem.at[i]))
        at += n
    for c in copies:
        c.start()
    for b in range(1, blocks):
        for c in per_block[b]:
            c.start()
    for c in copies:
        c.wait()
    for b in range(blocks):
        for c in per_block[b]:
            c.wait()
        span = pl.ds(b * rows, rows)
        acc = jnp.zeros((rows, out_ref.shape[1]), jnp.float32)
        for h in range(k_hub):
            p = hidx_ref[b * k_hub + h]
            acc = acc + jnp.dot(ht[b, h], hub[p], preferred_element_type=jnp.float32)
        gathered = (band[span] + acc) / deg[span]
        labels = spread_weight * gathered + (1.0 - spread_weight) * seeds[span]
        out_ref[span, :] = labels
        cur_ref[span, :] = labels.astype(cur_ref.dtype)
    owned = jnp.dot(pick_ref[...], cur_ref[...], preferred_element_type=jnp.float32).astype(owned_ref.dtype)
    owned_ref[...] = owned
    p1_ref[pl.ds(0, n_own), :] = owned
    p3_ref[pl.ds(0, n_own), :] = owned
    z = z_ref[0]
    top = cur_ref[pl.ds(own - width, width), :]
    bottom = cur_ref[pl.ds(0, width), :]
    p1_ref[pl.ds(n_own, width), :] = jnp.where(z % 2 == 0, top, bottom)
    p3_ref[pl.ds(n_own, width), :] = jnp.where(z == 1, top, bottom)
    pc_ref[...] = jnp.where(z == 3, top, bottom)


def hub_call(z, hub_index, pick, hub_pieces, hub_tiles, band, degree, seeds, width):
    blocks, k_hub, rows, _ = hub_tiles.shape
    classes = seeds.shape[1]
    n_hub = len(hub_pieces)
    n_hub_blocks = sum(p.shape[0] for p in hub_pieces)
    n_own = pick.shape[0]
    bf = jnp.bfloat16
    flops = 2 * blocks * k_hub * rows * rows * classes
    bytes_accessed = hub_tiles.size * 2 + n_hub_blocks * rows * classes * 2 + seeds.size * 4 * 4
    return pl.pallas_call(
        functools.partial(hub_kernel, n_hub, width),
        cost_estimate=pl.CostEstimate(flops=flops, transcendentals=0, bytes_accessed=bytes_accessed),
        in_specs=[SMEM, SMEM] + [ANY] * (n_hub + 4) + [VMEM],
        out_specs=[VMEM] * 6,
        out_shape=[
            jax.ShapeDtypeStruct(seeds.shape, jnp.float32),
            jax.ShapeDtypeStruct(seeds.shape, bf),
            jax.ShapeDtypeStruct((n_own, classes), bf),
            jax.ShapeDtypeStruct((n_own + width, classes), bf),
            jax.ShapeDtypeStruct((n_own + width, classes), bf),
            jax.ShapeDtypeStruct((width, classes), bf),
        ],
        scratch_shapes=[
            pltpu.VMEM((n_hub_blocks, rows, classes), bf),
            pltpu.VMEM(hub_tiles.shape, hub_tiles.dtype),
            pltpu.VMEM(seeds.shape, jnp.float32),
            pltpu.VMEM(degree.shape, jnp.float32),
            pltpu.VMEM(seeds.shape, jnp.float32),
            pltpu.SemaphoreType.DMA((n_hub + 4 * blocks,)),
        ],
    )(z, hub_index.reshape(-1), *hub_pieces, hub_tiles, band, degree, seeds, pick)


def body(seed_scores, seed_mask, band_offsets, band_tiles, hub_blocks, hub_tiles, hub_rows):
    block_rows = band_tiles.shape[2]
    seeds = seed_mask.astype(jnp.float32)[:, None] * seed_scores.astype(jnp.float32)
    degree = jnp.sum(band_tiles, axis=(1, 3), dtype=jnp.float32) + jnp.sum(
        hub_tiles, axis=(1, 3), dtype=jnp.float32
    )
    degree = degree.reshape(-1, 1)
    width = BW * block_rows
    z = lax.axis_index("hub").astype(jnp.int32).reshape(1)
    current = seeds.astype(jnp.bfloat16)
    owned = current[hub_rows]
    p1, p3, pc = payloads(current, owned, z[0], width)
    fast = fast_path(owned, block_rows)
    pick = (hub_rows[:, None] == jnp.arange(current.shape[0], dtype=hub_rows.dtype)[None, :]).astype(jnp.bfloat16)
    for step in range(ITERS):
        middle = functools.partial(
            band_call, z, band_offsets, current, band_tiles=band_tiles, fast=fast, n_own=owned.shape[0], width=width
        )
        band, hub_pieces, hub_index = exchange(
            current, owned, p1, p3, pc, hub_blocks, width, block_rows, lambda rims: middle(rims)
        )
        labels, current, owned, p1, p3, pc = hub_call(
            z, hub_index, pick, hub_pieces, hub_tiles, band, degree, seeds, width
        )
    return labels


def solution(mesh):
    placed = (
        P(AXES, None),
        P(AXES),
        P(AXES, None),
        P(AXES, None, None, None),
        P(AXES, None),
        P(AXES, None, None, None),
        P(AXES),
    )
    return jax.shard_map(
        body, mesh=mesh, in_specs=placed, out_specs=P(AXES, None), check_vma=False
    )
```

```python
import functools

import jax
import jax.numpy as jnp
import numpy as np
from jax import lax
from jax.experimental import pallas as pl
from jax.experimental.pallas import tpu as pltpu
from jax.sharding import PartitionSpec as P

BW = 2
ITERS = 3
AXES = ("node", "hub")
ROUNDS_32 = ((1, 2, 3), (8, 16, 24), (4,))


spread_weight = 0.8

SMEM = pl.BlockSpec(memory_space=pltpu.SMEM)
ANY = pl.BlockSpec(memory_space=pltpu.HBM)
VMEM = pl.BlockSpec(memory_space=pltpu.VMEM)


def fast_path(owned, block_rows):
    count = lax.axis_size(AXES)
    return count == 32 and owned.shape[0] == block_rows and lax.axis_size("hub") == 4


def payloads(current, owned, z, width):
    top = current[current.shape[0] - width:]
    bottom = current[:width]
    p1 = jnp.concatenate([owned, jnp.where(z % 2 == 0, top, bottom)], 0)
    p3 = jnp.concatenate([owned, jnp.where(z == 1, top, bottom)], 0)
    pc = jnp.where(z == 3, top, bottom)
    return p1, p3, pc


def exchange(current, owned, p1, p3, pc, hub_blocks, width, block_rows, middle, prep):
    count = lax.axis_size(AXES)
    if not fast_path(owned, block_rows):
        forward = [(i, i + 1) for i in range(count - 1)]
        backward = [(target, source) for source, target in forward]
        low = lax.ppermute(current[current.shape[0] - width:], AXES, forward)
        high = lax.ppermute(current[:width], AXES, backward)
        hub_all = lax.all_gather(owned, AXES, axis=0, tiled=True)
        return middle((low, high)), [hub_all.reshape(-1, block_rows, owned.shape[1])], hub_blocks, prep
    me = lax.axis_index(AXES)
    pairs = lambda m: [(i, i ^ m) for i in range(count)]
    r3 = lax.ppermute(p3, AXES, pairs(3))
    r2 = lax.ppermute(owned, AXES, pairs(2))
    r1 = lax.ppermute(p1, AXES, pairs(1))
    groups = count // 4
    cross = [(4 * g + 3, 4 * g + 4) for g in range(groups - 1)]
    cross += [(4 * g + 4, 4 * g + 3) for g in range(groups - 1)]
    rc = lax.ppermute(pc, AXES, cross)
    if prep is not None:
        (r1, r2, r3, rc), prep = lax.optimization_barrier(((r1, r2, r3, rc), prep))
    rows = block_rows
    buf = jnp.concatenate([owned[None], r1[None, :rows], r2[None], r3[None, :rows]], 0)
    offs = [0, 1, 2, 3]
    assert ROUNDS_32[0] == (1, 2, 3) and len(ROUNDS_32) == 3 and len(ROUNDS_32[2]) == 1
    group = ROUNDS_32[1]
    sent = {m: lax.ppermute(buf, AXES, pairs(m)) for m in sorted(group, key=lambda m: -m)}
    recvs = [sent[m] for m in group]
    done, recvs = lax.optimization_barrier((middle((r1, r3, rc)), recvs))
    offs = offs + [o ^ m for m in group for o in offs]
    rest = jnp.concatenate(recvs, 0)
    last = ROUNDS_32[2][0]
    pieces = [buf, rest, lax.ppermute(buf, AXES, pairs(last)), lax.ppermute(rest, AXES, pairs(last))]
    offs = offs + [o ^ last for o in offs]
    assert sorted(offs) == list(range(count))
    where = np.zeros(count, np.int32)
    for p, o in enumerate(offs):
        where[o] = p
    return done, pieces, jnp.asarray(where)[hub_blocks ^ me], prep


def band_kernel(fast, n_own, z_ref, off_ref, cur_hbm, *rest):
    if fast:
        r1_hbm, r3_hbm, rc_hbm, bt_hbm, out_ref, ext, bt, sem = rest
    else:
        low_hbm, high_hbm, bt_hbm, out_ref, ext, bt, sem = rest
    blocks, k_band, rows = bt.shape[0], bt.shape[1], bt.shape[2]
    own = cur_hbm.shape[0]
    width = (ext.shape[0] - own) // 2
    low_dst = ext.at[pl.ds(0, width)]
    high_dst = ext.at[pl.ds(width + own, width)]
    mid = pltpu.make_async_copy(cur_hbm, ext.at[pl.ds(width, own)], sem.at[1])
    band_copies = [pltpu.make_async_copy(bt_hbm.at[b], bt.at[b], sem.at[3 + b]) for b in range(blocks)]
    band_copies[0].start()
    mid.start()
    if fast:
        z = z_ref[0]
        low_r1 = pltpu.make_async_copy(r1_hbm.at[pl.ds(n_own, width)], low_dst, sem.at[0])
        low_r3 = pltpu.make_async_copy(r3_hbm.at[pl.ds(n_own, width)], low_dst, sem.at[0])
        low_rc = pltpu.make_async_copy(rc_hbm, low_dst, sem.at[0])
        high_r1 = pltpu.make_async_copy(r1_hbm.at[pl.ds(n_own, width)], high_dst, sem.at[2])
        high_r3 = pltpu.make_async_copy(r3_hbm.at[pl.ds(n_own, width)], high_dst, sem.at[2])
        high_rc = pltpu.make_async_copy(rc_hbm, high_dst, sem.at[2])

        @pl.when(z == 0)
        def _():
            low_rc.start()
            high_r1.start()

        @pl.when(z == 1)
        def _():
            low_r1.start()
            high_r3.start()

        @pl.when(z == 2)
        def _():
            low_r3.start()
            high_r1.start()

        @pl.when(z == 3)
        def _():
            low_r1.start()
            high_rc.start()

        low_wait, high_wait = low_rc, high_rc
    else:
        low_wait = pltpu.make_async_copy(low_hbm, low_dst, sem.at[0])
        high_wait = pltpu.make_async_copy(high_hbm, high_dst, sem.at[2])
        low_wait.start()
        high_wait.start()
    for b in range(1, blocks):
        band_copies[b].start()
    mid.wait()
    low_wait.wait()
    high_wait.wait()
    for b in range(blocks):
        band_copies[b].wait()
        acc = jnp.zeros((rows, out_ref.shape[1]), jnp.float32)
        for k in range(k_band):
            n = b + BW + off_ref[b * k_band + k]
            start = pl.multiple_of(n * rows, rows)
            acc = acc + jnp.dot(bt[b, k], ext[pl.ds(start, rows), :], preferred_element_type=jnp.float32)
        out_ref[pl.ds(b * rows, rows), :] = acc


def band_call(z, band_offsets, current, rim_sources, band_tiles, fast, n_own, width):
    blocks, k_band, rows, _ = band_tiles.shape
    classes = current.shape[1]
    flops = 2 * blocks * k_band * rows * rows * classes
    bytes_accessed = band_tiles.size * 2 + current.size * 2 * 2 + current.size * 4
    return pl.pallas_call(
        functools.partial(band_kernel, fast, n_own),
        cost_estimate=pl.CostEstimate(flops=flops, transcendentals=0, bytes_accessed=bytes_accessed),
        in_specs=[SMEM, SMEM] + [ANY] * (1 + len(rim_sources) + 1),
        out_specs=VMEM,
        out_shape=jax.ShapeDtypeStruct(current.shape, jnp.float32),
        scratch_shapes=[
            pltpu.VMEM((current.shape[0] + 2 * width, classes), current.dtype),
            pltpu.VMEM(band_tiles.shape, band_tiles.dtype),
            pltpu.SemaphoreType.DMA((3 + blocks,)),
        ],
    )(z, band_offsets.reshape(-1), current, *rim_sources, band_tiles)


def hub_kernel(n_hub, width, z_ref, hidx_ref, *rest):
    hub_hbm = rest[:n_hub]
    (ht_hbm, band_hbm, deg_hbm, seeds_hbm, pick_ref,
     out_ref, cur_ref, owned_ref, p1_ref, p3_ref, pc_ref,
     hub, ht, band, deg, seeds, sem) = rest[n_hub:]
    blocks, k_hub, rows = ht.shape[0], ht.shape[1], ht.shape[2]
    own = cur_ref.shape[0]
    n_own = owned_ref.shape[0]
    per_block = []
    for b in range(blocks):
        span = pl.ds(b * rows, rows)
        per_block.append([
            pltpu.make_async_copy(ht_hbm.at[b], ht.at[b], sem.at[n_hub + 4 * b]),
            pltpu.make_async_copy(band_hbm.at[span], band.at[span], sem.at[n_hub + 4 * b + 1]),
            pltpu.make_async_copy(deg_hbm.at[span], deg.at[span], sem.at[n_hub + 4 * b + 2]),
            pltpu.make_async_copy(seeds_hbm.at[span], seeds.at[span], sem.at[n_hub + 4 * b + 3]),
        ])
    for c in per_block[0]:
        c.start()
    copies = []
    at = 0
    for i, piece in enumerate(hub_hbm):
        n = piece.shape[0]
        copies.append(pltpu.make_async_copy(piece, hub.at[pl.ds(at, n)], sem.at[i]))
        at += n
    for c in copies:
        c.start()
    for b in range(1, blocks):
        for c in per_block[b]:
            c.start()
    for c in copies:
        c.wait()
    for b in range(blocks):
        for c in per_block[b]:
            c.wait()
        span = pl.ds(b * rows, rows)
        acc = jnp.zeros((rows, out_ref.shape[1]), jnp.float32)
        for h in range(k_hub):
            p = hidx_ref[b * k_hub + h]
            acc = acc + jnp.dot(ht[b, h], hub[p], preferred_element_type=jnp.float32)
        gathered = (band[span] + acc) / deg[span]
        labels = spread_weight * gathered + (1.0 - spread_weight) * seeds[span]
        out_ref[span, :] = labels
        cur_ref[span, :] = labels.astype(cur_ref.dtype)
    owned = jnp.dot(pick_ref[...], cur_ref[...], preferred_element_type=jnp.float32).astype(owned_ref.dtype)
    owned_ref[...] = owned
    p1_ref[pl.ds(0, n_own), :] = owned
    p3_ref[pl.ds(0, n_own), :] = owned
    z = z_ref[0]
    top = cur_ref[pl.ds(own - width, width), :]
    bottom = cur_ref[pl.ds(0, width), :]
    p1_ref[pl.ds(n_own, width), :] = jnp.where(z % 2 == 0, top, bottom)
    p3_ref[pl.ds(n_own, width), :] = jnp.where(z == 1, top, bottom)
    pc_ref[...] = jnp.where(z == 3, top, bottom)


def hub_call(z, hub_index, pick, hub_pieces, hub_tiles, band, degree, seeds, width):
    blocks, k_hub, rows, _ = hub_tiles.shape
    classes = seeds.shape[1]
    n_hub = len(hub_pieces)
    n_hub_blocks = sum(p.shape[0] for p in hub_pieces)
    n_own = pick.shape[0]
    bf = jnp.bfloat16
    flops = 2 * blocks * k_hub * rows * rows * classes
    bytes_accessed = hub_tiles.size * 2 + n_hub_blocks * rows * classes * 2 + seeds.size * 4 * 4
    return pl.pallas_call(
        functools.partial(hub_kernel, n_hub, width),
        cost_estimate=pl.CostEstimate(flops=flops, transcendentals=0, bytes_accessed=bytes_accessed),
        in_specs=[SMEM, SMEM] + [ANY] * (n_hub + 4) + [VMEM],
        out_specs=[VMEM] * 6,
        out_shape=[
            jax.ShapeDtypeStruct(seeds.shape, jnp.float32),
            jax.ShapeDtypeStruct(seeds.shape, bf),
            jax.ShapeDtypeStruct((n_own, classes), bf),
            jax.ShapeDtypeStruct((n_own + width, classes), bf),
            jax.ShapeDtypeStruct((n_own + width, classes), bf),
            jax.ShapeDtypeStruct((width, classes), bf),
        ],
        scratch_shapes=[
            pltpu.VMEM((n_hub_blocks, rows, classes), bf),
            pltpu.VMEM(hub_tiles.shape, hub_tiles.dtype),
            pltpu.VMEM(seeds.shape, jnp.float32),
            pltpu.VMEM(degree.shape, jnp.float32),
            pltpu.VMEM(seeds.shape, jnp.float32),
            pltpu.SemaphoreType.DMA((n_hub + 4 * blocks,)),
        ],
    )(z, hub_index.reshape(-1), *hub_pieces, hub_tiles, band, degree, seeds, pick)


def body(seed_scores, seed_mask, band_offsets, band_tiles, hub_blocks, hub_tiles, hub_rows):
    block_rows = band_tiles.shape[2]
    seeds = seed_mask.astype(jnp.float32)[:, None] * seed_scores.astype(jnp.float32)
    degree = jnp.sum(band_tiles, axis=(1, 3), dtype=jnp.float32) + jnp.sum(
        hub_tiles, axis=(1, 3), dtype=jnp.float32
    )
    degree = degree.reshape(-1, 1)
    width = BW * block_rows
    z = lax.axis_index("hub").astype(jnp.int32).reshape(1)
    current = seeds.astype(jnp.bfloat16)
    owned = current[hub_rows]
    p1, p3, pc = payloads(current, owned, z[0], width)
    fast = fast_path(owned, block_rows)
    pick = (hub_rows[:, None] == jnp.arange(current.shape[0], dtype=hub_rows.dtype)[None, :]).astype(jnp.bfloat16)
    prep = (pick, degree)
    hub_index = None
    for step in range(ITERS):
        middle = functools.partial(
            band_call, z, band_offsets, current, band_tiles=band_tiles, fast=fast, n_own=owned.shape[0], width=width
        )
        band, hub_pieces, index, prep = exchange(
            current, owned, p1, p3, pc, hub_blocks, width, block_rows, lambda rims: middle(rims), prep
        )
        if hub_index is None:
            hub_index = index
        if prep is not None:
            pick, degree = prep
            prep = None
        labels, current, owned, p1, p3, pc = hub_call(
            z, hub_index, pick, hub_pieces, hub_tiles, band, degree, seeds, width
        )
    return labels


def solution(mesh):
    placed = (
        P(AXES, None),
        P(AXES),
        P(AXES, None),
        P(AXES, None, None, None),
        P(AXES, None),
        P(AXES, None, None, None),
        P(AXES),
    )
    return jax.shard_map(
        body, mesh=mesh, in_specs=placed, out_specs=P(AXES, None), check_vma=False
    )
```

```python
import functools

import jax
import jax.numpy as jnp
import numpy as np
from jax import lax
from jax.experimental import pallas as pl
from jax.experimental.pallas import tpu as pltpu
from jax.sharding import PartitionSpec as P

BW = 2
ITERS = 3
AXES = ("node", "hub")
ROUNDS_32 = ((1, 2, 3), (8, 16, 24), (4,))


spread_weight = 0.8

SMEM = pl.BlockSpec(memory_space=pltpu.SMEM)
ANY = pl.BlockSpec(memory_space=pl.ANY)
VMEM = pl.BlockSpec(memory_space=pltpu.VMEM)


def fast_path(owned, block_rows):
    count = lax.axis_size(AXES)
    return count == 32 and owned.shape[0] == block_rows and lax.axis_size("hub") == 4


def payloads(current, owned, z, width):
    top = current[current.shape[0] - width:]
    bottom = current[:width]
    p1 = jnp.concatenate([owned, jnp.where(z % 2 == 0, top, bottom)], 0)
    p3 = jnp.concatenate([owned, jnp.where(z == 1, top, bottom)], 0)
    pc = jnp.where(z == 3, top, bottom)
    return p1, p3, pc


def exchange(current, owned, p1, p3, pc, hub_blocks, width, block_rows, middle, late):
    count = lax.axis_size(AXES)
    if not fast_path(owned, block_rows):
        forward = [(i, i + 1) for i in range(count - 1)]
        backward = [(target, source) for source, target in forward]
        low = lax.ppermute(current[current.shape[0] - width:], AXES, forward)
        high = lax.ppermute(current[:width], AXES, backward)
        hub_all = lax.all_gather(owned, AXES, axis=0, tiled=True)
        return middle((low, high)), [hub_all.reshape(-1, block_rows, owned.shape[1])], hub_blocks, 0
    me = lax.axis_index(AXES)
    pairs = lambda m: [(i, i ^ m) for i in range(count)]
    r3 = lax.ppermute(p3, AXES, pairs(3))
    r2 = lax.ppermute(owned, AXES, pairs(2))
    r1 = lax.ppermute(p1, AXES, pairs(1))
    groups = count // 4
    cross = [(4 * g + 3, 4 * g + 4) for g in range(groups - 1)]
    cross += [(4 * g + 4, 4 * g + 3) for g in range(groups - 1)]
    rc = lax.ppermute(pc, AXES, cross)
    rows = block_rows
    buf = jnp.concatenate([owned[None], r1[None, :rows], r2[None], r3[None, :rows]], 0)
    offs = [0, 1, 2, 3]
    rounds = ROUNDS_32
    pieces = [buf]
    done = None
    for r, group in enumerate(rounds[1:]):
        sent = {m: lax.ppermute(buf, AXES, pairs(m)) for m in sorted(group, key=lambda m: -m)}
        recvs = [sent[m] for m in group]
        if done is None:
            done, recvs = lax.optimization_barrier((middle((r1, r3, rc)), recvs))
        elif r + 2 == len(rounds):
            done, recvs = lax.optimization_barrier((late(done, buf), recvs))
        offs = offs + [o ^ m for m in group for o in offs]
        pieces = [buf] + recvs
        if r + 2 < len(rounds):
            buf = jnp.concatenate(pieces, 0)
    assert sorted(offs) == list(range(count))
    where = np.zeros(count, np.int32)
    for p, o in enumerate(offs):
        where[o] = p
    assert len(rounds[-1]) == 1
    return done, pieces[1:], jnp.asarray(where)[hub_blocks ^ me], pieces[0].shape[0]


def band_kernel(fast, n_own, z_ref, off_ref, cur_hbm, *rest):
    if fast:
        r1_hbm, r3_hbm, rc_hbm, bt_hbm, out_ref, ext, bt, sem = rest
    else:
        low_hbm, high_hbm, bt_hbm, out_ref, ext, bt, sem = rest
    blocks, k_band, rows = bt.shape[0], bt.shape[1], bt.shape[2]
    own = cur_hbm.shape[0]
    width = (ext.shape[0] - own) // 2
    low_dst = ext.at[pl.ds(0, width)]
    high_dst = ext.at[pl.ds(width + own, width)]
    mid = pltpu.make_async_copy(cur_hbm, ext.at[pl.ds(width, own)], sem.at[1])
    band_copies = [pltpu.make_async_copy(bt_hbm.at[b], bt.at[b], sem.at[3 + b]) for b in range(blocks)]
    band_copies[0].start()
    mid.start()
    if fast:
        z = z_ref[0]
        low_r1 = pltpu.make_async_copy(r1_hbm.at[pl.ds(n_own, width)], low_dst, sem.at[0])
        low_r3 = pltpu.make_async_copy(r3_hbm.at[pl.ds(n_own, width)], low_dst, sem.at[0])
        low_rc = pltpu.make_async_copy(rc_hbm, low_dst, sem.at[0])
        high_r1 = pltpu.make_async_copy(r1_hbm.at[pl.ds(n_own, width)], high_dst, sem.at[2])
        high_r3 = pltpu.make_async_copy(r3_hbm.at[pl.ds(n_own, width)], high_dst, sem.at[2])
        high_rc = pltpu.make_async_copy(rc_hbm, high_dst, sem.at[2])

        @pl.when(z == 0)
        def _():
            low_rc.start()
            high_r1.start()

        @pl.when(z == 1)
        def _():
            low_r1.start()
            high_r3.start()

        @pl.when(z == 2)
        def _():
            low_r3.start()
            high_r1.start()

        @pl.when(z == 3)
        def _():
            low_r1.start()
            high_rc.start()

        low_wait, high_wait = low_rc, high_rc
    else:
        low_wait = pltpu.make_async_copy(low_hbm, low_dst, sem.at[0])
        high_wait = pltpu.make_async_copy(high_hbm, high_dst, sem.at[2])
        low_wait.start()
        high_wait.start()
    for b in range(1, blocks):
        band_copies[b].start()
    mid.wait()
    low_wait.wait()
    high_wait.wait()
    for b in range(blocks):
        band_copies[b].wait()
        acc = jnp.zeros((rows, out_ref.shape[1]), jnp.float32)
        for k in range(k_band):
            n = b + BW + off_ref[b * k_band + k]
            start = pl.multiple_of(n * rows, rows)
            acc = acc + jnp.dot(bt[b, k], ext[pl.ds(start, rows), :], preferred_element_type=jnp.float32)
        out_ref[pl.ds(b * rows, rows), :] = acc


def band_call(z, band_offsets, current, rim_sources, band_tiles, fast, n_own, width):
    blocks, k_band, rows, _ = band_tiles.shape
    classes = current.shape[1]
    flops = 2 * blocks * k_band * rows * rows * classes
    bytes_accessed = band_tiles.size * 2 + current.size * 2 * 2 + current.size * 4
    return pl.pallas_call(
        functools.partial(band_kernel, fast, n_own),
        cost_estimate=pl.CostEstimate(flops=flops, transcendentals=0, bytes_accessed=bytes_accessed),
        in_specs=[SMEM, SMEM] + [ANY] * (1 + len(rim_sources) + 1),
        out_specs=VMEM,
        out_shape=jax.ShapeDtypeStruct(current.shape, jnp.float32),
        scratch_shapes=[
            pltpu.VMEM((current.shape[0] + 2 * width, classes), current.dtype),
            pltpu.VMEM(band_tiles.shape, band_tiles.dtype),
            pltpu.SemaphoreType.DMA((3 + blocks,)),
        ],
    )(z, band_offsets.reshape(-1), current, *rim_sources, band_tiles)


def early_kernel(hidx_ref, band_ref, hub_hbm, ht_hbm, out_ref, hub, ht, sem):
    blocks, k_hub, rows = ht.shape[0], ht.shape[1], ht.shape[2]
    n_early = hub.shape[0]
    tiles = [pltpu.make_async_copy(ht_hbm.at[b], ht.at[b], sem.at[1 + b]) for b in range(blocks)]
    mine = pltpu.make_async_copy(hub_hbm, hub, sem.at[0])
    tiles[0].start()
    mine.start()
    for b in range(1, blocks):
        tiles[b].start()
    mine.wait()
    for b in range(blocks):
        tiles[b].wait()
        span = pl.ds(b * rows, rows)
        out_ref[span, :] = band_ref[span, :]
        for h in range(k_hub):
            p = hidx_ref[b * k_hub + h]

            @pl.when(p < n_early)
            def _():
                out_ref[span, :] += jnp.dot(ht[b, h], hub[p], preferred_element_type=jnp.float32)


def early_call(hub_index, band, mine, hub_tiles):
    blocks = hub_tiles.shape[0]
    return pl.pallas_call(
        early_kernel,
        in_specs=[SMEM, VMEM, ANY, ANY],
        out_specs=VMEM,
        out_shape=jax.ShapeDtypeStruct(band.shape, jnp.float32),
        scratch_shapes=[
            pltpu.VMEM(mine.shape, mine.dtype),
            pltpu.VMEM(hub_tiles.shape, hub_tiles.dtype),
            pltpu.SemaphoreType.DMA((1 + blocks,)),
        ],
    )(hub_index.reshape(-1), band, mine, hub_tiles)


def hub_kernel(n_hub, width, lo, z_ref, hidx_ref, *rest):
    hub_hbm = rest[:n_hub]
    (ht_hbm, band_hbm, deg_hbm, seeds_hbm, pick_ref,
     out_ref, cur_ref, owned_ref, p1_ref, p3_ref, pc_ref,
     hub, ht, band, deg, seeds, sem) = rest[n_hub:]
    blocks, k_hub, rows = ht.shape[0], ht.shape[1], ht.shape[2]
    own = cur_ref.shape[0]
    n_own = owned_ref.shape[0]
    per_block = []
    for b in range(blocks):
        span = pl.ds(b * rows, rows)
        per_block.append([
            pltpu.make_async_copy(ht_hbm.at[b], ht.at[b], sem.at[n_hub + 4 * b]),
            pltpu.make_async_copy(band_hbm.at[span], band.at[span], sem.at[n_hub + 4 * b + 1]),
            pltpu.make_async_copy(deg_hbm.at[span], deg.at[span], sem.at[n_hub + 4 * b + 2]),
            pltpu.make_async_copy(seeds_hbm.at[span], seeds.at[span], sem.at[n_hub + 4 * b + 3]),
        ])
    for c in per_block[0]:
        c.start()
    copies = []
    at = 0
    for i, piece in enumerate(hub_hbm):
        n = piece.shape[0]
        copies.append(pltpu.make_async_copy(piece, hub.at[pl.ds(at, n)], sem.at[i]))
        at += n
    for c in copies:
        c.start()
    for b in range(1, blocks):
        for c in per_block[b]:
            c.start()
    for c in copies:
        c.wait()
    for b in range(blocks):
        for c in per_block[b]:
            c.wait()
        span = pl.ds(b * rows, rows)
        out_ref[span, :] = band[span]
        for h in range(k_hub):
            p = hidx_ref[b * k_hub + h] - lo

            @pl.when(p >= 0)
            def _():
                out_ref[span, :] += jnp.dot(ht[b, h], hub[p], preferred_element_type=jnp.float32)

        gathered = out_ref[span, :] / deg[span]
        labels = spread_weight * gathered + (1.0 - spread_weight) * seeds[span]
        out_ref[span, :] = labels
        cur_ref[span, :] = labels.astype(cur_ref.dtype)
    owned = jnp.dot(pick_ref[...], cur_ref[...], preferred_element_type=jnp.float32).astype(owned_ref.dtype)
    owned_ref[...] = owned
    p1_ref[pl.ds(0, n_own), :] = owned
    p3_ref[pl.ds(0, n_own), :] = owned
    z = z_ref[0]
    top = cur_ref[pl.ds(own - width, width), :]
    bottom = cur_ref[pl.ds(0, width), :]
    p1_ref[pl.ds(n_own, width), :] = jnp.where(z % 2 == 0, top, bottom)
    p3_ref[pl.ds(n_own, width), :] = jnp.where(z == 1, top, bottom)
    pc_ref[...] = jnp.where(z == 3, top, bottom)


def hub_call(z, hub_index, pick, hub_pieces, hub_tiles, band, degree, seeds, width, lo):
    blocks, k_hub, rows, _ = hub_tiles.shape
    classes = seeds.shape[1]
    n_hub = len(hub_pieces)
    n_hub_blocks = sum(p.shape[0] for p in hub_pieces)
    n_own = pick.shape[0]
    bf = jnp.bfloat16
    flops = 2 * blocks * k_hub * rows * rows * classes
    bytes_accessed = hub_tiles.size * 2 + n_hub_blocks * rows * classes * 2 + seeds.size * 4 * 4
    return pl.pallas_call(
        functools.partial(hub_kernel, n_hub, width, lo),
        cost_estimate=pl.CostEstimate(flops=flops, transcendentals=0, bytes_accessed=bytes_accessed),
        in_specs=[SMEM, SMEM] + [ANY] * (n_hub + 4) + [VMEM],
        out_specs=[VMEM] * 6,
        out_shape=[
            jax.ShapeDtypeStruct(seeds.shape, jnp.float32),
            jax.ShapeDtypeStruct(seeds.shape, bf),
            jax.ShapeDtypeStruct((n_own, classes), bf),
            jax.ShapeDtypeStruct((n_own + width, classes), bf),
            jax.ShapeDtypeStruct((n_own + width, classes), bf),
            jax.ShapeDtypeStruct((width, classes), bf),
        ],
        scratch_shapes=[
            pltpu.VMEM((n_hub_blocks, rows, classes), bf),
            pltpu.VMEM(hub_tiles.shape, hub_tiles.dtype),
            pltpu.VMEM(seeds.shape, jnp.float32),
            pltpu.VMEM(degree.shape, jnp.float32),
            pltpu.VMEM(seeds.shape, jnp.float32),
            pltpu.SemaphoreType.DMA((n_hub + 4 * blocks,)),
        ],
    )(z, hub_index.reshape(-1), *hub_pieces, hub_tiles, band, degree, seeds, pick)


def positions_of(hub_blocks, owned, block_rows):
    count = lax.axis_size(AXES)
    if not fast_path(owned, block_rows):
        return hub_blocks
    offs = [0]
    for group in ROUNDS_32:
        offs = offs + [o ^ m for m in group for o in offs]
    where = np.zeros(count, np.int32)
    for p, o in enumerate(offs):
        where[o] = p
    return jnp.asarray(where)[hub_blocks ^ lax.axis_index(AXES)]


def body(seed_scores, seed_mask, band_offsets, band_tiles, hub_blocks, hub_tiles, hub_rows):
    block_rows = band_tiles.shape[2]
    seeds = seed_mask.astype(jnp.float32)[:, None] * seed_scores.astype(jnp.float32)
    degree = jnp.sum(band_tiles, axis=(1, 3), dtype=jnp.float32) + jnp.sum(
        hub_tiles, axis=(1, 3), dtype=jnp.float32
    )
    degree = degree.reshape(-1, 1)
    width = BW * block_rows
    z = lax.axis_index("hub").astype(jnp.int32).reshape(1)
    current = seeds.astype(jnp.bfloat16)
    owned = current[hub_rows]
    p1, p3, pc = payloads(current, owned, z[0], width)
    fast = fast_path(owned, block_rows)
    pick = (hub_rows[:, None] == jnp.arange(current.shape[0], dtype=hub_rows.dtype)[None, :]).astype(jnp.bfloat16)
    for step in range(ITERS):
        middle = functools.partial(
            band_call, z, band_offsets, current, band_tiles=band_tiles, fast=fast, n_own=owned.shape[0], width=width
        )
        index = positions_of(hub_blocks, owned, block_rows)
        band, hub_pieces, hub_index, lo = exchange(
            current, owned, p1, p3, pc, hub_blocks, width, block_rows, lambda rims: middle(rims),
            lambda band, mine: early_call(index, band, mine, hub_tiles),
        )
        labels, current, owned, p1, p3, pc = hub_call(
            z, hub_index, pick, hub_pieces, hub_tiles, band, degree, seeds, width, lo
        )
    return labels


def solution(mesh):
    placed = (
        P(AXES, None),
        P(AXES),
        P(AXES, None),
        P(AXES, None, None, None),
        P(AXES, None),
        P(AXES, None, None, None),
        P(AXES),
    )
    return jax.shard_map(
        body, mesh=mesh, in_specs=placed, out_specs=P(AXES, None), check_vma=False
    )
```

```python
import functools

import jax
import jax.numpy as jnp
import numpy as np
from jax import lax
from jax.experimental import pallas as pl
from jax.experimental.pallas import tpu as pltpu
from jax.sharding import PartitionSpec as P

BW = 2
ITERS = 3
AXES = ("node", "hub")
ROUNDS_32 = ((1, 2, 3), (8, 16, 24), (4,))


spread_weight = 0.8

SMEM = pl.BlockSpec(memory_space=pltpu.SMEM)
ANY = pl.BlockSpec(memory_space=pl.ANY)
VMEM = pl.BlockSpec(memory_space=pltpu.VMEM)


def fast_path(owned, block_rows):
    count = lax.axis_size(AXES)
    return count == 32 and owned.shape[0] == block_rows and lax.axis_size("hub") == 4


def payloads(current, owned, z, width):
    top = current[current.shape[0] - width:]
    bottom = current[:width]
    p1 = jnp.concatenate([owned, jnp.where(z % 2 == 0, top, bottom)], 0)
    p3 = jnp.concatenate([owned, jnp.where(z == 1, top, bottom)], 0)
    pc = jnp.where(z == 3, top, bottom)
    return p1, p3, pc


def exchange(current, owned, p1, p3, pc, hub_blocks, width, block_rows, middle, prep):
    count = lax.axis_size(AXES)
    if not fast_path(owned, block_rows):
        forward = [(i, i + 1) for i in range(count - 1)]
        backward = [(target, source) for source, target in forward]
        low = lax.ppermute(current[current.shape[0] - width:], AXES, forward)
        high = lax.ppermute(current[:width], AXES, backward)
        hub_all = lax.all_gather(owned, AXES, axis=0, tiled=True)
        return middle((low, high)), [hub_all.reshape(-1, block_rows, owned.shape[1])], prep
    me = lax.axis_index(AXES)
    pairs = lambda m: [(i, i ^ m) for i in range(count)]
    r3 = lax.ppermute(p3, AXES, pairs(3))
    r2 = lax.ppermute(owned, AXES, pairs(2))
    r1 = lax.ppermute(p1, AXES, pairs(1))
    groups = count // 4
    cross = [(4 * g + 3, 4 * g + 4) for g in range(groups - 1)]
    cross += [(4 * g + 4, 4 * g + 3) for g in range(groups - 1)]
    rc = lax.ppermute(pc, AXES, cross)
    if prep is not None:
        (r1, r2, r3, rc), prep = lax.optimization_barrier(((r1, r2, r3, rc), prep))
    rows = block_rows
    buf = jnp.concatenate([owned[None], r1[None, :rows], r2[None], r3[None, :rows]], 0)
    offs = [0, 1, 2, 3]
    rounds = ROUNDS_32
    pieces = [buf]
    done = None
    for r, group in enumerate(rounds[1:]):
        sent = {m: lax.ppermute(buf, AXES, pairs(m)) for m in sorted(group, key=lambda m: -m)}
        recvs = [sent[m] for m in group]
        if done is None:
            done, recvs = lax.optimization_barrier((middle((r1, r3, rc)), recvs))
        offs = offs + [o ^ m for m in group for o in offs]
        pieces = [buf] + recvs
        if r + 2 < len(rounds):
            buf = jnp.concatenate(pieces, 0)
    assert sorted(offs) == list(range(count))
    where = np.zeros(count, np.int32)
    for p, o in enumerate(offs):
        where[o] = p
    return done, pieces, prep


def band_kernel(fast, n_own, z_ref, off_ref, cur_hbm, *rest):
    if fast:
        r1_hbm, r3_hbm, rc_hbm, bt_hbm, out_ref, ext, bt, sem = rest
    else:
        low_hbm, high_hbm, bt_hbm, out_ref, ext, bt, sem = rest
    blocks, k_band, rows = bt.shape[0], bt.shape[1], bt.shape[2]
    own = cur_hbm.shape[0]
    width = (ext.shape[0] - own) // 2
    low_dst = ext.at[pl.ds(0, width)]
    high_dst = ext.at[pl.ds(width + own, width)]
    mid = pltpu.make_async_copy(cur_hbm, ext.at[pl.ds(width, own)], sem.at[1])
    band_copies = [pltpu.make_async_copy(bt_hbm.at[b], bt.at[b], sem.at[3 + b]) for b in range(blocks)]
    band_copies[0].start()
    mid.start()
    if fast:
        z = z_ref[0]
        low_r1 = pltpu.make_async_copy(r1_hbm.at[pl.ds(n_own, width)], low_dst, sem.at[0])
        low_r3 = pltpu.make_async_copy(r3_hbm.at[pl.ds(n_own, width)], low_dst, sem.at[0])
        low_rc = pltpu.make_async_copy(rc_hbm, low_dst, sem.at[0])
        high_r1 = pltpu.make_async_copy(r1_hbm.at[pl.ds(n_own, width)], high_dst, sem.at[2])
        high_r3 = pltpu.make_async_copy(r3_hbm.at[pl.ds(n_own, width)], high_dst, sem.at[2])
        high_rc = pltpu.make_async_copy(rc_hbm, high_dst, sem.at[2])

        @pl.when(z == 0)
        def _():
            low_rc.start()
            high_r1.start()

        @pl.when(z == 1)
        def _():
            low_r1.start()
            high_r3.start()

        @pl.when(z == 2)
        def _():
            low_r3.start()
            high_r1.start()

        @pl.when(z == 3)
        def _():
            low_r1.start()
            high_rc.start()

        low_wait, high_wait = low_rc, high_rc
    else:
        low_wait = pltpu.make_async_copy(low_hbm, low_dst, sem.at[0])
        high_wait = pltpu.make_async_copy(high_hbm, high_dst, sem.at[2])
        low_wait.start()
        high_wait.start()
    for b in range(1, blocks):
        band_copies[b].start()
    mid.wait()
    low_wait.wait()
    high_wait.wait()
    for b in range(blocks):
        band_copies[b].wait()
        acc = jnp.zeros((rows, out_ref.shape[1]), jnp.float32)
        for k in range(k_band):
            n = b + BW + off_ref[b * k_band + k]
            start = pl.multiple_of(n * rows, rows)
            acc = acc + jnp.dot(bt[b, k], ext[pl.ds(start, rows), :], preferred_element_type=jnp.float32)
        out_ref[pl.ds(b * rows, rows), :] = acc


def band_call(z, band_offsets, current, rim_sources, band_tiles, fast, n_own, width):
    blocks, k_band, rows, _ = band_tiles.shape
    classes = current.shape[1]
    flops = 2 * blocks * k_band * rows * rows * classes
    bytes_accessed = band_tiles.size * 2 + current.size * 2 * 2 + current.size * 4
    return pl.pallas_call(
        functools.partial(band_kernel, fast, n_own),
        cost_estimate=pl.CostEstimate(flops=flops, transcendentals=0, bytes_accessed=bytes_accessed),
        in_specs=[SMEM, SMEM] + [ANY] * (1 + len(rim_sources) + 1),
        out_specs=VMEM,
        out_shape=jax.ShapeDtypeStruct(current.shape, jnp.float32),
        scratch_shapes=[
            pltpu.VMEM((current.shape[0] + 2 * width, classes), current.dtype),
            pltpu.VMEM(band_tiles.shape, band_tiles.dtype),
            pltpu.SemaphoreType.DMA((3 + blocks,)),
        ],
    )(z, band_offsets.reshape(-1), current, *rim_sources, band_tiles)


def hub_kernel(n_hub, width, final, z_ref, hidx_ref, *rest):
    hub_hbm = rest[:n_hub]
    if final:
        (ht_hbm, band_hbm, deg_hbm, seeds_hbm, out_ref, hub, ht, band, deg, seeds, sem) = rest[n_hub:]
    else:
        (ht_hbm, band_hbm, deg_hbm, seeds_hbm, pick_ref,
         cur_ref, owned_ref, p1_ref, p3_ref, pc_ref,
         hub, ht, band, deg, seeds, sem) = rest[n_hub:]
    blocks, k_hub, rows = ht.shape[0], ht.shape[1], ht.shape[2]
    per_block = []
    for b in range(blocks):
        span = pl.ds(b * rows, rows)
        per_block.append([
            pltpu.make_async_copy(ht_hbm.at[b], ht.at[b], sem.at[n_hub + 4 * b]),
            pltpu.make_async_copy(band_hbm.at[span], band.at[span], sem.at[n_hub + 4 * b + 1]),
            pltpu.make_async_copy(deg_hbm.at[span], deg.at[span], sem.at[n_hub + 4 * b + 2]),
            pltpu.make_async_copy(seeds_hbm.at[span], seeds.at[span], sem.at[n_hub + 4 * b + 3]),
        ])
    for c in per_block[0]:
        c.start()
    copies = []
    at = 0
    for i, piece in enumerate(hub_hbm):
        n = piece.shape[0]
        copies.append(pltpu.make_async_copy(piece, hub.at[pl.ds(at, n)], sem.at[i]))
        at += n
    for c in copies:
        c.start()
    for b in range(1, blocks):
        for c in per_block[b]:
            c.start()
    for c in copies:
        c.wait()
    for b in range(blocks):
        for c in per_block[b]:
            c.wait()
        span = pl.ds(b * rows, rows)
        acc = jnp.zeros((rows, hub.shape[2]), jnp.float32)
        for h in range(k_hub):
            p = hidx_ref[b * k_hub + h]
            acc = acc + jnp.dot(ht[b, h], hub[p], preferred_element_type=jnp.float32)
        gathered = (band[span] + acc) / deg[span]
        labels = spread_weight * gathered + (1.0 - spread_weight) * seeds[span].astype(jnp.float32)
        if final:
            out_ref[span, :] = labels
        else:
            cur_ref[span, :] = labels.astype(cur_ref.dtype)
    if final:
        return
    own = cur_ref.shape[0]
    n_own = owned_ref.shape[0]
    owned = jnp.dot(pick_ref[...], cur_ref[...], preferred_element_type=jnp.float32).astype(owned_ref.dtype)
    owned_ref[...] = owned
    p1_ref[pl.ds(0, n_own), :] = owned
    p3_ref[pl.ds(0, n_own), :] = owned
    z = z_ref[0]
    top = cur_ref[pl.ds(own - width, width), :]
    bottom = cur_ref[pl.ds(0, width), :]
    p1_ref[pl.ds(n_own, width), :] = jnp.where(z % 2 == 0, top, bottom)
    p3_ref[pl.ds(n_own, width), :] = jnp.where(z == 1, top, bottom)
    pc_ref[...] = jnp.where(z == 3, top, bottom)


def hub_call(z, hub_index, pick, hub_pieces, hub_tiles, band, degree, seeds, width, final):
    blocks, k_hub, rows, _ = hub_tiles.shape
    classes = seeds.shape[1]
    n_hub = len(hub_pieces)
    n_hub_blocks = sum(p.shape[0] for p in hub_pieces)
    n_own = pick.shape[0]
    bf = jnp.bfloat16
    flops = 2 * blocks * k_hub * rows * rows * classes
    bytes_accessed = hub_tiles.size * 2 + n_hub_blocks * rows * classes * 2 + seeds.size * 4 * 4
    if final:
        outs = [jax.ShapeDtypeStruct(seeds.shape, jnp.float32)]
    else:
        outs = [
            jax.ShapeDtypeStruct(seeds.shape, bf),
            jax.ShapeDtypeStruct((n_own, classes), bf),
            jax.ShapeDtypeStruct((n_own + width, classes), bf),
            jax.ShapeDtypeStruct((n_own + width, classes), bf),
            jax.ShapeDtypeStruct((width, classes), bf),
        ]
    return pl.pallas_call(
        functools.partial(hub_kernel, n_hub, width, final),
        cost_estimate=pl.CostEstimate(flops=flops, transcendentals=0, bytes_accessed=bytes_accessed),
        in_specs=[SMEM, SMEM] + [ANY] * (n_hub + 4) + ([] if final else [VMEM]),
        out_specs=[VMEM] * len(outs),
        out_shape=outs,
        scratch_shapes=[
            pltpu.VMEM((n_hub_blocks, rows, classes), bf),
            pltpu.VMEM(hub_tiles.shape, hub_tiles.dtype),
            pltpu.VMEM(seeds.shape, jnp.float32),
            pltpu.VMEM(degree.shape, jnp.float32),
            pltpu.VMEM(seeds.shape, seeds.dtype),
            pltpu.SemaphoreType.DMA((n_hub + 4 * blocks,)),
        ],
    )(z, hub_index.reshape(-1), *hub_pieces, hub_tiles, band, degree, seeds, *([] if final else [pick]))


def positions_of(hub_blocks, owned, block_rows):
    count = lax.axis_size(AXES)
    if not fast_path(owned, block_rows):
        return hub_blocks
    offs = [0]
    for group in ROUNDS_32:
        offs = offs + [o ^ m for m in group for o in offs]
    where = np.zeros(count, np.int32)
    for p, o in enumerate(offs):
        where[o] = p
    return jnp.asarray(where)[hub_blocks ^ lax.axis_index(AXES)]


def body(seed_scores, seed_mask, band_offsets, band_tiles, hub_blocks, hub_tiles, hub_rows):
    block_rows = band_tiles.shape[2]
    seeds = seed_mask.astype(jnp.float32)[:, None] * seed_scores.astype(jnp.float32)
    degree = jnp.sum(band_tiles, axis=(1, 3), dtype=jnp.float32) + jnp.sum(
        hub_tiles, axis=(1, 3), dtype=jnp.float32
    )
    degree = degree.reshape(-1, 1)
    width = BW * block_rows
    z = lax.axis_index("hub").astype(jnp.int32).reshape(1)
    current = seeds.astype(jnp.bfloat16)
    seeds16 = current
    owned = current[hub_rows]
    p1, p3, pc = payloads(current, owned, z[0], width)
    fast = fast_path(owned, block_rows)
    pick = (hub_rows[:, None] == jnp.arange(current.shape[0], dtype=hub_rows.dtype)[None, :]).astype(jnp.bfloat16)
    prep = (pick, degree, positions_of(hub_blocks, owned, block_rows))
    for step in range(ITERS):
        middle = functools.partial(
            band_call, z, band_offsets, current, band_tiles=band_tiles, fast=fast, n_own=owned.shape[0], width=width
        )
        band, hub_pieces, prep_out = exchange(
            current, owned, p1, p3, pc, hub_blocks, width, block_rows, lambda rims: middle(rims), prep
        )
        if prep is not None:
            pick, degree, hub_index = prep_out
            prep = None
        final = step + 1 == ITERS
        outs = hub_call(z, hub_index, pick, hub_pieces, hub_tiles, band, degree, seeds16, width, final)
        if final:
            labels = outs[0]
        else:
            current, owned, p1, p3, pc = outs
    return labels


def solution(mesh):
    placed = (
        P(AXES, None),
        P(AXES),
        P(AXES, None),
        P(AXES, None, None, None),
        P(AXES, None),
        P(AXES, None, None, None),
        P(AXES),
    )
    return jax.shard_map(
        body, mesh=mesh, in_specs=placed, out_specs=P(AXES, None), check_vma=False
    )
```

```python
import functools

import jax
import jax.numpy as jnp
import numpy as np
from jax import lax
from jax.experimental import pallas as pl
from jax.experimental.pallas import tpu as pltpu
from jax.sharding import PartitionSpec as P

BW = 2
ITERS = 3
AXES = ("node", "hub")
ROUNDS_32 = ((1, 2, 3), (8, 16, 24), (4,))


spread_weight = 0.8

SMEM = pl.BlockSpec(memory_space=pltpu.SMEM)
ANY = pl.BlockSpec(memory_space=pl.ANY)
VMEM = pl.BlockSpec(memory_space=pltpu.VMEM)


def fast_path(owned, block_rows):
    count = lax.axis_size(AXES)
    return count == 32 and owned.shape[0] == block_rows and lax.axis_size("hub") == 4


def payloads(current, owned, z, width):
    top = current[current.shape[0] - width:]
    bottom = current[:width]
    p1 = jnp.concatenate([owned, jnp.where(z % 2 == 0, top, bottom)], 0)
    p3 = jnp.concatenate([owned, jnp.where(z == 1, top, bottom)], 0)
    pc = jnp.where(z == 3, top, bottom)
    return p1, p3, pc


def exchange(current, owned, p1, p3, pc, hub_blocks, width, block_rows, middle, prep):
    count = lax.axis_size(AXES)
    if not fast_path(owned, block_rows):
        forward = [(i, i + 1) for i in range(count - 1)]
        backward = [(target, source) for source, target in forward]
        low = lax.ppermute(current[current.shape[0] - width:], AXES, forward)
        high = lax.ppermute(current[:width], AXES, backward)
        hub_all = lax.all_gather(owned, AXES, axis=0, tiled=True)
        done = (middle((low, high), 0), middle((low, high), 1))
        return done, [hub_all.reshape(-1, block_rows, owned.shape[1])], prep
    me = lax.axis_index(AXES)
    pairs = lambda m: [(i, i ^ m) for i in range(count)]
    r3 = lax.ppermute(p3, AXES, pairs(3))
    r2 = lax.ppermute(owned, AXES, pairs(2))
    r1 = lax.ppermute(p1, AXES, pairs(1))
    groups = count // 4
    cross = [(4 * g + 3, 4 * g + 4) for g in range(groups - 1)]
    cross += [(4 * g + 4, 4 * g + 3) for g in range(groups - 1)]
    rc = lax.ppermute(pc, AXES, cross)
    if prep is not None:
        (r1, r2, r3, rc), prep = lax.optimization_barrier(((r1, r2, r3, rc), prep))
    rows = block_rows
    buf = jnp.concatenate([owned[None], r1[None, :rows], r2[None], r3[None, :rows]], 0)
    offs = [0, 1, 2, 3]
    rounds = ROUNDS_32
    pieces = [buf]
    done = None
    for r, group in enumerate(rounds[1:]):
        sent = {m: lax.ppermute(buf, AXES, pairs(m)) for m in sorted(group, key=lambda m: -m)}
        recvs = [sent[m] for m in group]
        if done is None:
            done, recvs = lax.optimization_barrier((middle((r1, r3, rc), 0), recvs))
        else:
            done, recvs = lax.optimization_barrier(((done, middle((r1, r3, rc), 1)), recvs))
        offs = offs + [o ^ m for m in group for o in offs]
        pieces = [buf] + recvs
        if r + 2 < len(rounds):
            buf = jnp.concatenate(pieces, 0)
    assert sorted(offs) == list(range(count)) and len(rounds) == 3
    return done, pieces, prep


def band_kernel(fast, n_own, b0, z_ref, off_ref, cur_hbm, *rest):
    if fast:
        r1_hbm, r3_hbm, rc_hbm, bt_hbm, out_ref, ext, bt, sem = rest
    else:
        low_hbm, high_hbm, bt_hbm, out_ref, ext, bt, sem = rest
    blocks, k_band, rows = bt.shape[0], bt.shape[1], bt.shape[2]
    own = cur_hbm.shape[0]
    width = (ext.shape[0] - own) // 2
    low_dst = ext.at[pl.ds(0, width)]
    high_dst = ext.at[pl.ds(width + own, width)]
    mid = pltpu.make_async_copy(cur_hbm, ext.at[pl.ds(width, own)], sem.at[1])
    band_copies = [pltpu.make_async_copy(bt_hbm.at[b0 + b], bt.at[b], sem.at[3 + b]) for b in range(blocks)]
    band_copies[0].start()
    mid.start()
    if fast:
        z = z_ref[0]
        low_r1 = pltpu.make_async_copy(r1_hbm.at[pl.ds(n_own, width)], low_dst, sem.at[0])
        low_r3 = pltpu.make_async_copy(r3_hbm.at[pl.ds(n_own, width)], low_dst, sem.at[0])
        low_rc = pltpu.make_async_copy(rc_hbm, low_dst, sem.at[0])
        high_r1 = pltpu.make_async_copy(r1_hbm.at[pl.ds(n_own, width)], high_dst, sem.at[2])
        high_r3 = pltpu.make_async_copy(r3_hbm.at[pl.ds(n_own, width)], high_dst, sem.at[2])
        high_rc = pltpu.make_async_copy(rc_hbm, high_dst, sem.at[2])

        @pl.when(z == 0)
        def _():
            low_rc.start()
            high_r1.start()

        @pl.when(z == 1)
        def _():
            low_r1.start()
            high_r3.start()

        @pl.when(z == 2)
        def _():
            low_r3.start()
            high_r1.start()

        @pl.when(z == 3)
        def _():
            low_r1.start()
            high_rc.start()

        low_wait, high_wait = low_rc, high_rc
    else:
        low_wait = pltpu.make_async_copy(low_hbm, low_dst, sem.at[0])
        high_wait = pltpu.make_async_copy(high_hbm, high_dst, sem.at[2])
        low_wait.start()
        high_wait.start()
    for b in range(1, blocks):
        band_copies[b].start()
    mid.wait()
    low_wait.wait()
    high_wait.wait()
    for b in range(blocks):
        band_copies[b].wait()
        acc = jnp.zeros((rows, out_ref.shape[1]), jnp.float32)
        for k in range(k_band):
            n = b0 + b + BW + off_ref[(b0 + b) * k_band + k]
            start = pl.multiple_of(n * rows, rows)
            acc = acc + jnp.dot(bt[b, k], ext[pl.ds(start, rows), :], preferred_element_type=jnp.float32)
        out_ref[pl.ds(b * rows, rows), :] = acc


def band_call(z, band_offsets, current, rim_sources, half, band_tiles, fast, n_own, width):
    all_blocks, k_band, rows, _ = band_tiles.shape
    first = (all_blocks + 1) // 2
    b0, blocks = (0, first) if half == 0 else (first, all_blocks - first)
    classes = current.shape[1]
    flops = 2 * blocks * k_band * rows * rows * classes
    bytes_accessed = band_tiles.size * 2 + current.size * 2 * 2 + current.size * 4
    return pl.pallas_call(
        functools.partial(band_kernel, fast, n_own, b0),
        cost_estimate=pl.CostEstimate(flops=flops, transcendentals=0, bytes_accessed=bytes_accessed),
        in_specs=[SMEM, SMEM] + [ANY] * (1 + len(rim_sources) + 1),
        out_specs=VMEM,
        out_shape=jax.ShapeDtypeStruct((blocks * rows, classes), jnp.float32),
        scratch_shapes=[
            pltpu.VMEM((current.shape[0] + 2 * width, classes), current.dtype),
            pltpu.VMEM((blocks,) + band_tiles.shape[1:], band_tiles.dtype),
            pltpu.SemaphoreType.DMA((3 + blocks,)),
        ],
    )(z, band_offsets.reshape(-1), current, *rim_sources, band_tiles)


def hub_kernel(n_hub, width, final, z_ref, hidx_ref, *rest):
    hub_hbm = rest[:n_hub]
    if final:
        (ht_hbm, band_a, band_b, deg_hbm, seeds_hbm, out_ref, hub, ht, band, deg, seeds, sem) = rest[n_hub:]
    else:
        (ht_hbm, band_a, band_b, deg_hbm, seeds_hbm, pick_ref,
         cur_ref, owned_ref, p1_ref, p3_ref, pc_ref,
         hub, ht, band, deg, seeds, sem) = rest[n_hub:]
    blocks, k_hub, rows = ht.shape[0], ht.shape[1], ht.shape[2]
    split = band_a.shape[0] // rows
    per_block = []
    for b in range(blocks):
        span = pl.ds(b * rows, rows)
        per_block.append([
            pltpu.make_async_copy(ht_hbm.at[b], ht.at[b], sem.at[n_hub + 4 * b]),
            pltpu.make_async_copy(
                band_a.at[span] if b < split else band_b.at[pl.ds((b - split) * rows, rows)],
                band.at[span],
                sem.at[n_hub + 4 * b + 1],
            ),
            pltpu.make_async_copy(deg_hbm.at[span], deg.at[span], sem.at[n_hub + 4 * b + 2]),
            pltpu.make_async_copy(seeds_hbm.at[span], seeds.at[span], sem.at[n_hub + 4 * b + 3]),
        ])
    for c in per_block[0]:
        c.start()
    copies = []
    at = 0
    for i, piece in enumerate(hub_hbm):
        n = piece.shape[0]
        copies.append(pltpu.make_async_copy(piece, hub.at[pl.ds(at, n)], sem.at[i]))
        at += n
    for c in copies:
        c.start()
    for b in range(1, blocks):
        for c in per_block[b]:
            c.start()
    for c in copies:
        c.wait()
    for b in range(blocks):
        for c in per_block[b]:
            c.wait()
        span = pl.ds(b * rows, rows)
        acc = jnp.zeros((rows, hub.shape[2]), jnp.float32)
        for h in range(k_hub):
            p = hidx_ref[b * k_hub + h]
            acc = acc + jnp.dot(ht[b, h], hub[p], preferred_element_type=jnp.float32)
        gathered = (band[span] + acc) / deg[span]
        labels = spread_weight * gathered + (1.0 - spread_weight) * seeds[span].astype(jnp.float32)
        if final:
            out_ref[span, :] = labels
        else:
            cur_ref[span, :] = labels.astype(cur_ref.dtype)
    if final:
        return
    own = cur_ref.shape[0]
    n_own = owned_ref.shape[0]
    owned = jnp.dot(pick_ref[...], cur_ref[...], preferred_element_type=jnp.float32).astype(owned_ref.dtype)
    owned_ref[...] = owned
    p1_ref[pl.ds(0, n_own), :] = owned
    p3_ref[pl.ds(0, n_own), :] = owned
    z = z_ref[0]
    top = cur_ref[pl.ds(own - width, width), :]
    bottom = cur_ref[pl.ds(0, width), :]
    p1_ref[pl.ds(n_own, width), :] = jnp.where(z % 2 == 0, top, bottom)
    p3_ref[pl.ds(n_own, width), :] = jnp.where(z == 1, top, bottom)
    pc_ref[...] = jnp.where(z == 3, top, bottom)


def hub_call(z, hub_index, pick, hub_pieces, hub_tiles, band, degree, seeds, width, final):
    blocks, k_hub, rows, _ = hub_tiles.shape
    classes = seeds.shape[1]
    n_hub = len(hub_pieces)
    n_hub_blocks = sum(p.shape[0] for p in hub_pieces)
    n_own = pick.shape[0]
    bf = jnp.bfloat16
    flops = 2 * blocks * k_hub * rows * rows * classes
    bytes_accessed = hub_tiles.size * 2 + n_hub_blocks * rows * classes * 2 + seeds.size * 4 * 4
    if final:
        outs = [jax.ShapeDtypeStruct(seeds.shape, jnp.float32)]
    else:
        outs = [
            jax.ShapeDtypeStruct(seeds.shape, bf),
            jax.ShapeDtypeStruct((n_own, classes), bf),
            jax.ShapeDtypeStruct((n_own + width, classes), bf),
            jax.ShapeDtypeStruct((n_own + width, classes), bf),
            jax.ShapeDtypeStruct((width, classes), bf),
        ]
    return pl.pallas_call(
        functools.partial(hub_kernel, n_hub, width, final),
        cost_estimate=pl.CostEstimate(flops=flops, transcendentals=0, bytes_accessed=bytes_accessed),
        in_specs=[SMEM, SMEM] + [ANY] * (n_hub + 5) + ([] if final else [VMEM]),
        out_specs=[VMEM] * len(outs),
        out_shape=outs,
        scratch_shapes=[
            pltpu.VMEM((n_hub_blocks, rows, classes), bf),
            pltpu.VMEM(hub_tiles.shape, hub_tiles.dtype),
            pltpu.VMEM((seeds.shape[0], classes), jnp.float32),
            pltpu.VMEM(degree.shape, jnp.float32),
            pltpu.VMEM(seeds.shape, seeds.dtype),
            pltpu.SemaphoreType.DMA((n_hub + 4 * blocks,)),
        ],
    )(z, hub_index.reshape(-1), *hub_pieces, hub_tiles, *band, degree, seeds, *([] if final else [pick]))


def positions_of(hub_blocks, owned, block_rows):
    count = lax.axis_size(AXES)
    if not fast_path(owned, block_rows):
        return hub_blocks
    offs = [0]
    for group in ROUNDS_32:
        offs = offs + [o ^ m for m in group for o in offs]
    where = np.zeros(count, np.int32)
    for p, o in enumerate(offs):
        where[o] = p
    return jnp.asarray(where)[hub_blocks ^ lax.axis_index(AXES)]


def body(seed_scores, seed_mask, band_offsets, band_tiles, hub_blocks, hub_tiles, hub_rows):
    block_rows = band_tiles.shape[2]
    seeds = seed_mask.astype(jnp.float32)[:, None] * seed_scores.astype(jnp.float32)
    degree = jnp.sum(band_tiles, axis=(1, 3), dtype=jnp.float32) + jnp.sum(
        hub_tiles, axis=(1, 3), dtype=jnp.float32
    )
    degree = degree.reshape(-1, 1)
    width = BW * block_rows
    z = lax.axis_index("hub").astype(jnp.int32).reshape(1)
    current = seeds.astype(jnp.bfloat16)
    seeds16 = current
    owned = current[hub_rows]
    p1, p3, pc = payloads(current, owned, z[0], width)
    fast = fast_path(owned, block_rows)
    pick = (hub_rows[:, None] == jnp.arange(current.shape[0], dtype=hub_rows.dtype)[None, :]).astype(jnp.bfloat16)
    prep = (pick, degree, positions_of(hub_blocks, owned, block_rows))
    for step in range(ITERS):
        middle = functools.partial(
            band_call, z, band_offsets, current, band_tiles=band_tiles, fast=fast, n_own=owned.shape[0], width=width
        )
        band, hub_pieces, prep_out = exchange(
            current, owned, p1, p3, pc, hub_blocks, width, block_rows, lambda rims, half: middle(rims, half), prep
        )
        if prep is not None:
            pick, degree, hub_index = prep_out
            prep = None
        final = step + 1 == ITERS
        outs = hub_call(z, hub_index, pick, hub_pieces, hub_tiles, band, degree, seeds16, width, final)
        if final:
            labels = outs[0]
        else:
            current, owned, p1, p3, pc = outs
    return labels


def solution(mesh):
    placed = (
        P(AXES, None),
        P(AXES),
        P(AXES, None),
        P(AXES, None, None, None),
        P(AXES, None),
        P(AXES, None, None, None),
        P(AXES),
    )
    return jax.shard_map(
        body, mesh=mesh, in_specs=placed, out_specs=P(AXES, None), check_vma=False
    )
```

```python
import functools

import jax
import jax.numpy as jnp
import numpy as np
from jax import lax
from jax.experimental import pallas as pl
from jax.experimental.pallas import tpu as pltpu
from jax.sharding import PartitionSpec as P

BW = 2
ITERS = 3
AXES = ("node", "hub")
ROUNDS_32 = ((1, 2, 3), (8, 16, 24), (4,))


spread_weight = 0.8

SMEM = pl.BlockSpec(memory_space=pltpu.SMEM)
ANY = pl.BlockSpec(memory_space=pl.ANY)
VMEM = pl.BlockSpec(memory_space=pltpu.VMEM)


def fast_path(owned, block_rows):
    count = lax.axis_size(AXES)
    return count == 32 and owned.shape[0] == block_rows and lax.axis_size("hub") == 4


def payloads(current, owned, z, width):
    top = current[current.shape[0] - width:]
    bottom = current[:width]
    p1 = jnp.concatenate([owned, jnp.where(z % 2 == 0, top, bottom)], 0)
    p3 = jnp.concatenate([owned, jnp.where(z == 1, top, bottom)], 0)
    pc = jnp.where(z == 3, top, bottom)
    return p1, p3, pc


def exchange(current, owned, p1, p3, pc, hub_blocks, width, block_rows, middle, prep):
    count = lax.axis_size(AXES)
    if not fast_path(owned, block_rows):
        forward = [(i, i + 1) for i in range(count - 1)]
        backward = [(target, source) for source, target in forward]
        low = lax.ppermute(current[current.shape[0] - width:], AXES, forward)
        high = lax.ppermute(current[:width], AXES, backward)
        hub_all = lax.all_gather(owned, AXES, axis=0, tiled=True)
        return middle((low, high)), [hub_all.reshape(-1, block_rows, owned.shape[1])], prep
    me = lax.axis_index(AXES)
    pairs = lambda m: [(i, i ^ m) for i in range(count)]
    r3 = lax.ppermute(p3, AXES, pairs(3))
    r2 = lax.ppermute(owned, AXES, pairs(2))
    r1 = lax.ppermute(p1, AXES, pairs(1))
    groups = count // 4
    cross = [(4 * g + 3, 4 * g + 4) for g in range(groups - 1)]
    cross += [(4 * g + 4, 4 * g + 3) for g in range(groups - 1)]
    rc = lax.ppermute(pc, AXES, cross)
    if prep is not None:
        (r1, r2, r3, rc), prep = lax.optimization_barrier(((r1, r2, r3, rc), prep))
    rows = block_rows
    buf = jnp.concatenate([owned[None], r1[None, :rows], r2[None], r3[None, :rows]], 0)
    offs = [0, 1, 2, 3]
    rounds = ROUNDS_32
    pieces = [buf]
    done = None
    for r, group in enumerate(rounds[1:]):
        sent = {m: lax.ppermute(buf, AXES, pairs(m)) for m in sorted(group, key=lambda m: -m)}
        recvs = [sent[m] for m in group]
        if done is None:
            done, recvs = lax.optimization_barrier((middle((r1, r3, rc)), recvs))
        offs = offs + [o ^ m for m in group for o in offs]
        pieces = [buf] + recvs
        if r + 2 < len(rounds):
            buf = jnp.concatenate(pieces, 0)
    assert sorted(offs) == list(range(count))
    where = np.zeros(count, np.int32)
    for p, o in enumerate(offs):
        where[o] = p
    return done, pieces, prep


def band_kernel(fast, n_own, z_ref, off_ref, cur_hbm, *rest):
    if fast:
        r1_hbm, r3_hbm, rc_hbm, bt_hbm, out_ref, ext, bt, sem = rest
    else:
        low_hbm, high_hbm, bt_hbm, out_ref, ext, bt, sem = rest
    blocks, k_band, rows = bt.shape[0], bt.shape[1], bt.shape[2]
    own = cur_hbm.shape[0]
    width = (ext.shape[0] - own) // 2
    low_dst = ext.at[pl.ds(0, width)]
    high_dst = ext.at[pl.ds(width + own, width)]
    mid = pltpu.make_async_copy(cur_hbm, ext.at[pl.ds(width, own)], sem.at[1])
    band_copies = [pltpu.make_async_copy(bt_hbm.at[b], bt.at[b], sem.at[3 + b]) for b in range(blocks)]
    band_copies[0].start()
    mid.start()
    if fast:
        z = z_ref[0]
        low_r1 = pltpu.make_async_copy(r1_hbm.at[pl.ds(n_own, width)], low_dst, sem.at[0])
        low_r3 = pltpu.make_async_copy(r3_hbm.at[pl.ds(n_own, width)], low_dst, sem.at[0])
        low_rc = pltpu.make_async_copy(rc_hbm, low_dst, sem.at[0])
        high_r1 = pltpu.make_async_copy(r1_hbm.at[pl.ds(n_own, width)], high_dst, sem.at[2])
        high_r3 = pltpu.make_async_copy(r3_hbm.at[pl.ds(n_own, width)], high_dst, sem.at[2])
        high_rc = pltpu.make_async_copy(rc_hbm, high_dst, sem.at[2])

        @pl.when(z == 0)
        def _():
            low_rc.start()
            high_r1.start()

        @pl.when(z == 1)
        def _():
            low_r1.start()
            high_r3.start()

        @pl.when(z == 2)
        def _():
            low_r3.start()
            high_r1.start()

        @pl.when(z == 3)
        def _():
            low_r1.start()
            high_rc.start()

        low_wait, high_wait = low_rc, high_rc
    else:
        low_wait = pltpu.make_async_copy(low_hbm, low_dst, sem.at[0])
        high_wait = pltpu.make_async_copy(high_hbm, high_dst, sem.at[2])
        low_wait.start()
        high_wait.start()
    for b in range(1, blocks):
        band_copies[b].start()
    mid.wait()
    low_wait.wait()
    high_wait.wait()
    for b in range(blocks):
        band_copies[b].wait()
        acc = jnp.zeros((rows, out_ref.shape[1]), jnp.float32)
        for k in range(k_band):
            n = b + BW + off_ref[b * k_band + k]
            start = pl.multiple_of(n * rows, rows)
            acc = acc + jnp.dot(bt[b, k], ext[pl.ds(start, rows), :], preferred_element_type=jnp.float32)
        out_ref[pl.ds(b * rows, rows), :] = acc


def band_call(z, band_offsets, current, rim_sources, band_tiles, fast, n_own, width):
    blocks, k_band, rows, _ = band_tiles.shape
    classes = current.shape[1]
    flops = 2 * blocks * k_band * rows * rows * classes
    bytes_accessed = band_tiles.size * 2 + current.size * 2 * 2 + current.size * 4
    return pl.pallas_call(
        functools.partial(band_kernel, fast, n_own),
        cost_estimate=pl.CostEstimate(flops=flops, transcendentals=0, bytes_accessed=bytes_accessed),
        in_specs=[SMEM, SMEM] + [ANY] * (1 + len(rim_sources) + 1),
        out_specs=VMEM,
        out_shape=jax.ShapeDtypeStruct(current.shape, jnp.float32),
        scratch_shapes=[
            pltpu.VMEM((current.shape[0] + 2 * width, classes), current.dtype),
            pltpu.VMEM(band_tiles.shape, band_tiles.dtype),
            pltpu.SemaphoreType.DMA((3 + blocks,)),
        ],
    )(z, band_offsets.reshape(-1), current, *rim_sources, band_tiles)


def hub_kernel(n_hub, width, final, z_ref, hidx_ref, *rest):
    hub_hbm = rest[:n_hub]
    if final:
        (ht_hbm, band_hbm, deg_hbm, seeds_hbm, out_ref, hub, ht, band, deg, seeds, sem) = rest[n_hub:]
    else:
        (ht_hbm, band_hbm, deg_hbm, seeds_hbm, pick_ref,
         cur_ref, owned_ref, p1_ref, p3_ref, pc_ref,
         hub, ht, band, deg, seeds, sem) = rest[n_hub:]
    blocks, k_hub, rows = ht.shape[0], ht.shape[1], ht.shape[2]
    per_block = []
    for b in range(blocks):
        span = pl.ds(b * rows, rows)
        per_block.append([
            pltpu.make_async_copy(ht_hbm.at[b], ht.at[b], sem.at[n_hub + 4 * b]),
            pltpu.make_async_copy(band_hbm.at[span], band.at[span], sem.at[n_hub + 4 * b + 1]),
            pltpu.make_async_copy(deg_hbm.at[span], deg.at[span], sem.at[n_hub + 4 * b + 2]),
            pltpu.make_async_copy(seeds_hbm.at[span], seeds.at[span], sem.at[n_hub + 4 * b + 3]),
        ])
    for c in per_block[0]:
        c.start()
    copies = []
    at = 0
    for i, piece in enumerate(hub_hbm):
        n = piece.shape[0]
        copies.append(pltpu.make_async_copy(piece, hub.at[pl.ds(at, n)], sem.at[i]))
        at += n
    for c in copies:
        c.start()
    for b in range(1, blocks):
        for c in per_block[b]:
            c.start()
    for c in copies:
        c.wait()
    for b in range(blocks):
        for c in per_block[b]:
            c.wait()
        span = pl.ds(b * rows, rows)
        acc = jnp.zeros((rows, hub.shape[2]), jnp.float32)
        for h in range(k_hub):
            p = hidx_ref[b * k_hub + h]
            acc = acc + jnp.dot(ht[b, h], hub[p], preferred_element_type=jnp.float32)
        gathered = (band[span] + acc) / deg[span]
        labels = spread_weight * gathered + (1.0 - spread_weight) * seeds[span].astype(jnp.float32)
        if final:
            out_ref[span, :] = labels
        else:
            cur_ref[span, :] = labels.astype(cur_ref.dtype)
    if final:
        return
    own = cur_ref.shape[0]
    n_own = owned_ref.shape[0]
    owned = jnp.dot(pick_ref[...], cur_ref[...], preferred_element_type=jnp.float32).astype(owned_ref.dtype)
    owned_ref[...] = owned
    p1_ref[pl.ds(0, n_own), :] = owned
    p3_ref[pl.ds(0, n_own), :] = owned
    z = z_ref[0]
    top = cur_ref[pl.ds(own - width, width), :]
    bottom = cur_ref[pl.ds(0, width), :]
    p1_ref[pl.ds(n_own, width), :] = jnp.where(z % 2 == 0, top, bottom)
    p3_ref[pl.ds(n_own, width), :] = jnp.where(z == 1, top, bottom)
    pc_ref[...] = jnp.where(z == 3, top, bottom)


def hub_call(z, hub_index, pick, hub_pieces, hub_tiles, band, degree, seeds, width, final):
    blocks, k_hub, rows, _ = hub_tiles.shape
    classes = seeds.shape[1]
    n_hub = len(hub_pieces)
    n_hub_blocks = sum(p.shape[0] for p in hub_pieces)
    n_own = pick.shape[0]
    bf = jnp.bfloat16
    flops = 2 * blocks * k_hub * rows * rows * classes
    bytes_accessed = hub_tiles.size * 2 + n_hub_blocks * rows * classes * 2 + seeds.size * 4 * 4
    if final:
        outs = [jax.ShapeDtypeStruct(seeds.shape, jnp.float32)]
    else:
        outs = [
            jax.ShapeDtypeStruct(seeds.shape, bf),
            jax.ShapeDtypeStruct((n_own, classes), bf),
            jax.ShapeDtypeStruct((n_own + width, classes), bf),
            jax.ShapeDtypeStruct((n_own + width, classes), bf),
            jax.ShapeDtypeStruct((width, classes), bf),
        ]
    return pl.pallas_call(
        functools.partial(hub_kernel, n_hub, width, final),
        cost_estimate=pl.CostEstimate(flops=flops, transcendentals=0, bytes_accessed=bytes_accessed),
        in_specs=[SMEM, SMEM] + [ANY] * (n_hub + 4) + ([] if final else [VMEM]),
        out_specs=[VMEM] * len(outs),
        out_shape=outs,
        scratch_shapes=[
            pltpu.VMEM((n_hub_blocks, rows, classes), bf),
            pltpu.VMEM(hub_tiles.shape, hub_tiles.dtype),
            pltpu.VMEM(seeds.shape, jnp.float32),
            pltpu.VMEM(degree.shape, jnp.float32),
            pltpu.VMEM(seeds.shape, seeds.dtype),
            pltpu.SemaphoreType.DMA((n_hub + 4 * blocks,)),
        ],
    )(z, hub_index, *hub_pieces, hub_tiles, band, degree, seeds, *([] if final else [pick]))


def positions_of(hub_blocks, owned, block_rows):
    count = lax.axis_size(AXES)
    if not fast_path(owned, block_rows):
        return hub_blocks
    offs = [0]
    for group in ROUNDS_32:
        offs = offs + [o ^ m for m in group for o in offs]
    where = np.zeros(count, np.int32)
    for p, o in enumerate(offs):
        where[o] = p
    return jnp.asarray(where)[hub_blocks ^ lax.axis_index(AXES)]


def body(seed_scores, seed_mask, band_offsets, band_tiles, hub_blocks, hub_tiles, hub_rows):
    block_rows = band_tiles.shape[2]
    seeds = seed_mask.astype(jnp.float32)[:, None] * seed_scores.astype(jnp.float32)
    degree = jnp.sum(band_tiles, axis=(1, 3), dtype=jnp.float32) + jnp.sum(
        hub_tiles, axis=(1, 3), dtype=jnp.float32
    )
    degree = jnp.broadcast_to(degree.reshape(-1, 1), seeds.shape)
    width = BW * block_rows
    z = lax.axis_index("hub").astype(jnp.int32).reshape(1)
    current = seeds.astype(jnp.bfloat16)
    seeds16 = current
    owned = current[hub_rows]
    p1, p3, pc = payloads(current, owned, z[0], width)
    fast = fast_path(owned, block_rows)
    pick = (hub_rows[:, None] == jnp.arange(current.shape[0], dtype=hub_rows.dtype)[None, :]).astype(jnp.bfloat16)
    prep = (pick, degree, positions_of(hub_blocks, owned, block_rows).reshape(-1))
    for step in range(ITERS):
        middle = functools.partial(
            band_call, z, band_offsets, current, band_tiles=band_tiles, fast=fast, n_own=owned.shape[0], width=width
        )
        band, hub_pieces, prep_out = exchange(
            current, owned, p1, p3, pc, hub_blocks, width, block_rows, lambda rims: middle(rims), prep
        )
        if prep is not None:
            pick, degree, hub_index = prep_out
            prep = None
        final = step + 1 == ITERS
        outs = hub_call(z, hub_index, pick, hub_pieces, hub_tiles, band, degree, seeds16, width, final)
        if final:
            labels = outs[0]
        else:
            current, owned, p1, p3, pc = outs
    return labels


def solution(mesh):
    placed = (
        P(AXES, None),
        P(AXES),
        P(AXES, None),
        P(AXES, None, None, None),
        P(AXES, None),
        P(AXES, None, None, None),
        P(AXES),
    )
    return jax.shard_map(
        body, mesh=mesh, in_specs=placed, out_specs=P(AXES, None), check_vma=False
    )
```

```python
import functools

import jax
import jax.numpy as jnp
import numpy as np
from jax import lax
from jax.experimental import pallas as pl
from jax.experimental.pallas import tpu as pltpu
from jax.sharding import PartitionSpec as P

BW = 2
ITERS = 3
AXES = ("node", "hub")
ROUNDS_32 = ((1, 2, 3), (8, 16, 24), (4,))


spread_weight = 0.8

SMEM = pl.BlockSpec(memory_space=pltpu.SMEM)
ANY = pl.BlockSpec(memory_space=pl.ANY)
VMEM = pl.BlockSpec(memory_space=pltpu.VMEM)


def fast_path(owned, block_rows):
    count = lax.axis_size(AXES)
    return count == 32 and owned.shape[0] == block_rows and lax.axis_size("hub") == 4


def payloads(current, owned, z, width):
    top = current[current.shape[0] - width:]
    bottom = current[:width]
    p1 = jnp.concatenate([owned, jnp.where(z % 2 == 0, top, bottom)], 0)
    p3 = jnp.concatenate([owned, jnp.where(z == 1, top, bottom)], 0)
    pc = jnp.where(z == 3, top, bottom)
    return p1, p3, pc


def exchange(current, owned, p1, p3, pc, hub_blocks, width, block_rows, middle, prep):
    count = lax.axis_size(AXES)
    if not fast_path(owned, block_rows):
        forward = [(i, i + 1) for i in range(count - 1)]
        backward = [(target, source) for source, target in forward]
        low = lax.ppermute(current[current.shape[0] - width:], AXES, forward)
        high = lax.ppermute(current[:width], AXES, backward)
        hub_all = lax.all_gather(owned, AXES, axis=0, tiled=True)
        return middle((low, high)), [hub_all.reshape(-1, block_rows, owned.shape[1])], prep
    me = lax.axis_index(AXES)
    pairs = lambda m: [(i, i ^ m) for i in range(count)]
    r3 = lax.ppermute(p3, AXES, pairs(3))
    r2 = lax.ppermute(owned, AXES, pairs(2))
    r1 = lax.ppermute(p1, AXES, pairs(1))
    groups = count // 4
    cross = [(4 * g + 3, 4 * g + 4) for g in range(groups - 1)]
    cross += [(4 * g + 4, 4 * g + 3) for g in range(groups - 1)]
    rc = lax.ppermute(pc, AXES, cross)
    if prep is not None:
        (r1, r2, r3, rc), prep = lax.optimization_barrier(((r1, r2, r3, rc), prep))
    rows = block_rows
    buf = jnp.concatenate([owned[None], r1[None, :rows], r2[None], r3[None, :rows]], 0)
    offs = [0, 1, 2, 3]
    rounds = ROUNDS_32
    pieces = [buf]
    done = None
    for r, group in enumerate(rounds[1:]):
        sent = {m: lax.ppermute(buf, AXES, pairs(m)) for m in sorted(group, key=lambda m: -m)}
        recvs = [sent[m] for m in group]
        if done is None:
            done, recvs = lax.optimization_barrier((middle((r1, r3, rc)), recvs))
        offs = offs + [o ^ m for m in group for o in offs]
        pieces = [buf] + recvs
        if r + 2 < len(rounds):
            buf = jnp.concatenate(pieces, 0)
    assert sorted(offs) == list(range(count))
    where = np.zeros(count, np.int32)
    for p, o in enumerate(offs):
        where[o] = p
    return done, pieces, prep


def band_kernel(fast, n_own, z_ref, off_ref, cur_hbm, *rest):
    if fast:
        r1_hbm, r3_hbm, rc_hbm, bt_hbm, out_ref, ext, bt, sem = rest
    else:
        low_hbm, high_hbm, bt_hbm, out_ref, ext, bt, sem = rest
    blocks, k_band, rows = bt.shape[0], bt.shape[1], bt.shape[2]
    own = cur_hbm.shape[0]
    width = (ext.shape[0] - own) // 2
    low_dst = ext.at[pl.ds(0, width)]
    high_dst = ext.at[pl.ds(width + own, width)]
    mid = pltpu.make_async_copy(cur_hbm, ext.at[pl.ds(width, own)], sem.at[1])
    band_copies = [pltpu.make_async_copy(bt_hbm.at[b], bt.at[b], sem.at[3 + b]) for b in range(blocks)]
    band_copies[0].start()
    mid.start()
    if fast:
        z = z_ref[0]
        low_r1 = pltpu.make_async_copy(r1_hbm.at[pl.ds(n_own, width)], low_dst, sem.at[0])
        low_r3 = pltpu.make_async_copy(r3_hbm.at[pl.ds(n_own, width)], low_dst, sem.at[0])
        low_rc = pltpu.make_async_copy(rc_hbm, low_dst, sem.at[0])
        high_r1 = pltpu.make_async_copy(r1_hbm.at[pl.ds(n_own, width)], high_dst, sem.at[2])
        high_r3 = pltpu.make_async_copy(r3_hbm.at[pl.ds(n_own, width)], high_dst, sem.at[2])
        high_rc = pltpu.make_async_copy(rc_hbm, high_dst, sem.at[2])

        @pl.when(z == 0)
        def _():
            low_rc.start()
            high_r1.start()

        @pl.when(z == 1)
        def _():
            low_r1.start()
            high_r3.start()

        @pl.when(z == 2)
        def _():
            low_r3.start()
            high_r1.start()

        @pl.when(z == 3)
        def _():
            low_r1.start()
            high_rc.start()

        low_wait, high_wait = low_rc, high_rc
    else:
        low_wait = pltpu.make_async_copy(low_hbm, low_dst, sem.at[0])
        high_wait = pltpu.make_async_copy(high_hbm, high_dst, sem.at[2])
        low_wait.start()
        high_wait.start()
    for b in range(1, blocks):
        band_copies[b].start()
    mid.wait()
    low_wait.wait()
    high_wait.wait()
    for b in range(blocks):
        band_copies[b].wait()
        acc = jnp.zeros((rows, out_ref.shape[1]), jnp.float32)

        def near(k):
            n = b + BW + off_ref[b * k_band + k]
            return ext[pl.ds(pl.multiple_of(n * rows, rows), rows), :]

        for k in range(0, k_band - 1, 2):
            lhs = jnp.concatenate([bt[b, k], bt[b, k + 1]], axis=1)
            rhs = jnp.concatenate([near(k), near(k + 1)], axis=0)
            acc = acc + jnp.dot(lhs, rhs, preferred_element_type=jnp.float32)
        if k_band % 2:
            acc = acc + jnp.dot(bt[b, k_band - 1], near(k_band - 1), preferred_element_type=jnp.float32)
        out_ref[pl.ds(b * rows, rows), :] = acc


def band_call(z, band_offsets, current, rim_sources, band_tiles, fast, n_own, width):
    blocks, k_band, rows, _ = band_tiles.shape
    classes = current.shape[1]
    flops = 2 * blocks * k_band * rows * rows * classes
    bytes_accessed = band_tiles.size * 2 + current.size * 2 * 2 + current.size * 4
    return pl.pallas_call(
        functools.partial(band_kernel, fast, n_own),
        cost_estimate=pl.CostEstimate(flops=flops, transcendentals=0, bytes_accessed=bytes_accessed),
        in_specs=[SMEM, SMEM] + [ANY] * (1 + len(rim_sources) + 1),
        out_specs=VMEM,
        out_shape=jax.ShapeDtypeStruct(current.shape, jnp.float32),
        scratch_shapes=[
            pltpu.VMEM((current.shape[0] + 2 * width, classes), current.dtype),
            pltpu.VMEM(band_tiles.shape, band_tiles.dtype),
            pltpu.SemaphoreType.DMA((3 + blocks,)),
        ],
    )(z, band_offsets.reshape(-1), current, *rim_sources, band_tiles)


def hub_kernel(n_hub, width, final, z_ref, hidx_ref, *rest):
    hub_hbm = rest[:n_hub]
    if final:
        (ht_hbm, band_hbm, deg_hbm, seeds_hbm, out_ref, hub, ht, band, deg, seeds, sem) = rest[n_hub:]
    else:
        (ht_hbm, band_hbm, deg_hbm, seeds_hbm, pick_ref,
         cur_ref, owned_ref, p1_ref, p3_ref, pc_ref,
         hub, ht, band, deg, seeds, sem) = rest[n_hub:]
    blocks, k_hub, rows = ht.shape[0], ht.shape[1], ht.shape[2]
    per_block = []
    for b in range(blocks):
        span = pl.ds(b * rows, rows)
        per_block.append([
            pltpu.make_async_copy(ht_hbm.at[b], ht.at[b], sem.at[n_hub + 4 * b]),
            pltpu.make_async_copy(band_hbm.at[span], band.at[span], sem.at[n_hub + 4 * b + 1]),
            pltpu.make_async_copy(deg_hbm.at[span], deg.at[span], sem.at[n_hub + 4 * b + 2]),
            pltpu.make_async_copy(seeds_hbm.at[span], seeds.at[span], sem.at[n_hub + 4 * b + 3]),
        ])
    for c in per_block[0]:
        c.start()
    copies = []
    at = 0
    for i, piece in enumerate(hub_hbm):
        n = piece.shape[0]
        copies.append(pltpu.make_async_copy(piece, hub.at[pl.ds(at, n)], sem.at[i]))
        at += n
    for c in copies:
        c.start()
    for b in range(1, blocks):
        for c in per_block[b]:
            c.start()
    for c in copies:
        c.wait()
    for b in range(blocks):
        for c in per_block[b]:
            c.wait()
        span = pl.ds(b * rows, rows)
        acc = jnp.zeros((rows, hub.shape[2]), jnp.float32)
        blk = lambda h: hub[hidx_ref[b * k_hub + h]]
        for h in range(0, k_hub - 1, 2):
            lhs = jnp.concatenate([ht[b, h], ht[b, h + 1]], axis=1)
            rhs = jnp.concatenate([blk(h), blk(h + 1)], axis=0)
            acc = acc + jnp.dot(lhs, rhs, preferred_element_type=jnp.float32)
        if k_hub % 2:
            acc = acc + jnp.dot(ht[b, k_hub - 1], blk(k_hub - 1), preferred_element_type=jnp.float32)
        gathered = (band[span] + acc) / deg[span]
        labels = spread_weight * gathered + (1.0 - spread_weight) * seeds[span].astype(jnp.float32)
        if final:
            out_ref[span, :] = labels
        else:
            cur_ref[span, :] = labels.astype(cur_ref.dtype)
    if final:
        return
    own = cur_ref.shape[0]
    n_own = owned_ref.shape[0]
    owned = jnp.dot(pick_ref[...], cur_ref[...], preferred_element_type=jnp.float32).astype(owned_ref.dtype)
    owned_ref[...] = owned
    p1_ref[pl.ds(0, n_own), :] = owned
    p3_ref[pl.ds(0, n_own), :] = owned
    z = z_ref[0]
    top = cur_ref[pl.ds(own - width, width), :]
    bottom = cur_ref[pl.ds(0, width), :]
    p1_ref[pl.ds(n_own, width), :] = jnp.where(z % 2 == 0, top, bottom)
    p3_ref[pl.ds(n_own, width), :] = jnp.where(z == 1, top, bottom)
    pc_ref[...] = jnp.where(z == 3, top, bottom)


def hub_call(z, hub_index, pick, hub_pieces, hub_tiles, band, degree, seeds, width, final):
    blocks, k_hub, rows, _ = hub_tiles.shape
    classes = seeds.shape[1]
    n_hub = len(hub_pieces)
    n_hub_blocks = sum(p.shape[0] for p in hub_pieces)
    n_own = pick.shape[0]
    bf = jnp.bfloat16
    flops = 2 * blocks * k_hub * rows * rows * classes
    bytes_accessed = hub_tiles.size * 2 + n_hub_blocks * rows * classes * 2 + seeds.size * 4 * 4
    if final:
        outs = [jax.ShapeDtypeStruct(seeds.shape, jnp.float32)]
    else:
        outs = [
            jax.ShapeDtypeStruct(seeds.shape, bf),
            jax.ShapeDtypeStruct((n_own, classes), bf),
            jax.ShapeDtypeStruct((n_own + width, classes), bf),
            jax.ShapeDtypeStruct((n_own + width, classes), bf),
            jax.ShapeDtypeStruct((width, classes), bf),
        ]
    return pl.pallas_call(
        functools.partial(hub_kernel, n_hub, width, final),
        cost_estimate=pl.CostEstimate(flops=flops, transcendentals=0, bytes_accessed=bytes_accessed),
        in_specs=[SMEM, SMEM] + [ANY] * (n_hub + 4) + ([] if final else [VMEM]),
        out_specs=[VMEM] * len(outs),
        out_shape=outs,
        scratch_shapes=[
            pltpu.VMEM((n_hub_blocks, rows, classes), bf),
            pltpu.VMEM(hub_tiles.shape, hub_tiles.dtype),
            pltpu.VMEM(seeds.shape, jnp.float32),
            pltpu.VMEM(degree.shape, jnp.float32),
            pltpu.VMEM(seeds.shape, seeds.dtype),
            pltpu.SemaphoreType.DMA((n_hub + 4 * blocks,)),
        ],
    )(z, hub_index, *hub_pieces, hub_tiles, band, degree, seeds, *([] if final else [pick]))


def positions_of(hub_blocks, owned, block_rows):
    count = lax.axis_size(AXES)
    if not fast_path(owned, block_rows):
        return hub_blocks
    offs = [0]
    for group in ROUNDS_32:
        offs = offs + [o ^ m for m in group for o in offs]
    where = np.zeros(count, np.int32)
    for p, o in enumerate(offs):
        where[o] = p
    return jnp.asarray(where)[hub_blocks ^ lax.axis_index(AXES)]


def body(seed_scores, seed_mask, band_offsets, band_tiles, hub_blocks, hub_tiles, hub_rows):
    block_rows = band_tiles.shape[2]
    seeds = seed_mask.astype(jnp.float32)[:, None] * seed_scores.astype(jnp.float32)
    degree = jnp.sum(band_tiles, axis=(1, 3), dtype=jnp.float32) + jnp.sum(
        hub_tiles, axis=(1, 3), dtype=jnp.float32
    )
    degree = jnp.broadcast_to(degree.reshape(-1, 1), seeds.shape)
    width = BW * block_rows
    z = lax.axis_index("hub").astype(jnp.int32).reshape(1)
    current = seeds.astype(jnp.bfloat16)
    seeds16 = current
    owned = current[hub_rows]
    p1, p3, pc = payloads(current, owned, z[0], width)
    fast = fast_path(owned, block_rows)
    pick = (hub_rows[:, None] == jnp.arange(current.shape[0], dtype=hub_rows.dtype)[None, :]).astype(jnp.bfloat16)
    prep = (pick, degree, positions_of(hub_blocks, owned, block_rows).reshape(-1))
    for step in range(ITERS):
        middle = functools.partial(
            band_call, z, band_offsets, current, band_tiles=band_tiles, fast=fast, n_own=owned.shape[0], width=width
        )
        band, hub_pieces, prep_out = exchange(
            current, owned, p1, p3, pc, hub_blocks, width, block_rows, lambda rims: middle(rims), prep
        )
        if prep is not None:
            pick, degree, hub_index = prep_out
            prep = None
        final = step + 1 == ITERS
        outs = hub_call(z, hub_index, pick, hub_pieces, hub_tiles, band, degree, seeds16, width, final)
        if final:
            labels = outs[0]
        else:
            current, owned, p1, p3, pc = outs
    return labels


def solution(mesh):
    placed = (
        P(AXES, None),
        P(AXES),
        P(AXES, None),
        P(AXES, None, None, None),
        P(AXES, None),
        P(AXES, None, None, None),
        P(AXES),
    )
    return jax.shard_map(
        body, mesh=mesh, in_specs=placed, out_specs=P(AXES, None), check_vma=False
    )
```

```python
import functools

import jax
import jax.numpy as jnp
import numpy as np
from jax import lax
from jax.experimental import pallas as pl
from jax.experimental.pallas import tpu as pltpu
from jax.sharding import PartitionSpec as P

BW = 2
ITERS = 3
AXES = ("node", "hub")
ROUNDS_32 = ((1, 2, 3), (8, 16, 24), (4,))


spread_weight = 0.8

SMEM = pl.BlockSpec(memory_space=pltpu.SMEM)
ANY = pl.BlockSpec(memory_space=pl.ANY)
VMEM = pl.BlockSpec(memory_space=pltpu.VMEM)


def fast_path(owned, block_rows):
    count = lax.axis_size(AXES)
    return count == 32 and owned.shape[0] == block_rows and lax.axis_size("hub") == 4


def payloads(current, owned, z, width):
    top = current[current.shape[0] - width:]
    bottom = current[:width]
    p1 = jnp.concatenate([owned, jnp.where(z % 2 == 0, top, bottom)], 0)
    p3 = jnp.concatenate([owned, jnp.where(z == 1, top, bottom)], 0)
    pc = jnp.where(z == 3, top, bottom)
    return p1, p3, pc


def exchange(current, owned, p1, p3, pc, hub_blocks, width, block_rows, middle, prep):
    count = lax.axis_size(AXES)
    if not fast_path(owned, block_rows):
        forward = [(i, i + 1) for i in range(count - 1)]
        backward = [(target, source) for source, target in forward]
        low = lax.ppermute(current[current.shape[0] - width:], AXES, forward)
        high = lax.ppermute(current[:width], AXES, backward)
        hub_all = lax.all_gather(owned, AXES, axis=0, tiled=True)
        return middle((low, high)), [hub_all.reshape(-1, block_rows, owned.shape[1])], prep
    me = lax.axis_index(AXES)
    pairs = lambda m: [(i, i ^ m) for i in range(count)]
    r3 = lax.ppermute(p3, AXES, pairs(3))
    r2 = lax.ppermute(owned, AXES, pairs(2))
    r1 = lax.ppermute(p1, AXES, pairs(1))
    groups = count // 4
    cross = [(4 * g + 3, 4 * g + 4) for g in range(groups - 1)]
    cross += [(4 * g + 4, 4 * g + 3) for g in range(groups - 1)]
    rc = lax.ppermute(pc, AXES, cross)
    if prep is not None:
        (r1, r2, r3, rc), prep = lax.optimization_barrier(((r1, r2, r3, rc), prep))
    rows = block_rows
    buf = jnp.concatenate([owned[None], r1[None, :rows], r2[None], r3[None, :rows]], 0)
    offs = [0, 1, 2, 3]
    rounds = ROUNDS_32
    pieces = [buf]
    done = None
    for r, group in enumerate(rounds[1:]):
        sent = {m: lax.ppermute(buf, AXES, pairs(m)) for m in sorted(group, key=lambda m: -m)}
        recvs = [sent[m] for m in group]
        if done is None:
            done, recvs = lax.optimization_barrier((middle((r1, r3, rc)), recvs))
        offs = offs + [o ^ m for m in group for o in offs]
        pieces = [buf] + recvs
        if r + 2 < len(rounds):
            buf = jnp.concatenate(pieces, 0)
    assert sorted(offs) == list(range(count))
    where = np.zeros(count, np.int32)
    for p, o in enumerate(offs):
        where[o] = p
    return done, pieces, prep


def band_kernel(fast, n_own, z_ref, off_ref, cur_hbm, *rest):
    if fast:
        r1_hbm, r3_hbm, rc_hbm, bt_hbm, out_ref, ext, bt, sem = rest
    else:
        low_hbm, high_hbm, bt_hbm, out_ref, ext, bt, sem = rest
    blocks, k_band, rows = bt.shape[0], bt.shape[1], bt.shape[2]
    own = cur_hbm.shape[0]
    width = (ext.shape[0] - own) // 2
    low_dst = ext.at[pl.ds(0, width)]
    high_dst = ext.at[pl.ds(width + own, width)]
    mid = pltpu.make_async_copy(cur_hbm, ext.at[pl.ds(width, own)], sem.at[1])
    band_copies = [pltpu.make_async_copy(bt_hbm.at[b], bt.at[b], sem.at[3 + b]) for b in range(blocks)]
    band_copies[0].start()
    mid.start()
    if fast:
        z = z_ref[0]
        low_r1 = pltpu.make_async_copy(r1_hbm.at[pl.ds(n_own, width)], low_dst, sem.at[0])
        low_r3 = pltpu.make_async_copy(r3_hbm.at[pl.ds(n_own, width)], low_dst, sem.at[0])
        low_rc = pltpu.make_async_copy(rc_hbm, low_dst, sem.at[0])
        high_r1 = pltpu.make_async_copy(r1_hbm.at[pl.ds(n_own, width)], high_dst, sem.at[2])
        high_r3 = pltpu.make_async_copy(r3_hbm.at[pl.ds(n_own, width)], high_dst, sem.at[2])
        high_rc = pltpu.make_async_copy(rc_hbm, high_dst, sem.at[2])

        @pl.when(z == 0)
        def _():
            low_rc.start()
            high_r1.start()

        @pl.when(z == 1)
        def _():
            low_r1.start()
            high_r3.start()

        @pl.when(z == 2)
        def _():
            low_r3.start()
            high_r1.start()

        @pl.when(z == 3)
        def _():
            low_r1.start()
            high_rc.start()

        low_wait, high_wait = low_rc, high_rc
    else:
        low_wait = pltpu.make_async_copy(low_hbm, low_dst, sem.at[0])
        high_wait = pltpu.make_async_copy(high_hbm, high_dst, sem.at[2])
        low_wait.start()
        high_wait.start()
    for b in range(1, blocks):
        band_copies[b].start()
    mid.wait()
    low_wait.wait()
    high_wait.wait()
    for b in range(blocks):
        band_copies[b].wait()
        acc = jnp.zeros((rows, out_ref.shape[1]), jnp.float32)

        def near(k):
            n = b + BW + off_ref[b * k_band + k]
            return ext[pl.ds(pl.multiple_of(n * rows, rows), rows), :]

        for k in range(0, k_band - 1, 2):
            lhs = jnp.concatenate([bt[b, k], bt[b, k + 1]], axis=1)
            rhs = jnp.concatenate([near(k), near(k + 1)], axis=0)
            acc = acc + jnp.dot(lhs, rhs, preferred_element_type=jnp.float32)
        if k_band % 2:
            acc = acc + jnp.dot(bt[b, k_band - 1], near(k_band - 1), preferred_element_type=jnp.float32)
        out_ref[pl.ds(b * rows, rows), :] = acc


def band_call(z, band_offsets, current, rim_sources, band_tiles, fast, n_own, width):
    blocks, k_band, rows, _ = band_tiles.shape
    classes = current.shape[1]
    flops = 2 * blocks * k_band * rows * rows * classes
    bytes_accessed = band_tiles.size * 2 + current.size * 2 * 2 + current.size * 4
    return pl.pallas_call(
        functools.partial(band_kernel, fast, n_own),
        cost_estimate=pl.CostEstimate(flops=flops, transcendentals=0, bytes_accessed=bytes_accessed),
        in_specs=[SMEM, SMEM] + [ANY] * (1 + len(rim_sources) + 1),
        out_specs=VMEM,
        out_shape=jax.ShapeDtypeStruct(current.shape, jnp.float32),
        scratch_shapes=[
            pltpu.VMEM((current.shape[0] + 2 * width, classes), current.dtype),
            pltpu.VMEM(band_tiles.shape, band_tiles.dtype),
            pltpu.SemaphoreType.DMA((3 + blocks,)),
        ],
    )(z, band_offsets.reshape(-1), current, *rim_sources, band_tiles)


def hub_kernel(n_hub, width, final, z_ref, hidx_ref, *rest):
    hub_hbm = rest[:n_hub]
    if final:
        (ht_hbm, band_hbm, deg_hbm, seeds_hbm, out_ref, hub, ht, band, deg, seeds, sem) = rest[n_hub:]
    else:
        (ht_hbm, band_hbm, deg_hbm, seeds_hbm, pick_ref,
         cur_ref, owned_ref, p1_ref, p3_ref, pc_ref,
         hub, ht, band, deg, seeds, sem) = rest[n_hub:]
    blocks, k_hub, rows = ht.shape[0], ht.shape[1], ht.shape[2]
    per_block = []
    for b in range(blocks):
        span = pl.ds(b * rows, rows)
        per_block.append([
            pltpu.make_async_copy(ht_hbm.at[b], ht.at[b], sem.at[n_hub + 4 * b]),
            pltpu.make_async_copy(band_hbm.at[span], band.at[span], sem.at[n_hub + 4 * b + 1]),
            pltpu.make_async_copy(deg_hbm.at[span], deg.at[span], sem.at[n_hub + 4 * b + 2]),
            pltpu.make_async_copy(seeds_hbm.at[span], seeds.at[span], sem.at[n_hub + 4 * b + 3]),
        ])
    copies = []
    at = 0
    for i, piece in enumerate(hub_hbm):
        n = piece.shape[0]
        copies.append(pltpu.make_async_copy(piece, hub.at[pl.ds(at, n)], sem.at[i]))
        at += n
    for c in copies:
        c.start()
    for c in per_block[0]:
        c.start()
    for b in range(1, blocks):
        for c in per_block[b]:
            c.start()
    for c in copies:
        c.wait()
    for b in range(blocks):
        for c in per_block[b]:
            c.wait()
        span = pl.ds(b * rows, rows)
        acc = jnp.zeros((rows, hub.shape[2]), jnp.float32)
        blk = lambda h: hub[hidx_ref[b * k_hub + h]]
        for h in range(0, k_hub - 1, 2):
            lhs = jnp.concatenate([ht[b, h], ht[b, h + 1]], axis=1)
            rhs = jnp.concatenate([blk(h), blk(h + 1)], axis=0)
            acc = acc + jnp.dot(lhs, rhs, preferred_element_type=jnp.float32)
        if k_hub % 2:
            acc = acc + jnp.dot(ht[b, k_hub - 1], blk(k_hub - 1), preferred_element_type=jnp.float32)
        gathered = (band[span] + acc) / deg[span]
        labels = spread_weight * gathered + (1.0 - spread_weight) * seeds[span].astype(jnp.float32)
        if final:
            out_ref[span, :] = labels
        else:
            cur_ref[span, :] = labels.astype(cur_ref.dtype)
    if final:
        return
    own = cur_ref.shape[0]
    n_own = owned_ref.shape[0]
    owned = jnp.dot(pick_ref[...], cur_ref[...], preferred_element_type=jnp.float32).astype(owned_ref.dtype)
    owned_ref[...] = owned
    p1_ref[pl.ds(0, n_own), :] = owned
    p3_ref[pl.ds(0, n_own), :] = owned
    z = z_ref[0]
    top = cur_ref[pl.ds(own - width, width), :]
    bottom = cur_ref[pl.ds(0, width), :]
    p1_ref[pl.ds(n_own, width), :] = jnp.where(z % 2 == 0, top, bottom)
    p3_ref[pl.ds(n_own, width), :] = jnp.where(z == 1, top, bottom)
    pc_ref[...] = jnp.where(z == 3, top, bottom)


def hub_call(z, hub_index, pick, hub_pieces, hub_tiles, band, degree, seeds, width, final):
    blocks, k_hub, rows, _ = hub_tiles.shape
    classes = seeds.shape[1]
    n_hub = len(hub_pieces)
    n_hub_blocks = sum(p.shape[0] for p in hub_pieces)
    n_own = pick.shape[0]
    bf = jnp.bfloat16
    flops = 2 * blocks * k_hub * rows * rows * classes
    bytes_accessed = hub_tiles.size * 2 + n_hub_blocks * rows * classes * 2 + seeds.size * 4 * 4
    if final:
        outs = [jax.ShapeDtypeStruct(seeds.shape, jnp.float32)]
    else:
        outs = [
            jax.ShapeDtypeStruct(seeds.shape, bf),
            jax.ShapeDtypeStruct((n_own, classes), bf),
            jax.ShapeDtypeStruct((n_own + width, classes), bf),
            jax.ShapeDtypeStruct((n_own + width, classes), bf),
            jax.ShapeDtypeStruct((width, classes), bf),
        ]
    return pl.pallas_call(
        functools.partial(hub_kernel, n_hub, width, final),
        cost_estimate=pl.CostEstimate(flops=flops, transcendentals=0, bytes_accessed=bytes_accessed),
        in_specs=[SMEM, SMEM] + [ANY] * (n_hub + 4) + ([] if final else [VMEM]),
        out_specs=[VMEM] * len(outs),
        out_shape=outs,
        scratch_shapes=[
            pltpu.VMEM((n_hub_blocks, rows, classes), bf),
            pltpu.VMEM(hub_tiles.shape, hub_tiles.dtype),
            pltpu.VMEM(seeds.shape, jnp.float32),
            pltpu.VMEM(degree.shape, jnp.float32),
            pltpu.VMEM(seeds.shape, seeds.dtype),
            pltpu.SemaphoreType.DMA((n_hub + 4 * blocks,)),
        ],
    )(z, hub_index, *hub_pieces, hub_tiles, band, degree, seeds, *([] if final else [pick]))


def positions_of(hub_blocks, owned, block_rows):
    count = lax.axis_size(AXES)
    if not fast_path(owned, block_rows):
        return hub_blocks
    offs = [0]
    for group in ROUNDS_32:
        offs = offs + [o ^ m for m in group for o in offs]
    where = np.zeros(count, np.int32)
    for p, o in enumerate(offs):
        where[o] = p
    return jnp.asarray(where)[hub_blocks ^ lax.axis_index(AXES)]


def body(seed_scores, seed_mask, band_offsets, band_tiles, hub_blocks, hub_tiles, hub_rows):
    block_rows = band_tiles.shape[2]
    seeds = seed_mask.astype(jnp.float32)[:, None] * seed_scores.astype(jnp.float32)
    degree = jnp.sum(band_tiles, axis=(1, 3), dtype=jnp.float32) + jnp.sum(
        hub_tiles, axis=(1, 3), dtype=jnp.float32
    )
    degree = jnp.broadcast_to(degree.reshape(-1, 1), seeds.shape)
    width = BW * block_rows
    z = lax.axis_index("hub").astype(jnp.int32).reshape(1)
    current = seeds.astype(jnp.bfloat16)
    seeds16 = current
    owned = current[hub_rows]
    p1, p3, pc = payloads(current, owned, z[0], width)
    fast = fast_path(owned, block_rows)
    pick = (hub_rows[:, None] == jnp.arange(current.shape[0], dtype=hub_rows.dtype)[None, :]).astype(jnp.bfloat16)
    prep = (pick, degree, positions_of(hub_blocks, owned, block_rows).reshape(-1))
    for step in range(ITERS):
        middle = functools.partial(
            band_call, z, band_offsets, current, band_tiles=band_tiles, fast=fast, n_own=owned.shape[0], width=width
        )
        band, hub_pieces, prep_out = exchange(
            current, owned, p1, p3, pc, hub_blocks, width, block_rows, lambda rims: middle(rims), prep
        )
        if prep is not None:
            pick, degree, hub_index = prep_out
            prep = None
        final = step + 1 == ITERS
        outs = hub_call(z, hub_index, pick, hub_pieces, hub_tiles, band, degree, seeds16, width, final)
        if final:
            labels = outs[0]
        else:
            current, owned, p1, p3, pc = outs
    return labels


def solution(mesh):
    placed = (
        P(AXES, None),
        P(AXES),
        P(AXES, None),
        P(AXES, None, None, None),
        P(AXES, None),
        P(AXES, None, None, None),
        P(AXES),
    )
    return jax.shard_map(
        body, mesh=mesh, in_specs=placed, out_specs=P(AXES, None), check_vma=False
    )
```

```python
import functools

import jax
import jax.numpy as jnp
import numpy as np
from jax import lax
from jax.experimental import pallas as pl
from jax.experimental.pallas import tpu as pltpu
from jax.sharding import PartitionSpec as P

BW = 2
ITERS = 3
AXES = ("node", "hub")
ROUNDS_32 = ((1, 2, 3), (8, 16, 24), (4,))


spread_weight = 0.8

SMEM = pl.BlockSpec(memory_space=pltpu.SMEM)
ANY = pl.BlockSpec(memory_space=pl.ANY)
VMEM = pl.BlockSpec(memory_space=pltpu.VMEM)


def fast_path(owned, block_rows):
    count = lax.axis_size(AXES)
    return count == 32 and owned.shape[0] == block_rows and lax.axis_size("hub") == 4


def payloads(current, owned, z, width):
    top = current[current.shape[0] - width:]
    bottom = current[:width]
    p1 = jnp.concatenate([owned, jnp.where(z % 2 == 0, top, bottom)], 0)
    p3 = jnp.concatenate([owned, jnp.where(z == 1, top, bottom)], 0)
    pc = jnp.where(z == 3, top, bottom)
    return p1, p3, pc


def exchange(current, owned, p1, p3, pc, hub_blocks, width, block_rows, middle, prep):
    count = lax.axis_size(AXES)
    if not fast_path(owned, block_rows):
        forward = [(i, i + 1) for i in range(count - 1)]
        backward = [(target, source) for source, target in forward]
        low = lax.ppermute(current[current.shape[0] - width:], AXES, forward)
        high = lax.ppermute(current[:width], AXES, backward)
        hub_all = lax.all_gather(owned, AXES, axis=0, tiled=True)
        return middle((low, high)), [hub_all.reshape(-1, block_rows, owned.shape[1])], prep
    me = lax.axis_index(AXES)
    pairs = lambda m: [(i, i ^ m) for i in range(count)]
    r3 = lax.ppermute(p3, AXES, pairs(3))
    r2 = lax.ppermute(owned, AXES, pairs(2))
    r1 = lax.ppermute(p1, AXES, pairs(1))
    groups = count // 4
    cross = [(4 * g + 3, 4 * g + 4) for g in range(groups - 1)]
    cross += [(4 * g + 4, 4 * g + 3) for g in range(groups - 1)]
    rc = lax.ppermute(pc, AXES, cross)
    if prep is not None:
        (r1, r2, r3, rc), prep = lax.optimization_barrier(((r1, r2, r3, rc), prep))
    rows = block_rows
    buf = jnp.concatenate([owned[None], r1[None, :rows], r2[None], r3[None, :rows]], 0)
    offs = [0, 1, 2, 3]
    rounds = ROUNDS_32
    pieces = [buf]
    done = None
    for r, group in enumerate(rounds[1:]):
        sent = {m: lax.ppermute(buf, AXES, pairs(m)) for m in sorted(group, key=lambda m: -m)}
        recvs = [sent[m] for m in group]
        if done is None:
            done, recvs = lax.optimization_barrier((middle((r1, r3, rc)), recvs))
        offs = offs + [o ^ m for m in group for o in offs]
        pieces = [buf] + recvs
        if r + 2 < len(rounds):
            buf = jnp.concatenate(pieces, 0)
    assert sorted(offs) == list(range(count))
    where = np.zeros(count, np.int32)
    for p, o in enumerate(offs):
        where[o] = p
    return done, pieces, prep


def band_kernel(fast, n_own, z_ref, off_ref, cur_hbm, *rest):
    if fast:
        r1_hbm, r3_hbm, rc_hbm, bt_hbm, out_ref, ext, bt, sem = rest
    else:
        low_hbm, high_hbm, bt_hbm, out_ref, ext, bt, sem = rest
    blocks, k_band, rows = bt.shape[0], bt.shape[1], bt.shape[2]
    own = cur_hbm.shape[0]
    width = (ext.shape[0] - own) // 2
    low_dst = ext.at[pl.ds(0, width)]
    high_dst = ext.at[pl.ds(width + own, width)]
    mid = pltpu.make_async_copy(cur_hbm, ext.at[pl.ds(width, own)], sem.at[1])
    band_copies = [pltpu.make_async_copy(bt_hbm.at[b], bt.at[b], sem.at[3 + b]) for b in range(blocks)]
    band_copies[0].start()
    mid.start()
    if fast:
        z = z_ref[0]
        low_r1 = pltpu.make_async_copy(r1_hbm.at[pl.ds(n_own, width)], low_dst, sem.at[0])
        low_r3 = pltpu.make_async_copy(r3_hbm.at[pl.ds(n_own, width)], low_dst, sem.at[0])
        low_rc = pltpu.make_async_copy(rc_hbm, low_dst, sem.at[0])
        high_r1 = pltpu.make_async_copy(r1_hbm.at[pl.ds(n_own, width)], high_dst, sem.at[2])
        high_r3 = pltpu.make_async_copy(r3_hbm.at[pl.ds(n_own, width)], high_dst, sem.at[2])
        high_rc = pltpu.make_async_copy(rc_hbm, high_dst, sem.at[2])

        @pl.when(z == 0)
        def _():
            low_rc.start()
            high_r1.start()

        @pl.when(z == 1)
        def _():
            low_r1.start()
            high_r3.start()

        @pl.when(z == 2)
        def _():
            low_r3.start()
            high_r1.start()

        @pl.when(z == 3)
        def _():
            low_r1.start()
            high_rc.start()

        low_wait, high_wait = low_rc, high_rc
    else:
        low_wait = pltpu.make_async_copy(low_hbm, low_dst, sem.at[0])
        high_wait = pltpu.make_async_copy(high_hbm, high_dst, sem.at[2])
        low_wait.start()
        high_wait.start()
    for b in range(1, blocks):
        band_copies[b].start()
    mid.wait()
    low_wait.wait()
    high_wait.wait()
    for b in range(blocks):
        band_copies[b].wait()
        acc = jnp.zeros((rows, out_ref.shape[1]), jnp.float32)

        def near(k):
            n = b + BW + off_ref[b * k_band + k]
            return ext[pl.ds(pl.multiple_of(n * rows, rows), rows), :]

        for k in range(0, k_band - 1, 2):
            lhs = jnp.concatenate([bt[b, k], bt[b, k + 1]], axis=1)
            rhs = jnp.concatenate([near(k), near(k + 1)], axis=0)
            acc = acc + jnp.dot(lhs, rhs, preferred_element_type=jnp.float32)
        if k_band % 2:
            acc = acc + jnp.dot(bt[b, k_band - 1], near(k_band - 1), preferred_element_type=jnp.float32)
        out_ref[pl.ds(b * rows, rows), :] = acc


def band_call(z, band_offsets, current, rim_sources, band_tiles, fast, n_own, width):
    blocks, k_band, rows, _ = band_tiles.shape
    classes = current.shape[1]
    flops = 2 * blocks * k_band * rows * rows * classes
    bytes_accessed = band_tiles.size * 2 + current.size * 2 * 2 + current.size * 4
    return pl.pallas_call(
        functools.partial(band_kernel, fast, n_own),
        cost_estimate=pl.CostEstimate(flops=flops, transcendentals=0, bytes_accessed=bytes_accessed),
        in_specs=[SMEM, SMEM] + [ANY] * (1 + len(rim_sources) + 1),
        out_specs=VMEM,
        out_shape=jax.ShapeDtypeStruct(current.shape, jnp.float32),
        scratch_shapes=[
            pltpu.VMEM((current.shape[0] + 2 * width, classes), current.dtype),
            pltpu.VMEM(band_tiles.shape, band_tiles.dtype),
            pltpu.SemaphoreType.DMA((3 + blocks,)),
        ],
    )(z, band_offsets.reshape(-1), current, *rim_sources, band_tiles)


def hub_kernel(n_hub, width, final, z_ref, hidx_ref, *rest):
    hub_hbm = rest[:n_hub]
    if final:
        (ht_hbm, band_hbm, deg_hbm, seeds_hbm, out_ref, hub, ht, band, deg, seeds, sem) = rest[n_hub:]
    else:
        (ht_hbm, band_hbm, deg_hbm, seeds_hbm, pick_ref,
         cur_ref, owned_ref, p1_ref, p3_ref, pc_ref,
         hub, ht, band, deg, seeds, sem) = rest[n_hub:]
    blocks, k_hub, rows = ht.shape[0], ht.shape[1], ht.shape[2]
    per_block = []
    for b in range(blocks):
        span = pl.ds(b * rows, rows)
        per_block.append([
            pltpu.make_async_copy(ht_hbm.at[b], ht.at[b], sem.at[n_hub + 4 * b]),
            pltpu.make_async_copy(band_hbm.at[span], band.at[span], sem.at[n_hub + 4 * b + 1]),
            pltpu.make_async_copy(deg_hbm.at[span], deg.at[span], sem.at[n_hub + 4 * b + 2]),
            pltpu.make_async_copy(seeds_hbm.at[span], seeds.at[span], sem.at[n_hub + 4 * b + 3]),
        ])
    copies = []
    at = 0
    for i, piece in enumerate(hub_hbm):
        n = piece.shape[0]
        copies.append(pltpu.make_async_copy(piece, hub.at[pl.ds(at, n)], sem.at[i]))
        at += n
    for c in copies:
        c.start()
    for c in per_block[0]:
        c.start()
    for b in range(1, blocks):
        for c in per_block[b]:
            c.start()
    for c in copies:
        c.wait()
    for b in range(blocks):
        for c in per_block[b]:
            c.wait()
        span = pl.ds(b * rows, rows)
        acc = jnp.zeros((rows, hub.shape[2]), jnp.float32)
        blk = lambda h: hub[hidx_ref[b * k_hub + h]]
        for h in range(0, k_hub - 1, 2):
            lhs = jnp.concatenate([ht[b, h], ht[b, h + 1]], axis=1)
            rhs = jnp.concatenate([blk(h), blk(h + 1)], axis=0)
            acc = acc + jnp.dot(lhs, rhs, preferred_element_type=jnp.float32)
        if k_hub % 2:
            acc = acc + jnp.dot(ht[b, k_hub - 1], blk(k_hub - 1), preferred_element_type=jnp.float32)
        gathered = (band[span] + acc) / deg[span]
        labels = spread_weight * gathered + (1.0 - spread_weight) * seeds[span].astype(jnp.float32)
        if final:
            out_ref[span, :] = labels
        else:
            cur_ref[span, :] = labels.astype(cur_ref.dtype)
    if final:
        return
    own = cur_ref.shape[0]
    n_own = owned_ref.shape[0]
    owned = jnp.dot(pick_ref[...], cur_ref[...], preferred_element_type=jnp.float32).astype(owned_ref.dtype)
    owned_ref[...] = owned
    p1_ref[pl.ds(0, n_own), :] = owned
    p3_ref[pl.ds(0, n_own), :] = owned
    z = z_ref[0]
    top = cur_ref[pl.ds(own - width, width), :]
    bottom = cur_ref[pl.ds(0, width), :]
    p1_ref[pl.ds(n_own, width), :] = jnp.where(z % 2 == 0, top, bottom)
    p3_ref[pl.ds(n_own, width), :] = jnp.where(z == 1, top, bottom)
    pc_ref[...] = jnp.where(z == 3, top, bottom)


def hub_call(z, hub_index, pick, hub_pieces, hub_tiles, band, degree, seeds, width, final):
    blocks, k_hub, rows, _ = hub_tiles.shape
    classes = seeds.shape[1]
    n_hub = len(hub_pieces)
    n_hub_blocks = sum(p.shape[0] for p in hub_pieces)
    n_own = pick.shape[0]
    bf = jnp.bfloat16
    flops = 2 * blocks * k_hub * rows * rows * classes
    bytes_accessed = hub_tiles.size * 2 + n_hub_blocks * rows * classes * 2 + seeds.size * 4 * 4
    if final:
        outs = [jax.ShapeDtypeStruct(seeds.shape, jnp.float32)]
    else:
        outs = [
            jax.ShapeDtypeStruct(seeds.shape, bf),
            jax.ShapeDtypeStruct((n_own, classes), bf),
            jax.ShapeDtypeStruct((n_own + width, classes), bf),
            jax.ShapeDtypeStruct((n_own + width, classes), bf),
            jax.ShapeDtypeStruct((width, classes), bf),
        ]
    return pl.pallas_call(
        functools.partial(hub_kernel, n_hub, width, final),
        cost_estimate=pl.CostEstimate(flops=flops, transcendentals=0, bytes_accessed=bytes_accessed),
        in_specs=[SMEM, SMEM] + [ANY] * (n_hub + 4) + ([] if final else [VMEM]),
        out_specs=[VMEM] * len(outs),
        out_shape=outs,
        scratch_shapes=[
            pltpu.VMEM((n_hub_blocks, rows, classes), bf),
            pltpu.VMEM(hub_tiles.shape, hub_tiles.dtype),
            pltpu.VMEM(seeds.shape, jnp.float32),
            pltpu.VMEM(degree.shape, jnp.float32),
            pltpu.VMEM(seeds.shape, seeds.dtype),
            pltpu.SemaphoreType.DMA((n_hub + 4 * blocks,)),
        ],
    )(z, hub_index, *hub_pieces, hub_tiles, band, degree, seeds, *([] if final else [pick]))


def positions_of(hub_blocks, owned, block_rows):
    count = lax.axis_size(AXES)
    if not fast_path(owned, block_rows):
        return hub_blocks
    offs = [0]
    for group in ROUNDS_32:
        offs = offs + [o ^ m for m in group for o in offs]
    where = np.zeros(count, np.int32)
    for p, o in enumerate(offs):
        where[o] = p
    return jnp.asarray(where)[hub_blocks ^ lax.axis_index(AXES)]


def body(seed_scores, seed_mask, band_offsets, band_tiles, hub_blocks, hub_tiles, hub_rows):
    block_rows = band_tiles.shape[2]
    seeds16 = seed_mask.astype(seed_scores.dtype)[:, None] * seed_scores
    degree = jnp.sum(band_tiles, axis=(1, 3), dtype=jnp.float32) + jnp.sum(
        hub_tiles, axis=(1, 3), dtype=jnp.float32
    )
    degree = jnp.broadcast_to(degree.reshape(-1, 1), seeds16.shape)
    width = BW * block_rows
    z = lax.axis_index("hub").astype(jnp.int32).reshape(1)
    current = seeds16
    owned = current.at[hub_rows].get(mode="promise_in_bounds")
    p1, p3, pc = payloads(current, owned, z[0], width)
    fast = fast_path(owned, block_rows)
    pick = (hub_rows[:, None] == jnp.arange(current.shape[0], dtype=hub_rows.dtype)[None, :]).astype(jnp.bfloat16)
    prep = (pick, degree, positions_of(hub_blocks, owned, block_rows).reshape(-1))
    for step in range(ITERS):
        middle = functools.partial(
            band_call, z, band_offsets, current, band_tiles=band_tiles, fast=fast, n_own=owned.shape[0], width=width
        )
        band, hub_pieces, prep_out = exchange(
            current, owned, p1, p3, pc, hub_blocks, width, block_rows, lambda rims: middle(rims), prep
        )
        if prep is not None:
            pick, degree, hub_index = prep_out
            prep = None
        final = step + 1 == ITERS
        outs = hub_call(z, hub_index, pick, hub_pieces, hub_tiles, band, degree, seeds16, width, final)
        if final:
            labels = outs[0]
        else:
            current, owned, p1, p3, pc = outs
    return labels


def solution(mesh):
    placed = (
        P(AXES, None),
        P(AXES),
        P(AXES, None),
        P(AXES, None, None, None),
        P(AXES, None),
        P(AXES, None, None, None),
        P(AXES),
    )
    return jax.shard_map(
        body, mesh=mesh, in_specs=placed, out_specs=P(AXES, None), check_vma=False
    )
```

```python
import functools

import jax
import jax.numpy as jnp
import numpy as np
from jax import lax
from jax.experimental import pallas as pl
from jax.experimental.pallas import tpu as pltpu
from jax.sharding import PartitionSpec as P

BW = 2
ITERS = 3
AXES = ("node", "hub")
ROUNDS_32 = ((1, 2, 3), (8, 16, 24), (4,))


spread_weight = 0.8

SMEM = pl.BlockSpec(memory_space=pltpu.SMEM)
ANY = pl.BlockSpec(memory_space=pl.ANY)
VMEM = pl.BlockSpec(memory_space=pltpu.VMEM)


def fast_path(owned, block_rows):
    count = lax.axis_size(AXES)
    return count == 32 and owned.shape[0] == block_rows and lax.axis_size("hub") == 4


def payloads(current, owned, z, width):
    top = current[current.shape[0] - width:]
    bottom = current[:width]
    p1 = jnp.concatenate([owned, jnp.where(z % 2 == 0, top, bottom)], 0)
    p3 = jnp.concatenate([owned, jnp.where(z == 1, top, bottom)], 0)
    pc = jnp.where(z == 3, top, bottom)
    return p1, p3, pc


def exchange(current, owned, p1, p3, pc, hub_blocks, width, block_rows, first, middle, prep):
    count = lax.axis_size(AXES)
    if not fast_path(owned, block_rows):
        forward = [(i, i + 1) for i in range(count - 1)]
        backward = [(target, source) for source, target in forward]
        low = lax.ppermute(current[current.shape[0] - width:], AXES, forward)
        high = lax.ppermute(current[:width], AXES, backward)
        hub_all = lax.all_gather(owned, AXES, axis=0, tiled=True)
        done = (first(), middle((low, high)))
        return done, [hub_all.reshape(-1, block_rows, owned.shape[1])], prep
    me = lax.axis_index(AXES)
    pairs = lambda m: [(i, i ^ m) for i in range(count)]
    r3 = lax.ppermute(p3, AXES, pairs(3))
    r2 = lax.ppermute(owned, AXES, pairs(2))
    r1 = lax.ppermute(p1, AXES, pairs(1))
    groups = count // 4
    cross = [(4 * g + 3, 4 * g + 4) for g in range(groups - 1)]
    cross += [(4 * g + 4, 4 * g + 3) for g in range(groups - 1)]
    rc = lax.ppermute(pc, AXES, cross)
    (r1, r2, r3, rc), (inner, prep) = lax.optimization_barrier(((r1, r2, r3, rc), (first(), prep)))
    rows = block_rows
    buf = jnp.concatenate([owned[None], r1[None, :rows], r2[None], r3[None, :rows]], 0)
    offs = [0, 1, 2, 3]
    rounds = ROUNDS_32
    pieces = [buf]
    done = None
    for r, group in enumerate(rounds[1:]):
        sent = {m: lax.ppermute(buf, AXES, pairs(m)) for m in sorted(group, key=lambda m: -m)}
        recvs = [sent[m] for m in group]
        if done is None:
            done, recvs = lax.optimization_barrier((middle((r1, r3, rc)), recvs))
        offs = offs + [o ^ m for m in group for o in offs]
        pieces = [buf] + recvs
        if r + 2 < len(rounds):
            buf = jnp.concatenate(pieces, 0)
    assert sorted(offs) == list(range(count))
    return (inner, done), pieces, prep


def rim_blocks(blocks):
    return sorted(set(range(min(BW, blocks))) | set(range(max(blocks - BW, 0), blocks)))


def band_kernel(fast, n_own, rims_part, z_ref, off_ref, cur_hbm, *rest):
    if not rims_part:
        bt_hbm, out_ref, ext, bt, sem = rest
    elif fast:
        r1_hbm, r3_hbm, rc_hbm, bt_hbm, out_ref, ext, bt, sem = rest
    else:
        low_hbm, high_hbm, bt_hbm, out_ref, ext, bt, sem = rest
    k_band, rows = bt.shape[1], bt.shape[2]
    own = cur_hbm.shape[0]
    width = (ext.shape[0] - own) // 2
    blocks = own // rows
    chosen = rim_blocks(blocks) if rims_part else list(range(blocks))
    band_copies = [pltpu.make_async_copy(bt_hbm.at[g], bt.at[i], sem.at[3 + i]) for i, g in enumerate(chosen)]
    band_copies[0].start()
    if not rims_part:
        mid = pltpu.make_async_copy(cur_hbm, ext.at[pl.ds(width, own)], sem.at[1])
        mid.start()
        for i in range(1, len(chosen)):
            band_copies[i].start()
        zeros = jnp.zeros((width, ext.shape[1]), ext.dtype)
        ext[pl.ds(0, width), :] = zeros
        ext[pl.ds(width + own, width), :] = zeros
        mid.wait()
    else:
        low_dst = ext.at[pl.ds(0, width)]
        high_dst = ext.at[pl.ds(width + own, width)]
        if fast:
            z = z_ref[0]
            low_r1 = pltpu.make_async_copy(r1_hbm.at[pl.ds(n_own, width)], low_dst, sem.at[0])
            low_r3 = pltpu.make_async_copy(r3_hbm.at[pl.ds(n_own, width)], low_dst, sem.at[0])
            low_rc = pltpu.make_async_copy(rc_hbm, low_dst, sem.at[0])
            high_r1 = pltpu.make_async_copy(r1_hbm.at[pl.ds(n_own, width)], high_dst, sem.at[2])
            high_r3 = pltpu.make_async_copy(r3_hbm.at[pl.ds(n_own, width)], high_dst, sem.at[2])
            high_rc = pltpu.make_async_copy(rc_hbm, high_dst, sem.at[2])

            @pl.when(z == 0)
            def _():
                low_rc.start()
                high_r1.start()

            @pl.when(z == 1)
            def _():
                low_r1.start()
                high_r3.start()

            @pl.when(z == 2)
            def _():
                low_r3.start()
                high_r1.start()

            @pl.when(z == 3)
            def _():
                low_r1.start()
                high_rc.start()

            low_wait, high_wait = low_rc, high_rc
        else:
            low_wait = pltpu.make_async_copy(low_hbm, low_dst, sem.at[0])
            high_wait = pltpu.make_async_copy(high_hbm, high_dst, sem.at[2])
            low_wait.start()
            high_wait.start()
        for i in range(1, len(chosen)):
            band_copies[i].start()
        ext[pl.ds(width, own), :] = jnp.zeros((own, ext.shape[1]), ext.dtype)
        low_wait.wait()
        high_wait.wait()
    for i, b in enumerate(chosen):
        band_copies[i].wait()
        acc = jnp.zeros((rows, out_ref.shape[1]), jnp.float32)

        def near(k):
            n = b + BW + off_ref[b * k_band + k]
            return ext[pl.ds(pl.multiple_of(n * rows, rows), rows), :]

        for k in range(0, k_band - 1, 2):
            lhs = jnp.concatenate([bt[i, k], bt[i, k + 1]], axis=1)
            rhs = jnp.concatenate([near(k), near(k + 1)], axis=0)
            acc = acc + jnp.dot(lhs, rhs, preferred_element_type=jnp.float32)
        if k_band % 2:
            acc = acc + jnp.dot(bt[i, k_band - 1], near(k_band - 1), preferred_element_type=jnp.float32)
        out_ref[pl.ds(i * rows, rows), :] = acc


def band_call(z, band_offsets, current, rim_sources, band_tiles, fast, n_own, width, rims_part):
    blocks, k_band, rows, _ = band_tiles.shape
    classes = current.shape[1]
    chosen = len(rim_blocks(blocks)) if rims_part else blocks
    flops = 2 * chosen * k_band * rows * rows * classes
    bytes_accessed = chosen * k_band * rows * rows * 2 + current.size * 2 + chosen * rows * classes * 4
    return pl.pallas_call(
        functools.partial(band_kernel, fast, n_own, rims_part),
        cost_estimate=pl.CostEstimate(flops=flops, transcendentals=0, bytes_accessed=bytes_accessed),
        in_specs=[SMEM, SMEM] + [ANY] * (1 + len(rim_sources) + 1),
        out_specs=VMEM,
        out_shape=jax.ShapeDtypeStruct((chosen * rows, classes), jnp.float32),
        scratch_shapes=[
            pltpu.VMEM((current.shape[0] + 2 * width, classes), current.dtype),
            pltpu.VMEM((chosen,) + band_tiles.shape[1:], band_tiles.dtype),
            pltpu.SemaphoreType.DMA((3 + chosen,)),
        ],
    )(z, band_offsets.reshape(-1), current, *rim_sources, band_tiles)


def hub_kernel(n_hub, width, final, z_ref, hidx_ref, *rest):
    hub_hbm = rest[:n_hub]
    if final:
        (ht_hbm, band_hbm, rim_hbm, deg_hbm, seeds_hbm, out_ref, hub, ht, band, rim, deg, seeds, sem) = rest[n_hub:]
    else:
        (ht_hbm, band_hbm, rim_hbm, deg_hbm, seeds_hbm, pick_ref,
         cur_ref, owned_ref, p1_ref, p3_ref, pc_ref,
         hub, ht, band, rim, deg, seeds, sem) = rest[n_hub:]
    blocks, k_hub, rows = ht.shape[0], ht.shape[1], ht.shape[2]
    chosen = rim_blocks(blocks)
    rim_copy = pltpu.make_async_copy(rim_hbm, rim, sem.at[n_hub + 4 * blocks])
    rim_copy.start()
    per_block = []
    for b in range(blocks):
        span = pl.ds(b * rows, rows)
        per_block.append([
            pltpu.make_async_copy(ht_hbm.at[b], ht.at[b], sem.at[n_hub + 4 * b]),
            pltpu.make_async_copy(band_hbm.at[span], band.at[span], sem.at[n_hub + 4 * b + 1]),
            pltpu.make_async_copy(deg_hbm.at[span], deg.at[span], sem.at[n_hub + 4 * b + 2]),
            pltpu.make_async_copy(seeds_hbm.at[span], seeds.at[span], sem.at[n_hub + 4 * b + 3]),
        ])
    copies = []
    at = 0
    for i, piece in enumerate(hub_hbm):
        n = piece.shape[0]
        copies.append(pltpu.make_async_copy(piece, hub.at[pl.ds(at, n)], sem.at[i]))
        at += n
    for c in copies:
        c.start()
    for c in per_block[0]:
        c.start()
    for b in range(1, blocks):
        for c in per_block[b]:
            c.start()
    for c in copies:
        c.wait()
    rim_copy.wait()
    for b in range(blocks):
        for c in per_block[b]:
            c.wait()
        span = pl.ds(b * rows, rows)
        acc = jnp.zeros((rows, hub.shape[2]), jnp.float32)
        blk = lambda h: hub[hidx_ref[b * k_hub + h]]
        for h in range(0, k_hub - 1, 2):
            lhs = jnp.concatenate([ht[b, h], ht[b, h + 1]], axis=1)
            rhs = jnp.concatenate([blk(h), blk(h + 1)], axis=0)
            acc = acc + jnp.dot(lhs, rhs, preferred_element_type=jnp.float32)
        if k_hub % 2:
            acc = acc + jnp.dot(ht[b, k_hub - 1], blk(k_hub - 1), preferred_element_type=jnp.float32)
        near = band[span]
        if b in chosen:
            near = near + rim[pl.ds(chosen.index(b) * rows, rows), :]
        gathered = (near + acc) / deg[span]
        labels = spread_weight * gathered + (1.0 - spread_weight) * seeds[span].astype(jnp.float32)
        if final:
            out_ref[span, :] = labels
        else:
            cur_ref[span, :] = labels.astype(cur_ref.dtype)
    if final:
        return
    own = cur_ref.shape[0]
    n_own = owned_ref.shape[0]
    owned = jnp.dot(pick_ref[...], cur_ref[...], preferred_element_type=jnp.float32).astype(owned_ref.dtype)
    owned_ref[...] = owned
    p1_ref[pl.ds(0, n_own), :] = owned
    p3_ref[pl.ds(0, n_own), :] = owned
    z = z_ref[0]
    top = cur_ref[pl.ds(own - width, width), :]
    bottom = cur_ref[pl.ds(0, width), :]
    p1_ref[pl.ds(n_own, width), :] = jnp.where(z % 2 == 0, top, bottom)
    p3_ref[pl.ds(n_own, width), :] = jnp.where(z == 1, top, bottom)
    pc_ref[...] = jnp.where(z == 3, top, bottom)


def hub_call(z, hub_index, pick, hub_pieces, hub_tiles, band, degree, seeds, width, final):
    blocks, k_hub, rows, _ = hub_tiles.shape
    classes = seeds.shape[1]
    n_hub = len(hub_pieces)
    n_hub_blocks = sum(p.shape[0] for p in hub_pieces)
    n_own = pick.shape[0]
    bf = jnp.bfloat16
    flops = 2 * blocks * k_hub * rows * rows * classes
    bytes_accessed = hub_tiles.size * 2 + n_hub_blocks * rows * classes * 2 + seeds.size * 4 * 4
    if final:
        outs = [jax.ShapeDtypeStruct(seeds.shape, jnp.float32)]
    else:
        outs = [
            jax.ShapeDtypeStruct(seeds.shape, bf),
            jax.ShapeDtypeStruct((n_own, classes), bf),
            jax.ShapeDtypeStruct((n_own + width, classes), bf),
            jax.ShapeDtypeStruct((n_own + width, classes), bf),
            jax.ShapeDtypeStruct((width, classes), bf),
        ]
    return pl.pallas_call(
        functools.partial(hub_kernel, n_hub, width, final),
        cost_estimate=pl.CostEstimate(flops=flops, transcendentals=0, bytes_accessed=bytes_accessed),
        in_specs=[SMEM, SMEM] + [ANY] * (n_hub + 5) + ([] if final else [VMEM]),
        out_specs=[VMEM] * len(outs),
        out_shape=outs,
        scratch_shapes=[
            pltpu.VMEM((n_hub_blocks, rows, classes), bf),
            pltpu.VMEM(hub_tiles.shape, hub_tiles.dtype),
            pltpu.VMEM(seeds.shape, jnp.float32),
            pltpu.VMEM(band[1].shape, jnp.float32),
            pltpu.VMEM(degree.shape, jnp.float32),
            pltpu.VMEM(seeds.shape, seeds.dtype),
            pltpu.SemaphoreType.DMA((n_hub + 4 * blocks + 1,)),
        ],
    )(z, hub_index, *hub_pieces, hub_tiles, *band, degree, seeds, *([] if final else [pick]))


def positions_of(hub_blocks, owned, block_rows):
    count = lax.axis_size(AXES)
    if not fast_path(owned, block_rows):
        return hub_blocks
    offs = [0]
    for group in ROUNDS_32:
        offs = offs + [o ^ m for m in group for o in offs]
    where = np.zeros(count, np.int32)
    for p, o in enumerate(offs):
        where[o] = p
    return jnp.asarray(where)[hub_blocks ^ lax.axis_index(AXES)]


def body(seed_scores, seed_mask, band_offsets, band_tiles, hub_blocks, hub_tiles, hub_rows):
    block_rows = band_tiles.shape[2]
    seeds16 = seed_mask.astype(seed_scores.dtype)[:, None] * seed_scores
    degree = jnp.sum(band_tiles, axis=(1, 3), dtype=jnp.float32) + jnp.sum(
        hub_tiles, axis=(1, 3), dtype=jnp.float32
    )
    degree = jnp.broadcast_to(degree.reshape(-1, 1), seeds16.shape)
    width = BW * block_rows
    z = lax.axis_index("hub").astype(jnp.int32).reshape(1)
    current = seeds16
    owned = current.at[hub_rows].get(mode="promise_in_bounds")
    p1, p3, pc = payloads(current, owned, z[0], width)
    fast = fast_path(owned, block_rows)
    pick = (hub_rows[:, None] == jnp.arange(current.shape[0], dtype=hub_rows.dtype)[None, :]).astype(jnp.bfloat16)
    prep = (pick, degree, positions_of(hub_blocks, owned, block_rows).reshape(-1))
    for step in range(ITERS):
        part = functools.partial(
            band_call, z, band_offsets, current, band_tiles=band_tiles, fast=fast, n_own=owned.shape[0], width=width
        )
        band, hub_pieces, prep_out = exchange(
            current, owned, p1, p3, pc, hub_blocks, width, block_rows,
            lambda: part((), rims_part=False), lambda rims: part(rims, rims_part=True), prep,
        )
        if prep is not None:
            pick, degree, hub_index = prep_out
            prep = None
        final = step + 1 == ITERS
        outs = hub_call(z, hub_index, pick, hub_pieces, hub_tiles, band, degree, seeds16, width, final)
        if final:
            labels = outs[0]
        else:
            current, owned, p1, p3, pc = outs
    return labels


def solution(mesh):
    placed = (
        P(AXES, None),
        P(AXES),
        P(AXES, None),
        P(AXES, None, None, None),
        P(AXES, None),
        P(AXES, None, None, None),
        P(AXES),
    )
    return jax.shard_map(
        body, mesh=mesh, in_specs=placed, out_specs=P(AXES, None), check_vma=False
    )
```

```python
import functools

import jax
import jax.numpy as jnp
import numpy as np
from jax import lax
from jax.experimental import pallas as pl
from jax.experimental.pallas import tpu as pltpu
from jax.sharding import PartitionSpec as P

BW = 2
ITERS = 3
AXES = ("node", "hub")
ROUNDS_32 = ((1, 2, 3), (8, 16, 24), (4,))


spread_weight = 0.8

SMEM = pl.BlockSpec(memory_space=pltpu.SMEM)
ANY = pl.BlockSpec(memory_space=pl.ANY)
VMEM = pl.BlockSpec(memory_space=pltpu.VMEM)


def fast_path(owned, block_rows):
    count = lax.axis_size(AXES)
    return count == 32 and owned.shape[0] == block_rows and lax.axis_size("hub") == 4


def payloads(current, owned, z, width):
    top = current[current.shape[0] - width:]
    bottom = current[:width]
    p1 = jnp.concatenate([owned, jnp.where(z % 2 == 0, top, bottom)], 0)
    p3 = jnp.concatenate([owned, jnp.where(z == 1, top, bottom)], 0)
    pc = jnp.where(z == 3, top, bottom)
    return p1, p3, pc


def exchange(current, owned, p1, p3, pc, hub_blocks, width, block_rows, middle, prep):
    count = lax.axis_size(AXES)
    if not fast_path(owned, block_rows):
        forward = [(i, i + 1) for i in range(count - 1)]
        backward = [(target, source) for source, target in forward]
        low = lax.ppermute(current[current.shape[0] - width:], AXES, forward)
        high = lax.ppermute(current[:width], AXES, backward)
        hub_all = lax.all_gather(owned, AXES, axis=0, tiled=True)
        return middle((low, high)), [hub_all.reshape(-1, block_rows, owned.shape[1])], prep
    me = lax.axis_index(AXES)
    pairs = lambda m: [(i, i ^ m) for i in range(count)]
    r3 = lax.ppermute(p3, AXES, pairs(3))
    r2 = lax.ppermute(owned, AXES, pairs(2))
    r1 = lax.ppermute(p1, AXES, pairs(1))
    groups = count // 4
    cross = [(4 * g + 3, 4 * g + 4) for g in range(groups - 1)]
    cross += [(4 * g + 4, 4 * g + 3) for g in range(groups - 1)]
    rc = lax.ppermute(pc, AXES, cross)
    if prep is not None:
        (r1, r2, r3, rc), prep = lax.optimization_barrier(((r1, r2, r3, rc), prep))
    rows = block_rows
    buf = jnp.concatenate([owned[None], r1[None, :rows], r2[None], r3[None, :rows]], 0)
    offs = [0, 1, 2, 3]
    rounds = ROUNDS_32
    pieces = [buf]
    done = None
    for r, group in enumerate(rounds[1:]):
        sent = {m: lax.ppermute(buf, AXES, pairs(m)) for m in sorted(group, key=lambda m: -m)}
        recvs = [sent[m] for m in group]
        if done is None:
            done, recvs = lax.optimization_barrier((middle((r1, r3, rc)), recvs))
        offs = offs + [o ^ m for m in group for o in offs]
        pieces = [buf] + recvs
        if r + 2 < len(rounds):
            buf = jnp.concatenate(pieces, 0)
    assert sorted(offs) == list(range(count))
    where = np.zeros(count, np.int32)
    for p, o in enumerate(offs):
        where[o] = p
    return done, pieces, prep


def band_kernel(fast, n_own, z_ref, off_ref, cur_hbm, *rest):
    if fast:
        r1_hbm, r3_hbm, rc_hbm, bt_hbm, out_ref, ext, bt, sem = rest
    else:
        low_hbm, high_hbm, bt_hbm, out_ref, ext, bt, sem = rest
    blocks, k_band, rows = bt.shape[0], bt.shape[1], bt.shape[2]
    own = cur_hbm.shape[0]
    width = (ext.shape[0] - own) // 2
    low_dst = ext.at[pl.ds(0, width)]
    high_dst = ext.at[pl.ds(width + own, width)]
    mid = pltpu.make_async_copy(cur_hbm, ext.at[pl.ds(width, own)], sem.at[1])
    band_copies = [pltpu.make_async_copy(bt_hbm.at[b], bt.at[b], sem.at[3 + b]) for b in range(blocks)]
    band_copies[0].start()
    mid.start()
    if fast:
        z = z_ref[0]
        low_r1 = pltpu.make_async_copy(r1_hbm.at[pl.ds(n_own, width)], low_dst, sem.at[0])
        low_r3 = pltpu.make_async_copy(r3_hbm.at[pl.ds(n_own, width)], low_dst, sem.at[0])
        low_rc = pltpu.make_async_copy(rc_hbm, low_dst, sem.at[0])
        high_r1 = pltpu.make_async_copy(r1_hbm.at[pl.ds(n_own, width)], high_dst, sem.at[2])
        high_r3 = pltpu.make_async_copy(r3_hbm.at[pl.ds(n_own, width)], high_dst, sem.at[2])
        high_rc = pltpu.make_async_copy(rc_hbm, high_dst, sem.at[2])

        @pl.when(z == 0)
        def _():
            low_rc.start()
            high_r1.start()

        @pl.when(z == 1)
        def _():
            low_r1.start()
            high_r3.start()

        @pl.when(z == 2)
        def _():
            low_r3.start()
            high_r1.start()

        @pl.when(z == 3)
        def _():
            low_r1.start()
            high_rc.start()

        low_wait, high_wait = low_rc, high_rc
    else:
        low_wait = pltpu.make_async_copy(low_hbm, low_dst, sem.at[0])
        high_wait = pltpu.make_async_copy(high_hbm, high_dst, sem.at[2])
        low_wait.start()
        high_wait.start()
    for b in range(1, blocks):
        band_copies[b].start()
    mid.wait()
    low_wait.wait()
    high_wait.wait()
    for b in range(blocks):
        band_copies[b].wait()
        acc = jnp.zeros((rows, out_ref.shape[1]), jnp.float32)

        def near(k):
            n = b + BW + off_ref[b * k_band + k]
            return ext[pl.ds(pl.multiple_of(n * rows, rows), rows), :]

        for k in range(0, k_band - 1, 2):
            lhs = jnp.concatenate([bt[b, k], bt[b, k + 1]], axis=1)
            rhs = jnp.concatenate([near(k), near(k + 1)], axis=0)
            acc = acc + jnp.dot(lhs, rhs, preferred_element_type=jnp.float32)
        if k_band % 2:
            acc = acc + jnp.dot(bt[b, k_band - 1], near(k_band - 1), preferred_element_type=jnp.float32)
        out_ref[pl.ds(b * rows, rows), :] = acc


def band_call(z, band_offsets, current, rim_sources, band_tiles, fast, n_own, width):
    blocks, k_band, rows, _ = band_tiles.shape
    classes = current.shape[1]
    flops = 2 * blocks * k_band * rows * rows * classes
    bytes_accessed = band_tiles.size * 2 + current.size * 2 * 2 + current.size * 4
    return pl.pallas_call(
        functools.partial(band_kernel, fast, n_own),
        cost_estimate=pl.CostEstimate(flops=flops, transcendentals=0, bytes_accessed=bytes_accessed),
        in_specs=[SMEM, SMEM] + [ANY] * (1 + len(rim_sources) + 1),
        out_specs=VMEM,
        out_shape=jax.ShapeDtypeStruct(current.shape, jnp.float32),
        scratch_shapes=[
            pltpu.VMEM((current.shape[0] + 2 * width, classes), current.dtype),
            pltpu.VMEM(band_tiles.shape, band_tiles.dtype),
            pltpu.SemaphoreType.DMA((3 + blocks,)),
        ],
    )(z, band_offsets.reshape(-1), current, *rim_sources, band_tiles)


def hub_kernel(n_hub, width, final, z_ref, hidx_ref, *rest):
    hub_hbm = rest[:n_hub]
    if final:
        (ht_hbm, band_hbm, deg_hbm, seeds_hbm, out_ref, ht, band, deg, seeds, sem) = rest[n_hub:]
    else:
        (ht_hbm, band_hbm, deg_hbm, seeds_hbm, pick_ref,
         cur_ref, owned_ref, p1_ref, p3_ref, pc_ref,
         ht, band, deg, seeds, sem) = rest[n_hub:]
    blocks, k_hub, rows = ht.shape[0], ht.shape[1], ht.shape[2]
    per_block = []
    for b in range(blocks):
        span = pl.ds(b * rows, rows)
        per_block.append([
            pltpu.make_async_copy(ht_hbm.at[b], ht.at[b], sem.at[n_hub + 4 * b]),
            pltpu.make_async_copy(band_hbm.at[span], band.at[span], sem.at[n_hub + 4 * b + 1]),
            pltpu.make_async_copy(deg_hbm.at[span], deg.at[span], sem.at[n_hub + 4 * b + 2]),
            pltpu.make_async_copy(seeds_hbm.at[span], seeds.at[span], sem.at[n_hub + 4 * b + 3]),
        ])
    copies = []
    for c in per_block[0]:
        c.start()
    for b in range(1, blocks):
        for c in per_block[b]:
            c.start()
    for c in copies:
        c.wait()
    for b in range(blocks):
        for c in per_block[b]:
            c.wait()
        span = pl.ds(b * rows, rows)
        acc = jnp.zeros((rows, rows), jnp.float32)

        def blk(h):
            p = hidx_ref[b * k_hub + h]
            first = hub_hbm[0].shape[0]
            if n_hub == 1:
                return hub_hbm[0][p]
            mine = hub_hbm[0][jnp.minimum(p, first - 1)]
            theirs = hub_hbm[1][jnp.maximum(p - first, 0)]
            return jnp.where(p < first, mine, theirs)

        for h in range(0, k_hub - 1, 2):
            lhs = jnp.concatenate([ht[b, h], ht[b, h + 1]], axis=1)
            rhs = jnp.concatenate([blk(h), blk(h + 1)], axis=0)
            acc = acc + jnp.dot(lhs, rhs, preferred_element_type=jnp.float32)
        if k_hub % 2:
            acc = acc + jnp.dot(ht[b, k_hub - 1], blk(k_hub - 1), preferred_element_type=jnp.float32)
        gathered = (band[span] + acc) / deg[span]
        labels = spread_weight * gathered + (1.0 - spread_weight) * seeds[span].astype(jnp.float32)
        if final:
            out_ref[span, :] = labels
        else:
            cur_ref[span, :] = labels.astype(cur_ref.dtype)
    if final:
        return
    own = cur_ref.shape[0]
    n_own = owned_ref.shape[0]
    owned = jnp.dot(pick_ref[...], cur_ref[...], preferred_element_type=jnp.float32).astype(owned_ref.dtype)
    owned_ref[...] = owned
    p1_ref[pl.ds(0, n_own), :] = owned
    p3_ref[pl.ds(0, n_own), :] = owned
    z = z_ref[0]
    top = cur_ref[pl.ds(own - width, width), :]
    bottom = cur_ref[pl.ds(0, width), :]
    p1_ref[pl.ds(n_own, width), :] = jnp.where(z % 2 == 0, top, bottom)
    p3_ref[pl.ds(n_own, width), :] = jnp.where(z == 1, top, bottom)
    pc_ref[...] = jnp.where(z == 3, top, bottom)


def hub_call(z, hub_index, pick, hub_pieces, hub_tiles, band, degree, seeds, width, final):
    blocks, k_hub, rows, _ = hub_tiles.shape
    classes = seeds.shape[1]
    n_hub = len(hub_pieces)
    n_hub_blocks = sum(p.shape[0] for p in hub_pieces)
    n_own = pick.shape[0]
    bf = jnp.bfloat16
    flops = 2 * blocks * k_hub * rows * rows * classes
    bytes_accessed = hub_tiles.size * 2 + n_hub_blocks * rows * classes * 2 + seeds.size * 4 * 4
    if final:
        outs = [jax.ShapeDtypeStruct(seeds.shape, jnp.float32)]
    else:
        outs = [
            jax.ShapeDtypeStruct(seeds.shape, bf),
            jax.ShapeDtypeStruct((n_own, classes), bf),
            jax.ShapeDtypeStruct((n_own + width, classes), bf),
            jax.ShapeDtypeStruct((n_own + width, classes), bf),
            jax.ShapeDtypeStruct((width, classes), bf),
        ]
    return pl.pallas_call(
        functools.partial(hub_kernel, n_hub, width, final),
        cost_estimate=pl.CostEstimate(flops=flops, transcendentals=0, bytes_accessed=bytes_accessed),
        in_specs=[SMEM, SMEM] + [VMEM] * n_hub + [ANY] * 4 + ([] if final else [VMEM]),
        out_specs=[VMEM] * len(outs),
        out_shape=outs,
        scratch_shapes=[
            pltpu.VMEM(hub_tiles.shape, hub_tiles.dtype),
            pltpu.VMEM(seeds.shape, jnp.float32),
            pltpu.VMEM(degree.shape, jnp.float32),
            pltpu.VMEM(seeds.shape, seeds.dtype),
            pltpu.SemaphoreType.DMA((n_hub + 4 * blocks,)),
        ],
    )(z, hub_index, *hub_pieces, hub_tiles, band, degree, seeds, *([] if final else [pick]))


def positions_of(hub_blocks, owned, block_rows):
    count = lax.axis_size(AXES)
    if not fast_path(owned, block_rows):
        return hub_blocks
    offs = [0]
    for group in ROUNDS_32:
        offs = offs + [o ^ m for m in group for o in offs]
    where = np.zeros(count, np.int32)
    for p, o in enumerate(offs):
        where[o] = p
    return jnp.asarray(where)[hub_blocks ^ lax.axis_index(AXES)]


def body(seed_scores, seed_mask, band_offsets, band_tiles, hub_blocks, hub_tiles, hub_rows):
    block_rows = band_tiles.shape[2]
    seeds = seed_mask.astype(jnp.float32)[:, None] * seed_scores.astype(jnp.float32)
    degree = jnp.sum(band_tiles, axis=(1, 3), dtype=jnp.float32) + jnp.sum(
        hub_tiles, axis=(1, 3), dtype=jnp.float32
    )
    degree = jnp.broadcast_to(degree.reshape(-1, 1), seeds.shape)
    width = BW * block_rows
    z = lax.axis_index("hub").astype(jnp.int32).reshape(1)
    current = seeds.astype(jnp.bfloat16)
    seeds16 = current
    owned = current[hub_rows]
    p1, p3, pc = payloads(current, owned, z[0], width)
    fast = fast_path(owned, block_rows)
    pick = (hub_rows[:, None] == jnp.arange(current.shape[0], dtype=hub_rows.dtype)[None, :]).astype(jnp.bfloat16)
    prep = (pick, degree, positions_of(hub_blocks, owned, block_rows).reshape(-1))
    for step in range(ITERS):
        middle = functools.partial(
            band_call, z, band_offsets, current, band_tiles=band_tiles, fast=fast, n_own=owned.shape[0], width=width
        )
        band, hub_pieces, prep_out = exchange(
            current, owned, p1, p3, pc, hub_blocks, width, block_rows, lambda rims: middle(rims), prep
        )
        if prep is not None:
            pick, degree, hub_index = prep_out
            prep = None
        final = step + 1 == ITERS
        outs = hub_call(z, hub_index, pick, hub_pieces, hub_tiles, band, degree, seeds16, width, final)
        if final:
            labels = outs[0]
        else:
            current, owned, p1, p3, pc = outs
    return labels


def solution(mesh):
    placed = (
        P(AXES, None),
        P(AXES),
        P(AXES, None),
        P(AXES, None, None, None),
        P(AXES, None),
        P(AXES, None, None, None),
        P(AXES),
    )
    return jax.shard_map(
        body, mesh=mesh, in_specs=placed, out_specs=P(AXES, None), check_vma=False
    )
```

```python
import functools

import jax
import jax.numpy as jnp
import numpy as np
from jax import lax
from jax.experimental import pallas as pl
from jax.experimental.pallas import tpu as pltpu
from jax.sharding import PartitionSpec as P

BW = 2
ITERS = 3
AXES = ("node", "hub")
ROUNDS_32 = ((1, 2, 3), (8, 16, 24), (4,))


spread_weight = 0.8

SMEM = pl.BlockSpec(memory_space=pltpu.SMEM)
ANY = pl.BlockSpec(memory_space=pl.ANY)
VMEM = pl.BlockSpec(memory_space=pltpu.VMEM)


def fast_path(owned, block_rows):
    count = lax.axis_size(AXES)
    return count == 32 and owned.shape[0] == block_rows and lax.axis_size("hub") == 4


def payloads(current, owned, z, width):
    top = current[current.shape[0] - width:]
    bottom = current[:width]
    p1 = jnp.concatenate([owned, jnp.where(z % 2 == 0, top, bottom)], 0)
    p3 = jnp.concatenate([owned, jnp.where(z == 1, top, bottom)], 0)
    pc = jnp.where(z == 3, top, bottom)
    return p1, p3, pc


def exchange(current, owned, p1, p3, pc, hub_blocks, width, block_rows, middle, prep):
    count = lax.axis_size(AXES)
    if not fast_path(owned, block_rows):
        forward = [(i, i + 1) for i in range(count - 1)]
        backward = [(target, source) for source, target in forward]
        low = lax.ppermute(current[current.shape[0] - width:], AXES, forward)
        high = lax.ppermute(current[:width], AXES, backward)
        hub_all = lax.all_gather(owned, AXES, axis=0, tiled=True)
        return middle((low, high)), [hub_all.reshape(-1, block_rows, owned.shape[1])], prep
    me = lax.axis_index(AXES)
    pairs = lambda m: [(i, i ^ m) for i in range(count)]
    r3 = lax.ppermute(p3, AXES, pairs(3))
    r2 = lax.ppermute(owned, AXES, pairs(2))
    r1 = lax.ppermute(p1, AXES, pairs(1))
    groups = count // 4
    cross = [(4 * g + 3, 4 * g + 4) for g in range(groups - 1)]
    cross += [(4 * g + 4, 4 * g + 3) for g in range(groups - 1)]
    rc = lax.ppermute(pc, AXES, cross)
    if prep is not None:
        (r1, r2, r3, rc), prep = lax.optimization_barrier(((r1, r2, r3, rc), prep))
    rows = block_rows
    buf = jnp.concatenate([owned[None], r1[None, :rows], r2[None], r3[None, :rows]], 0)
    offs = [0, 1, 2, 3]
    rounds = ROUNDS_32
    assert len(rounds) == 3 and len(rounds[2]) == 1
    last = rounds[2][0]
    early = lax.ppermute(buf, AXES, pairs(last))
    group = rounds[1]
    sent = {m: lax.ppermute(buf, AXES, pairs(m)) for m in sorted(group, key=lambda m: -m)}
    recvs = [sent[m] for m in group]
    done, recvs = lax.optimization_barrier((middle((r1, r3, rc)), recvs))
    more = [o ^ m for m in group for o in offs]
    rest = jnp.concatenate(recvs, 0)
    pieces = [buf, rest, early, lax.ppermute(rest, AXES, pairs(last))]
    offs = offs + more + [o ^ last for o in offs] + [o ^ last for o in more]
    assert sorted(offs) == list(range(count))
    return done, pieces, prep


def band_kernel(fast, n_own, z_ref, off_ref, cur_hbm, *rest):
    if fast:
        r1_hbm, r3_hbm, rc_hbm, bt_hbm, out_ref, ext, bt, sem = rest
    else:
        low_hbm, high_hbm, bt_hbm, out_ref, ext, bt, sem = rest
    blocks, k_band, rows = bt.shape[0], bt.shape[1], bt.shape[2]
    own = cur_hbm.shape[0]
    width = (ext.shape[0] - own) // 2
    low_dst = ext.at[pl.ds(0, width)]
    high_dst = ext.at[pl.ds(width + own, width)]
    mid = pltpu.make_async_copy(cur_hbm, ext.at[pl.ds(width, own)], sem.at[1])
    band_copies = [pltpu.make_async_copy(bt_hbm.at[b], bt.at[b], sem.at[3 + b]) for b in range(blocks)]
    band_copies[0].start()
    mid.start()
    if fast:
        z = z_ref[0]
        low_r1 = pltpu.make_async_copy(r1_hbm.at[pl.ds(n_own, width)], low_dst, sem.at[0])
        low_r3 = pltpu.make_async_copy(r3_hbm.at[pl.ds(n_own, width)], low_dst, sem.at[0])
        low_rc = pltpu.make_async_copy(rc_hbm, low_dst, sem.at[0])
        high_r1 = pltpu.make_async_copy(r1_hbm.at[pl.ds(n_own, width)], high_dst, sem.at[2])
        high_r3 = pltpu.make_async_copy(r3_hbm.at[pl.ds(n_own, width)], high_dst, sem.at[2])
        high_rc = pltpu.make_async_copy(rc_hbm, high_dst, sem.at[2])

        @pl.when(z == 0)
        def _():
            low_rc.start()
            high_r1.start()

        @pl.when(z == 1)
        def _():
            low_r1.start()
            high_r3.start()

        @pl.when(z == 2)
        def _():
            low_r3.start()
            high_r1.start()

        @pl.when(z == 3)
        def _():
            low_r1.start()
            high_rc.start()

        low_wait, high_wait = low_rc, high_rc
    else:
        low_wait = pltpu.make_async_copy(low_hbm, low_dst, sem.at[0])
        high_wait = pltpu.make_async_copy(high_hbm, high_dst, sem.at[2])
        low_wait.start()
        high_wait.start()
    for b in range(1, blocks):
        band_copies[b].start()
    mid.wait()
    low_wait.wait()
    high_wait.wait()
    for b in range(blocks):
        band_copies[b].wait()
        acc = jnp.zeros((rows, out_ref.shape[1]), jnp.float32)

        def near(k):
            n = b + BW + off_ref[b * k_band + k]
            return ext[pl.ds(pl.multiple_of(n * rows, rows), rows), :]

        for k in range(0, k_band - 1, 2):
            lhs = jnp.concatenate([bt[b, k], bt[b, k + 1]], axis=1)
            rhs = jnp.concatenate([near(k), near(k + 1)], axis=0)
            acc = acc + jnp.dot(lhs, rhs, preferred_element_type=jnp.float32)
        if k_band % 2:
            acc = acc + jnp.dot(bt[b, k_band - 1], near(k_band - 1), preferred_element_type=jnp.float32)
        out_ref[pl.ds(b * rows, rows), :] = acc


def band_call(z, band_offsets, current, rim_sources, band_tiles, fast, n_own, width):
    blocks, k_band, rows, _ = band_tiles.shape
    classes = current.shape[1]
    flops = 2 * blocks * k_band * rows * rows * classes
    bytes_accessed = band_tiles.size * 2 + current.size * 2 * 2 + current.size * 4
    return pl.pallas_call(
        functools.partial(band_kernel, fast, n_own),
        cost_estimate=pl.CostEstimate(flops=flops, transcendentals=0, bytes_accessed=bytes_accessed),
        in_specs=[SMEM, SMEM] + [ANY] * (1 + len(rim_sources) + 1),
        out_specs=VMEM,
        out_shape=jax.ShapeDtypeStruct(current.shape, jnp.float32),
        scratch_shapes=[
            pltpu.VMEM((current.shape[0] + 2 * width, classes), current.dtype),
            pltpu.VMEM(band_tiles.shape, band_tiles.dtype),
            pltpu.SemaphoreType.DMA((3 + blocks,)),
        ],
    )(z, band_offsets.reshape(-1), current, *rim_sources, band_tiles)


def hub_kernel(n_hub, width, final, z_ref, hidx_ref, *rest):
    hub_hbm = rest[:n_hub]
    if final:
        (ht_hbm, band_hbm, deg_hbm, seeds_hbm, out_ref, hub, ht, band, deg, seeds, sem) = rest[n_hub:]
    else:
        (ht_hbm, band_hbm, deg_hbm, seeds_hbm, pick_ref,
         cur_ref, owned_ref, p1_ref, p3_ref, pc_ref,
         hub, ht, band, deg, seeds, sem) = rest[n_hub:]
    blocks, k_hub, rows = ht.shape[0], ht.shape[1], ht.shape[2]
    per_block = []
    for b in range(blocks):
        span = pl.ds(b * rows, rows)
        per_block.append([
            pltpu.make_async_copy(ht_hbm.at[b], ht.at[b], sem.at[n_hub + 4 * b]),
            pltpu.make_async_copy(band_hbm.at[span], band.at[span], sem.at[n_hub + 4 * b + 1]),
            pltpu.make_async_copy(deg_hbm.at[span], deg.at[span], sem.at[n_hub + 4 * b + 2]),
            pltpu.make_async_copy(seeds_hbm.at[span], seeds.at[span], sem.at[n_hub + 4 * b + 3]),
        ])
    copies = []
    at = 0
    for i, piece in enumerate(hub_hbm):
        n = piece.shape[0]
        copies.append(pltpu.make_async_copy(piece, hub.at[pl.ds(at, n)], sem.at[i]))
        at += n
    for c in copies:
        c.start()
    for c in per_block[0]:
        c.start()
    for b in range(1, blocks):
        for c in per_block[b]:
            c.start()
    for c in copies:
        c.wait()
    for b in range(blocks):
        for c in per_block[b]:
            c.wait()
        span = pl.ds(b * rows, rows)
        acc = jnp.zeros((rows, hub.shape[2]), jnp.float32)
        blk = lambda h: hub[hidx_ref[b * k_hub + h]]
        for h in range(0, k_hub - 1, 2):
            lhs = jnp.concatenate([ht[b, h], ht[b, h + 1]], axis=1)
            rhs = jnp.concatenate([blk(h), blk(h + 1)], axis=0)
            acc = acc + jnp.dot(lhs, rhs, preferred_element_type=jnp.float32)
        if k_hub % 2:
            acc = acc + jnp.dot(ht[b, k_hub - 1], blk(k_hub - 1), preferred_element_type=jnp.float32)
        gathered = (band[span] + acc) / deg[span]
        labels = spread_weight * gathered + (1.0 - spread_weight) * seeds[span].astype(jnp.float32)
        if final:
            out_ref[span, :] = labels
        else:
            cur_ref[span, :] = labels.astype(cur_ref.dtype)
    if final:
        return
    own = cur_ref.shape[0]
    n_own = owned_ref.shape[0]
    owned = jnp.dot(pick_ref[...], cur_ref[...], preferred_element_type=jnp.float32).astype(owned_ref.dtype)
    owned_ref[...] = owned
    p1_ref[pl.ds(0, n_own), :] = owned
    p3_ref[pl.ds(0, n_own), :] = owned
    z = z_ref[0]
    top = cur_ref[pl.ds(own - width, width), :]
    bottom = cur_ref[pl.ds(0, width), :]
    p1_ref[pl.ds(n_own, width), :] = jnp.where(z % 2 == 0, top, bottom)
    p3_ref[pl.ds(n_own, width), :] = jnp.where(z == 1, top, bottom)
    pc_ref[...] = jnp.where(z == 3, top, bottom)


def hub_call(z, hub_index, pick, hub_pieces, hub_tiles, band, degree, seeds, width, final):
    blocks, k_hub, rows, _ = hub_tiles.shape
    classes = seeds.shape[1]
    n_hub = len(hub_pieces)
    n_hub_blocks = sum(p.shape[0] for p in hub_pieces)
    n_own = pick.shape[0]
    bf = jnp.bfloat16
    flops = 2 * blocks * k_hub * rows * rows * classes
    bytes_accessed = hub_tiles.size * 2 + n_hub_blocks * rows * classes * 2 + seeds.size * 4 * 4
    if final:
        outs = [jax.ShapeDtypeStruct(seeds.shape, jnp.float32)]
    else:
        outs = [
            jax.ShapeDtypeStruct(seeds.shape, bf),
            jax.ShapeDtypeStruct((n_own, classes), bf),
            jax.ShapeDtypeStruct((n_own + width, classes), bf),
            jax.ShapeDtypeStruct((n_own + width, classes), bf),
            jax.ShapeDtypeStruct((width, classes), bf),
        ]
    return pl.pallas_call(
        functools.partial(hub_kernel, n_hub, width, final),
        cost_estimate=pl.CostEstimate(flops=flops, transcendentals=0, bytes_accessed=bytes_accessed),
        in_specs=[SMEM, SMEM] + [ANY] * (n_hub + 4) + ([] if final else [VMEM]),
        out_specs=[VMEM] * len(outs),
        out_shape=outs,
        scratch_shapes=[
            pltpu.VMEM((n_hub_blocks, rows, classes), bf),
            pltpu.VMEM(hub_tiles.shape, hub_tiles.dtype),
            pltpu.VMEM(seeds.shape, jnp.float32),
            pltpu.VMEM(degree.shape, jnp.float32),
            pltpu.VMEM(seeds.shape, seeds.dtype),
            pltpu.SemaphoreType.DMA((n_hub + 4 * blocks,)),
        ],
    )(z, hub_index, *hub_pieces, hub_tiles, band, degree, seeds, *([] if final else [pick]))


def positions_of(hub_blocks, owned, block_rows):
    count = lax.axis_size(AXES)
    if not fast_path(owned, block_rows):
        return hub_blocks
    offs = [0]
    for group in ROUNDS_32:
        offs = offs + [o ^ m for m in group for o in offs]
    where = np.zeros(count, np.int32)
    for p, o in enumerate(offs):
        where[o] = p
    return jnp.asarray(where)[hub_blocks ^ lax.axis_index(AXES)]


def body(seed_scores, seed_mask, band_offsets, band_tiles, hub_blocks, hub_tiles, hub_rows):
    block_rows = band_tiles.shape[2]
    seeds = seed_mask.astype(jnp.float32)[:, None] * seed_scores.astype(jnp.float32)
    degree = jnp.sum(band_tiles, axis=(1, 3), dtype=jnp.float32) + jnp.sum(
        hub_tiles, axis=(1, 3), dtype=jnp.float32
    )
    degree = jnp.broadcast_to(degree.reshape(-1, 1), seeds.shape)
    width = BW * block_rows
    z = lax.axis_index("hub").astype(jnp.int32).reshape(1)
    current = seeds.astype(jnp.bfloat16)
    seeds16 = current
    owned = current[hub_rows]
    p1, p3, pc = payloads(current, owned, z[0], width)
    fast = fast_path(owned, block_rows)
    pick = (hub_rows[:, None] == jnp.arange(current.shape[0], dtype=hub_rows.dtype)[None, :]).astype(jnp.bfloat16)
    prep = (pick, degree, positions_of(hub_blocks, owned, block_rows).reshape(-1))
    for step in range(ITERS):
        middle = functools.partial(
            band_call, z, band_offsets, current, band_tiles=band_tiles, fast=fast, n_own=owned.shape[0], width=width
        )
        band, hub_pieces, prep_out = exchange(
            current, owned, p1, p3, pc, hub_blocks, width, block_rows, lambda rims: middle(rims), prep
        )
        if prep is not None:
            pick, degree, hub_index = prep_out
            prep = None
        final = step + 1 == ITERS
        outs = hub_call(z, hub_index, pick, hub_pieces, hub_tiles, band, degree, seeds16, width, final)
        if final:
            labels = outs[0]
        else:
            current, owned, p1, p3, pc = outs
    return labels


def solution(mesh):
    placed = (
        P(AXES, None),
        P(AXES),
        P(AXES, None),
        P(AXES, None, None, None),
        P(AXES, None),
        P(AXES, None, None, None),
        P(AXES),
    )
    return jax.shard_map(
        body, mesh=mesh, in_specs=placed, out_specs=P(AXES, None), check_vma=False
    )
```

```python
import functools

import jax
import jax.numpy as jnp
import numpy as np
from jax import lax
from jax.experimental import pallas as pl
from jax.experimental.pallas import tpu as pltpu
from jax.sharding import PartitionSpec as P

BW = 2
ITERS = 3
AXES = ("node", "hub")
ROUNDS_32 = ((1, 2, 3), (8, 16, 24), (4,))


spread_weight = 0.8

SMEM = pl.BlockSpec(memory_space=pltpu.SMEM)
ANY = pl.BlockSpec(memory_space=pl.ANY)
VMEM = pl.BlockSpec(memory_space=pltpu.VMEM)


def fast_path(owned, block_rows):
    count = lax.axis_size(AXES)
    return count == 32 and owned.shape[0] == block_rows and lax.axis_size("hub") == 4


def payloads(current, owned, z, width):
    top = current[current.shape[0] - width:]
    bottom = current[:width]
    p1 = jnp.concatenate([owned, jnp.where(z % 2 == 0, top, bottom)], 0)
    p3 = jnp.concatenate([owned, jnp.where(z == 1, top, bottom)], 0)
    pc = jnp.where(z == 3, top, bottom)
    return p1, p3, pc


def exchange(current, owned, p1, p3, pc, hub_blocks, width, block_rows, middle, prep):
    count = lax.axis_size(AXES)
    if not fast_path(owned, block_rows):
        forward = [(i, i + 1) for i in range(count - 1)]
        backward = [(target, source) for source, target in forward]
        low = lax.ppermute(current[current.shape[0] - width:], AXES, forward)
        high = lax.ppermute(current[:width], AXES, backward)
        hub_all = lax.all_gather(owned, AXES, axis=0, tiled=True)
        return middle((low, high)), [hub_all.reshape(-1, block_rows, owned.shape[1])], prep
    me = lax.axis_index(AXES)
    pairs = lambda m: [(i, i ^ m) for i in range(count)]
    r3 = lax.ppermute(p3, AXES, pairs(3))
    r2 = lax.ppermute(owned, AXES, pairs(2))
    r1 = lax.ppermute(p1, AXES, pairs(1))
    groups = count // 4
    cross = [(4 * g + 3, 4 * g + 4) for g in range(groups - 1)]
    cross += [(4 * g + 4, 4 * g + 3) for g in range(groups - 1)]
    rc = lax.ppermute(pc, AXES, cross)
    if prep is not None:
        (r1, r2, r3, rc), prep = lax.optimization_barrier(((r1, r2, r3, rc), prep))
    rows = block_rows
    buf = jnp.concatenate([owned[None], r1[None, :rows], r2[None], r3[None, :rows]], 0)
    offs = [0, 1, 2, 3]
    rounds = ROUNDS_32
    pieces = [buf]
    done = None
    for r, group in enumerate(rounds[1:]):
        sent = {m: lax.ppermute(buf, AXES, pairs(m)) for m in sorted(group, key=lambda m: -m)}
        recvs = [sent[m] for m in group]
        if done is None:
            done, recvs = lax.optimization_barrier((middle((r1, r3, rc)), recvs))
        offs = offs + [o ^ m for m in group for o in offs]
        pieces = [buf] + recvs
        if r + 2 < len(rounds):
            buf = jnp.concatenate(pieces, 0)
    assert sorted(offs) == list(range(count))
    where = np.zeros(count, np.int32)
    for p, o in enumerate(offs):
        where[o] = p
    return done, pieces, prep


def band_kernel(fast, n_own, z_ref, off_ref, cur_hbm, *rest):
    if fast:
        r1_hbm, r3_hbm, rc_hbm, bt_hbm, out_ref, ext, bt, sem = rest
    else:
        low_hbm, high_hbm, bt_hbm, out_ref, ext, bt, sem = rest
    blocks, k_band, rows = bt.shape[0], bt.shape[1], bt.shape[2]
    own = cur_hbm.shape[0]
    width = (ext.shape[0] - own) // 2
    low_dst = ext.at[pl.ds(0, width)]
    high_dst = ext.at[pl.ds(width + own, width)]
    mid = pltpu.make_async_copy(cur_hbm, ext.at[pl.ds(width, own)], sem.at[1])
    band_copies = [pltpu.make_async_copy(bt_hbm.at[b], bt.at[b], sem.at[3 + b]) for b in range(blocks)]
    band_copies[0].start()
    mid.start()
    if fast:
        z = z_ref[0]
        low_r1 = pltpu.make_async_copy(r1_hbm.at[pl.ds(n_own, width)], low_dst, sem.at[0])
        low_r3 = pltpu.make_async_copy(r3_hbm.at[pl.ds(n_own, width)], low_dst, sem.at[0])
        low_rc = pltpu.make_async_copy(rc_hbm, low_dst, sem.at[0])
        high_r1 = pltpu.make_async_copy(r1_hbm.at[pl.ds(n_own, width)], high_dst, sem.at[2])
        high_r3 = pltpu.make_async_copy(r3_hbm.at[pl.ds(n_own, width)], high_dst, sem.at[2])
        high_rc = pltpu.make_async_copy(rc_hbm, high_dst, sem.at[2])

        @pl.when(z == 0)
        def _():
            low_rc.start()
            high_r1.start()

        @pl.when(z == 1)
        def _():
            low_r1.start()
            high_r3.start()

        @pl.when(z == 2)
        def _():
            low_r3.start()
            high_r1.start()

        @pl.when(z == 3)
        def _():
            low_r1.start()
            high_rc.start()

        low_wait, high_wait = low_rc, high_rc
    else:
        low_wait = pltpu.make_async_copy(low_hbm, low_dst, sem.at[0])
        high_wait = pltpu.make_async_copy(high_hbm, high_dst, sem.at[2])
        low_wait.start()
        high_wait.start()
    for b in range(1, blocks):
        band_copies[b].start()
    mid.wait()
    low_wait.wait()
    high_wait.wait()
    for b in range(blocks):
        band_copies[b].wait()
        acc = jnp.zeros((rows, out_ref.shape[1]), jnp.float32)

        def near(k):
            n = b + BW + off_ref[b * k_band + k]
            return ext[pl.ds(pl.multiple_of(n * rows, rows), rows), :]

        for k in range(0, k_band - 1, 2):
            lhs = jnp.concatenate([bt[b, k], bt[b, k + 1]], axis=1)
            rhs = jnp.concatenate([near(k), near(k + 1)], axis=0)
            acc = acc + jnp.dot(lhs, rhs, preferred_element_type=jnp.float32)
        if k_band % 2:
            acc = acc + jnp.dot(bt[b, k_band - 1], near(k_band - 1), preferred_element_type=jnp.float32)
        out_ref[pl.ds(b * rows, rows), :] = acc


def band_call(z, band_offsets, current, rim_sources, band_tiles, fast, n_own, width):
    blocks, k_band, rows, _ = band_tiles.shape
    classes = current.shape[1]
    flops = 2 * blocks * k_band * rows * rows * classes
    bytes_accessed = band_tiles.size * 2 + current.size * 2 * 2 + current.size * 4
    return pl.pallas_call(
        functools.partial(band_kernel, fast, n_own),
        cost_estimate=pl.CostEstimate(flops=flops, transcendentals=0, bytes_accessed=bytes_accessed),
        in_specs=[SMEM, SMEM] + [ANY] * (1 + len(rim_sources) + 1),
        out_specs=VMEM,
        out_shape=jax.ShapeDtypeStruct(current.shape, jnp.float32),
        scratch_shapes=[
            pltpu.VMEM((current.shape[0] + 2 * width, classes), current.dtype),
            pltpu.VMEM(band_tiles.shape, band_tiles.dtype),
            pltpu.SemaphoreType.DMA((3 + blocks,)),
        ],
    )(z, band_offsets.reshape(-1), current, *rim_sources, band_tiles)


def hub_kernel(n_hub, width, final, z_ref, hidx_ref, *rest):
    hub_hbm = rest[:n_hub]
    if final:
        (ht_hbm, band_hbm, deg_ref, seeds_hbm, out_ref, hub, ht, band, seeds, sem) = rest[n_hub:]
    else:
        (ht_hbm, band_hbm, deg_ref, seeds_hbm, pick_ref,
         cur_ref, owned_ref, p1_ref, p3_ref, pc_ref,
         hub, ht, band, seeds, sem) = rest[n_hub:]
    blocks, k_hub, rows = ht.shape[0], ht.shape[1], ht.shape[2]
    per_block = []
    for b in range(blocks):
        span = pl.ds(b * rows, rows)
        per_block.append([
            pltpu.make_async_copy(ht_hbm.at[b], ht.at[b], sem.at[n_hub + 4 * b]),
            pltpu.make_async_copy(band_hbm.at[span], band.at[span], sem.at[n_hub + 4 * b + 1]),
            pltpu.make_async_copy(seeds_hbm.at[span], seeds.at[span], sem.at[n_hub + 4 * b + 3]),
        ])
    copies = []
    at = 0
    for i, piece in enumerate(hub_hbm):
        n = piece.shape[0]
        copies.append(pltpu.make_async_copy(piece, hub.at[pl.ds(at, n)], sem.at[i]))
        at += n
    for c in copies:
        c.start()
    for c in per_block[0]:
        c.start()
    for b in range(1, blocks):
        for c in per_block[b]:
            c.start()
    by_row = jnp.transpose(deg_ref[...])
    for c in copies:
        c.wait()
    for b in range(blocks):
        for c in per_block[b]:
            c.wait()
        span = pl.ds(b * rows, rows)
        acc = jnp.zeros((rows, hub.shape[2]), jnp.float32)
        blk = lambda h: hub[hidx_ref[b * k_hub + h]]
        for h in range(0, k_hub - 1, 2):
            lhs = jnp.concatenate([ht[b, h], ht[b, h + 1]], axis=1)
            rhs = jnp.concatenate([blk(h), blk(h + 1)], axis=0)
            acc = acc + jnp.dot(lhs, rhs, preferred_element_type=jnp.float32)
        if k_hub % 2:
            acc = acc + jnp.dot(ht[b, k_hub - 1], blk(k_hub - 1), preferred_element_type=jnp.float32)
        gathered = (band[span] + acc) / by_row[:, b:b + 1]
        labels = spread_weight * gathered + (1.0 - spread_weight) * seeds[span].astype(jnp.float32)
        if final:
            out_ref[span, :] = labels
        else:
            cur_ref[span, :] = labels.astype(cur_ref.dtype)
    if final:
        return
    own = cur_ref.shape[0]
    n_own = owned_ref.shape[0]
    owned = jnp.dot(pick_ref[...], cur_ref[...], preferred_element_type=jnp.float32).astype(owned_ref.dtype)
    owned_ref[...] = owned
    p1_ref[pl.ds(0, n_own), :] = owned
    p3_ref[pl.ds(0, n_own), :] = owned
    z = z_ref[0]
    top = cur_ref[pl.ds(own - width, width), :]
    bottom = cur_ref[pl.ds(0, width), :]
    p1_ref[pl.ds(n_own, width), :] = jnp.where(z % 2 == 0, top, bottom)
    p3_ref[pl.ds(n_own, width), :] = jnp.where(z == 1, top, bottom)
    pc_ref[...] = jnp.where(z == 3, top, bottom)


def hub_call(z, hub_index, pick, hub_pieces, hub_tiles, band, degree, seeds, width, final):
    blocks, k_hub, rows, _ = hub_tiles.shape
    classes = seeds.shape[1]
    n_hub = len(hub_pieces)
    n_hub_blocks = sum(p.shape[0] for p in hub_pieces)
    n_own = pick.shape[0]
    bf = jnp.bfloat16
    flops = 2 * blocks * k_hub * rows * rows * classes
    bytes_accessed = hub_tiles.size * 2 + n_hub_blocks * rows * classes * 2 + seeds.size * 4 * 4
    if final:
        outs = [jax.ShapeDtypeStruct(seeds.shape, jnp.float32)]
    else:
        outs = [
            jax.ShapeDtypeStruct(seeds.shape, bf),
            jax.ShapeDtypeStruct((n_own, classes), bf),
            jax.ShapeDtypeStruct((n_own + width, classes), bf),
            jax.ShapeDtypeStruct((n_own + width, classes), bf),
            jax.ShapeDtypeStruct((width, classes), bf),
        ]
    return pl.pallas_call(
        functools.partial(hub_kernel, n_hub, width, final),
        cost_estimate=pl.CostEstimate(flops=flops, transcendentals=0, bytes_accessed=bytes_accessed),
        in_specs=[SMEM, SMEM] + [ANY] * (n_hub + 2) + [VMEM, ANY] + ([] if final else [VMEM]),
        out_specs=[VMEM] * len(outs),
        out_shape=outs,
        scratch_shapes=[
            pltpu.VMEM((n_hub_blocks, rows, classes), bf),
            pltpu.VMEM(hub_tiles.shape, hub_tiles.dtype),
            pltpu.VMEM(seeds.shape, jnp.float32),
            pltpu.VMEM(seeds.shape, seeds.dtype),
            pltpu.SemaphoreType.DMA((n_hub + 4 * blocks,)),
        ],
    )(z, hub_index, *hub_pieces, hub_tiles, band, degree, seeds, *([] if final else [pick]))


def positions_of(hub_blocks, owned, block_rows):
    count = lax.axis_size(AXES)
    if not fast_path(owned, block_rows):
        return hub_blocks
    offs = [0]
    for group in ROUNDS_32:
        offs = offs + [o ^ m for m in group for o in offs]
    where = np.zeros(count, np.int32)
    for p, o in enumerate(offs):
        where[o] = p
    return jnp.asarray(where)[hub_blocks ^ lax.axis_index(AXES)]


def body(seed_scores, seed_mask, band_offsets, band_tiles, hub_blocks, hub_tiles, hub_rows):
    block_rows = band_tiles.shape[2]
    seeds = seed_mask.astype(jnp.float32)[:, None] * seed_scores.astype(jnp.float32)
    degree = jnp.sum(band_tiles, axis=(1, 3), dtype=jnp.float32) + jnp.sum(
        hub_tiles, axis=(1, 3), dtype=jnp.float32
    )
    lanes = degree.shape[1]
    degree = jnp.zeros((lanes, lanes), jnp.float32).at[: degree.shape[0]].set(degree)
    width = BW * block_rows
    z = lax.axis_index("hub").astype(jnp.int32).reshape(1)
    current = seeds.astype(jnp.bfloat16)
    seeds16 = current
    owned = current[hub_rows]
    p1, p3, pc = payloads(current, owned, z[0], width)
    fast = fast_path(owned, block_rows)
    pick = (hub_rows[:, None] == jnp.arange(current.shape[0], dtype=hub_rows.dtype)[None, :]).astype(jnp.bfloat16)
    prep = (pick, degree, positions_of(hub_blocks, owned, block_rows).reshape(-1))
    for step in range(ITERS):
        middle = functools.partial(
            band_call, z, band_offsets, current, band_tiles=band_tiles, fast=fast, n_own=owned.shape[0], width=width
        )
        band, hub_pieces, prep_out = exchange(
            current, owned, p1, p3, pc, hub_blocks, width, block_rows, lambda rims: middle(rims), prep
        )
        if prep is not None:
            pick, degree, hub_index = prep_out
            prep = None
        final = step + 1 == ITERS
        outs = hub_call(z, hub_index, pick, hub_pieces, hub_tiles, band, degree, seeds16, width, final)
        if final:
            labels = outs[0]
        else:
            current, owned, p1, p3, pc = outs
    return labels


def solution(mesh):
    placed = (
        P(AXES, None),
        P(AXES),
        P(AXES, None),
        P(AXES, None, None, None),
        P(AXES, None),
        P(AXES, None, None, None),
        P(AXES),
    )
    return jax.shard_map(
        body, mesh=mesh, in_specs=placed, out_specs=P(AXES, None), check_vma=False
    )
```

```python
import functools

import jax
import jax.numpy as jnp
import numpy as np
from jax import lax
from jax.experimental import pallas as pl
from jax.experimental.pallas import tpu as pltpu
from jax.sharding import PartitionSpec as P

BW = 2
ITERS = 3
AXES = ("node", "hub")
ROUNDS_32 = ((1, 2, 3), (8, 16, 24), (4,))


spread_weight = 0.8

SMEM = pl.BlockSpec(memory_space=pltpu.SMEM)
ANY = pl.BlockSpec(memory_space=pl.ANY)
VMEM = pl.BlockSpec(memory_space=pltpu.VMEM)


def fast_path(owned, block_rows):
    count = lax.axis_size(AXES)
    return count == 32 and owned.shape[0] == block_rows and lax.axis_size("hub") == 4


def payloads(current, owned, z, width):
    top = current[current.shape[0] - width:]
    bottom = current[:width]
    p1 = jnp.concatenate([owned, jnp.where(z % 2 == 0, top, bottom)], 0)
    p3 = jnp.concatenate([owned, jnp.where(z == 1, top, bottom)], 0)
    pc = jnp.where(z == 3, top, bottom)
    return p1, p3, pc


def exchange(current, owned, p1, p3, pc, hub_blocks, width, block_rows, middle, prep):
    count = lax.axis_size(AXES)
    if not fast_path(owned, block_rows):
        forward = [(i, i + 1) for i in range(count - 1)]
        backward = [(target, source) for source, target in forward]
        low = lax.ppermute(current[current.shape[0] - width:], AXES, forward)
        high = lax.ppermute(current[:width], AXES, backward)
        hub_all = lax.all_gather(owned, AXES, axis=0, tiled=True)
        return middle((low, high)), [hub_all.reshape(-1, block_rows, owned.shape[1])], prep
    me = lax.axis_index(AXES)
    pairs = lambda m: [(i, i ^ m) for i in range(count)]
    r3 = lax.ppermute(p3, AXES, pairs(3))
    r2 = lax.ppermute(owned, AXES, pairs(2))
    r1 = lax.ppermute(p1, AXES, pairs(1))
    groups = count // 4
    cross = [(4 * g + 3, 4 * g + 4) for g in range(groups - 1)]
    cross += [(4 * g + 4, 4 * g + 3) for g in range(groups - 1)]
    rc = lax.ppermute(pc, AXES, cross)
    if prep is not None:
        (r1, r2, r3, rc), prep = lax.optimization_barrier(((r1, r2, r3, rc), prep))
    rows = block_rows
    buf = jnp.concatenate([owned[None], r1[None, :rows], r2[None], r3[None, :rows]], 0)
    offs = [0, 1, 2, 3]
    rounds = ROUNDS_32
    pieces = [buf]
    done = None
    for r, group in enumerate(rounds[1:]):
        sent = {m: lax.ppermute(buf, AXES, pairs(m)) for m in sorted(group, key=lambda m: -m)}
        recvs = [sent[m] for m in group]
        if done is None:
            done, recvs = lax.optimization_barrier((middle((r1, r3, rc)), recvs))
        offs = offs + [o ^ m for m in group for o in offs]
        pieces = [buf] + recvs
        if r + 2 < len(rounds):
            buf = jnp.concatenate(pieces, 0)
    assert sorted(offs) == list(range(count))
    where = np.zeros(count, np.int32)
    for p, o in enumerate(offs):
        where[o] = p
    return done, pieces, prep


def band_kernel(fast, n_own, z_ref, off_ref, cur_hbm, *rest):
    if fast:
        r1_hbm, r3_hbm, rc_hbm, bt_hbm, out_hbm, ext, bt, stage, sem = rest
    else:
        low_hbm, high_hbm, bt_hbm, out_hbm, ext, bt, stage, sem = rest
    blocks, k_band, rows = bt.shape[0], bt.shape[1], bt.shape[2]
    own = cur_hbm.shape[0]
    width = (ext.shape[0] - own) // 2
    low_dst = ext.at[pl.ds(0, width)]
    high_dst = ext.at[pl.ds(width + own, width)]
    mid = pltpu.make_async_copy(cur_hbm, ext.at[pl.ds(width, own)], sem.at[1])
    band_copies = [pltpu.make_async_copy(bt_hbm.at[b], bt.at[b], sem.at[3 + b]) for b in range(blocks)]
    band_copies[0].start()
    mid.start()
    if fast:
        z = z_ref[0]
        low_r1 = pltpu.make_async_copy(r1_hbm.at[pl.ds(n_own, width)], low_dst, sem.at[0])
        low_r3 = pltpu.make_async_copy(r3_hbm.at[pl.ds(n_own, width)], low_dst, sem.at[0])
        low_rc = pltpu.make_async_copy(rc_hbm, low_dst, sem.at[0])
        high_r1 = pltpu.make_async_copy(r1_hbm.at[pl.ds(n_own, width)], high_dst, sem.at[2])
        high_r3 = pltpu.make_async_copy(r3_hbm.at[pl.ds(n_own, width)], high_dst, sem.at[2])
        high_rc = pltpu.make_async_copy(rc_hbm, high_dst, sem.at[2])

        @pl.when(z == 0)
        def _():
            low_rc.start()
            high_r1.start()

        @pl.when(z == 1)
        def _():
            low_r1.start()
            high_r3.start()

        @pl.when(z == 2)
        def _():
            low_r3.start()
            high_r1.start()

        @pl.when(z == 3)
        def _():
            low_r1.start()
            high_rc.start()

        low_wait, high_wait = low_rc, high_rc
    else:
        low_wait = pltpu.make_async_copy(low_hbm, low_dst, sem.at[0])
        high_wait = pltpu.make_async_copy(high_hbm, high_dst, sem.at[2])
        low_wait.start()
        high_wait.start()
    for b in range(1, blocks):
        band_copies[b].start()
    mid.wait()
    low_wait.wait()
    high_wait.wait()
    outs = []
    for b in range(blocks):
        band_copies[b].wait()
        acc = jnp.zeros((rows, stage.shape[1]), jnp.float32)

        def near(k):
            n = b + BW + off_ref[b * k_band + k]
            return ext[pl.ds(pl.multiple_of(n * rows, rows), rows), :]

        for k in range(0, k_band - 1, 2):
            lhs = jnp.concatenate([bt[b, k], bt[b, k + 1]], axis=1)
            rhs = jnp.concatenate([near(k), near(k + 1)], axis=0)
            acc = acc + jnp.dot(lhs, rhs, preferred_element_type=jnp.float32)
        if k_band % 2:
            acc = acc + jnp.dot(bt[b, k_band - 1], near(k_band - 1), preferred_element_type=jnp.float32)
        span = pl.ds(b * rows, rows)
        stage[span, :] = acc
        outs.append(pltpu.make_async_copy(stage.at[span], out_hbm.at[span], sem.at[3 + blocks + b]))
        outs[-1].start()
    for c in outs:
        c.wait()


def band_call(z, band_offsets, current, rim_sources, band_tiles, fast, n_own, width):
    blocks, k_band, rows, _ = band_tiles.shape
    classes = current.shape[1]
    flops = 2 * blocks * k_band * rows * rows * classes
    bytes_accessed = band_tiles.size * 2 + current.size * 2 * 2 + current.size * 4
    return pl.pallas_call(
        functools.partial(band_kernel, fast, n_own),
        cost_estimate=pl.CostEstimate(flops=flops, transcendentals=0, bytes_accessed=bytes_accessed),
        in_specs=[SMEM, SMEM] + [ANY] * (1 + len(rim_sources) + 1),
        out_specs=ANY,
        out_shape=jax.ShapeDtypeStruct(current.shape, jnp.float32),
        scratch_shapes=[
            pltpu.VMEM((current.shape[0] + 2 * width, classes), current.dtype),
            pltpu.VMEM(band_tiles.shape, band_tiles.dtype),
            pltpu.VMEM(current.shape, jnp.float32),
            pltpu.SemaphoreType.DMA((3 + 2 * blocks,)),
        ],
    )(z, band_offsets.reshape(-1), current, *rim_sources, band_tiles)


def hub_kernel(n_hub, width, final, z_ref, hidx_ref, *rest):
    hub_hbm = rest[:n_hub]
    if final:
        (ht_hbm, band_hbm, deg_ref, seeds_hbm, out_hbm, hub, ht, band, seeds, stage, sem) = rest[n_hub:]
    else:
        (ht_hbm, band_hbm, deg_ref, seeds_hbm, pick_ref,
         cur_ref, owned_ref, p1_ref, p3_ref, pc_ref,
         hub, ht, band, seeds, sem) = rest[n_hub:]
    blocks, k_hub, rows = ht.shape[0], ht.shape[1], ht.shape[2]
    per_block = []
    for b in range(blocks):
        span = pl.ds(b * rows, rows)
        per_block.append([
            pltpu.make_async_copy(ht_hbm.at[b], ht.at[b], sem.at[n_hub + 4 * b]),
            pltpu.make_async_copy(band_hbm.at[span], band.at[span], sem.at[n_hub + 4 * b + 1]),
            pltpu.make_async_copy(seeds_hbm.at[span], seeds.at[span], sem.at[n_hub + 4 * b + 3]),
        ])
    copies = []
    at = 0
    for i, piece in enumerate(hub_hbm):
        n = piece.shape[0]
        copies.append(pltpu.make_async_copy(piece, hub.at[pl.ds(at, n)], sem.at[i]))
        at += n
    for c in copies:
        c.start()
    for c in per_block[0]:
        c.start()
    for b in range(1, blocks):
        for c in per_block[b]:
            c.start()
    by_row = jnp.transpose(deg_ref[...])
    outs = []
    for c in copies:
        c.wait()
    for b in range(blocks):
        for c in per_block[b]:
            c.wait()
        span = pl.ds(b * rows, rows)
        acc = jnp.zeros((rows, hub.shape[2]), jnp.float32)
        blk = lambda h: hub[hidx_ref[b * k_hub + h]]
        for h in range(0, k_hub - 1, 2):
            lhs = jnp.concatenate([ht[b, h], ht[b, h + 1]], axis=1)
            rhs = jnp.concatenate([blk(h), blk(h + 1)], axis=0)
            acc = acc + jnp.dot(lhs, rhs, preferred_element_type=jnp.float32)
        if k_hub % 2:
            acc = acc + jnp.dot(ht[b, k_hub - 1], blk(k_hub - 1), preferred_element_type=jnp.float32)
        gathered = (band[span] + acc) / by_row[:, b:b + 1]
        labels = spread_weight * gathered + (1.0 - spread_weight) * seeds[span].astype(jnp.float32)
        if final:
            stage[span, :] = labels
            outs.append(pltpu.make_async_copy(stage.at[span], out_hbm.at[span], sem.at[n_hub + 4 * blocks + b]))
            outs[-1].start()
        else:
            cur_ref[span, :] = labels.astype(cur_ref.dtype)
    if final:
        for c in outs:
            c.wait()
        return
    own = cur_ref.shape[0]
    n_own = owned_ref.shape[0]
    owned = jnp.dot(pick_ref[...], cur_ref[...], preferred_element_type=jnp.float32).astype(owned_ref.dtype)
    owned_ref[...] = owned
    p1_ref[pl.ds(0, n_own), :] = owned
    p3_ref[pl.ds(0, n_own), :] = owned
    z = z_ref[0]
    top = cur_ref[pl.ds(own - width, width), :]
    bottom = cur_ref[pl.ds(0, width), :]
    p1_ref[pl.ds(n_own, width), :] = jnp.where(z % 2 == 0, top, bottom)
    p3_ref[pl.ds(n_own, width), :] = jnp.where(z == 1, top, bottom)
    pc_ref[...] = jnp.where(z == 3, top, bottom)


def hub_call(z, hub_index, pick, hub_pieces, hub_tiles, band, degree, seeds, width, final):
    blocks, k_hub, rows, _ = hub_tiles.shape
    classes = seeds.shape[1]
    n_hub = len(hub_pieces)
    n_hub_blocks = sum(p.shape[0] for p in hub_pieces)
    n_own = pick.shape[0]
    bf = jnp.bfloat16
    flops = 2 * blocks * k_hub * rows * rows * classes
    bytes_accessed = hub_tiles.size * 2 + n_hub_blocks * rows * classes * 2 + seeds.size * 4 * 4
    if final:
        outs = [jax.ShapeDtypeStruct(seeds.shape, jnp.float32)]
    else:
        outs = [
            jax.ShapeDtypeStruct(seeds.shape, bf),
            jax.ShapeDtypeStruct((n_own, classes), bf),
            jax.ShapeDtypeStruct((n_own + width, classes), bf),
            jax.ShapeDtypeStruct((n_own + width, classes), bf),
            jax.ShapeDtypeStruct((width, classes), bf),
        ]
    return pl.pallas_call(
        functools.partial(hub_kernel, n_hub, width, final),
        cost_estimate=pl.CostEstimate(flops=flops, transcendentals=0, bytes_accessed=bytes_accessed),
        in_specs=[SMEM, SMEM] + [ANY] * (n_hub + 2) + [VMEM, ANY] + ([] if final else [VMEM]),
        out_specs=[ANY] if final else [VMEM] * len(outs),
        out_shape=outs,
        scratch_shapes=[
            pltpu.VMEM((n_hub_blocks, rows, classes), bf),
            pltpu.VMEM(hub_tiles.shape, hub_tiles.dtype),
            pltpu.VMEM(seeds.shape, jnp.float32),
            pltpu.VMEM(seeds.shape, seeds.dtype),
            *([pltpu.VMEM(seeds.shape, jnp.float32)] if final else []),
            pltpu.SemaphoreType.DMA((n_hub + 5 * blocks,)),
        ],
    )(z, hub_index, *hub_pieces, hub_tiles, band, degree, seeds, *([] if final else [pick]))


def positions_of(hub_blocks, owned, block_rows):
    count = lax.axis_size(AXES)
    if not fast_path(owned, block_rows):
        return hub_blocks
    offs = [0]
    for group in ROUNDS_32:
        offs = offs + [o ^ m for m in group for o in offs]
    where = np.zeros(count, np.int32)
    for p, o in enumerate(offs):
        where[o] = p
    return jnp.asarray(where)[hub_blocks ^ lax.axis_index(AXES)]


def body(seed_scores, seed_mask, band_offsets, band_tiles, hub_blocks, hub_tiles, hub_rows):
    block_rows = band_tiles.shape[2]
    seeds = seed_mask.astype(jnp.float32)[:, None] * seed_scores.astype(jnp.float32)
    degree = jnp.sum(band_tiles, axis=(1, 3), dtype=jnp.float32) + jnp.sum(
        hub_tiles, axis=(1, 3), dtype=jnp.float32
    )
    lanes = degree.shape[1]
    degree = jnp.zeros((lanes, lanes), jnp.float32).at[: degree.shape[0]].set(degree)
    width = BW * block_rows
    z = lax.axis_index("hub").astype(jnp.int32).reshape(1)
    current = seeds.astype(jnp.bfloat16)
    seeds16 = current
    owned = current[hub_rows]
    p1, p3, pc = payloads(current, owned, z[0], width)
    fast = fast_path(owned, block_rows)
    pick = (hub_rows[:, None] == jnp.arange(current.shape[0], dtype=hub_rows.dtype)[None, :]).astype(jnp.bfloat16)
    prep = (pick, degree, positions_of(hub_blocks, owned, block_rows).reshape(-1))
    for step in range(ITERS):
        middle = functools.partial(
            band_call, z, band_offsets, current, band_tiles=band_tiles, fast=fast, n_own=owned.shape[0], width=width
        )
        band, hub_pieces, prep_out = exchange(
            current, owned, p1, p3, pc, hub_blocks, width, block_rows, lambda rims: middle(rims), prep
        )
        if prep is not None:
            pick, degree, hub_index = prep_out
            prep = None
        final = step + 1 == ITERS
        outs = hub_call(z, hub_index, pick, hub_pieces, hub_tiles, band, degree, seeds16, width, final)
        if final:
            labels = outs[0]
        else:
            current, owned, p1, p3, pc = outs
    return labels


def solution(mesh):
    placed = (
        P(AXES, None),
        P(AXES),
        P(AXES, None),
        P(AXES, None, None, None),
        P(AXES, None),
        P(AXES, None, None, None),
        P(AXES),
    )
    return jax.shard_map(
        body, mesh=mesh, in_specs=placed, out_specs=P(AXES, None), check_vma=False
    )
```

```python
import functools

import jax
import jax.numpy as jnp
import numpy as np
from jax import lax
from jax.experimental import pallas as pl
from jax.experimental.pallas import tpu as pltpu
from jax.sharding import PartitionSpec as P

BW = 2
ITERS = 3
AXES = ("node", "hub")
ROUNDS_32 = ((1, 2, 3), (8, 16, 24), (4,))


spread_weight = 0.8

SMEM = pl.BlockSpec(memory_space=pltpu.SMEM)
ANY = pl.BlockSpec(memory_space=pl.ANY)
VMEM = pl.BlockSpec(memory_space=pltpu.VMEM)


def fast_path(owned, block_rows):
    count = lax.axis_size(AXES)
    return count == 32 and owned.shape[0] == block_rows and lax.axis_size("hub") == 4


def payloads(current, owned, z, width):
    top = current[current.shape[0] - width:]
    bottom = current[:width]
    p1 = jnp.concatenate([owned, jnp.where(z % 2 == 0, top, bottom)], 0)
    p3 = jnp.concatenate([owned, jnp.where(z == 1, top, bottom)], 0)
    pc = jnp.where(z == 3, top, bottom)
    return p1, p3, pc


def exchange(current, owned, p1, p3, pc, hub_blocks, width, block_rows, first, middle, prep):
    count = lax.axis_size(AXES)
    if not fast_path(owned, block_rows):
        forward = [(i, i + 1) for i in range(count - 1)]
        backward = [(target, source) for source, target in forward]
        low = lax.ppermute(current[current.shape[0] - width:], AXES, forward)
        high = lax.ppermute(current[:width], AXES, backward)
        hub_all = lax.all_gather(owned, AXES, axis=0, tiled=True)
        done = (first(), middle((low, high)))
        return done, [hub_all.reshape(-1, block_rows, owned.shape[1])], prep
    me = lax.axis_index(AXES)
    pairs = lambda m: [(i, i ^ m) for i in range(count)]
    r3 = lax.ppermute(p3, AXES, pairs(3))
    r2 = lax.ppermute(owned, AXES, pairs(2))
    r1 = lax.ppermute(p1, AXES, pairs(1))
    groups = count // 4
    cross = [(4 * g + 3, 4 * g + 4) for g in range(groups - 1)]
    cross += [(4 * g + 4, 4 * g + 3) for g in range(groups - 1)]
    rc = lax.ppermute(pc, AXES, cross)
    (r1, r2, r3, rc), (inner, prep) = lax.optimization_barrier(((r1, r2, r3, rc), (first(), prep)))
    rows = block_rows
    buf = jnp.concatenate([owned[None], r1[None, :rows], r2[None], r3[None, :rows]], 0)
    offs = [0, 1, 2, 3]
    rounds = ROUNDS_32
    pieces = [buf]
    done = None
    for r, group in enumerate(rounds[1:]):
        sent = {m: lax.ppermute(buf, AXES, pairs(m)) for m in sorted(group, key=lambda m: -m)}
        recvs = [sent[m] for m in group]
        if done is None:
            done, recvs = lax.optimization_barrier((middle((r1, r3, rc)), recvs))
        offs = offs + [o ^ m for m in group for o in offs]
        pieces = [buf] + recvs
        if r + 2 < len(rounds):
            buf = jnp.concatenate(pieces, 0)
    assert sorted(offs) == list(range(count))
    where = np.zeros(count, np.int32)
    for p, o in enumerate(offs):
        where[o] = p
    return (inner, done), pieces, prep


def inner_blocks(blocks):
    return [b for b in range(blocks) if b - BW >= 0 and b + BW < blocks]


def band_kernel(fast, n_own, chosen, z_ref, off_ref, cur_hbm, *rest):
    if not chosen[1]:
        bt_hbm, out_hbm, ext, bt, stage, sem = rest
    elif fast:
        r1_hbm, r3_hbm, rc_hbm, bt_hbm, out_hbm, ext, bt, stage, sem = rest
    else:
        low_hbm, high_hbm, bt_hbm, out_hbm, ext, bt, stage, sem = rest
    chosen, with_rims = chosen
    blocks, k_band, rows = bt.shape[0], bt.shape[1], bt.shape[2]
    own = cur_hbm.shape[0]
    width = (ext.shape[0] - own) // 2
    low_dst = ext.at[pl.ds(0, width)]
    high_dst = ext.at[pl.ds(width + own, width)]
    mid = pltpu.make_async_copy(cur_hbm, ext.at[pl.ds(width, own)], sem.at[1])
    band_copies = [pltpu.make_async_copy(bt_hbm.at[g], bt.at[b], sem.at[3 + b]) for b, g in enumerate(chosen)]
    band_copies[0].start()
    mid.start()
    if not with_rims:
        low_wait = high_wait = None
    elif fast:
        z = z_ref[0]
        low_r1 = pltpu.make_async_copy(r1_hbm.at[pl.ds(n_own, width)], low_dst, sem.at[0])
        low_r3 = pltpu.make_async_copy(r3_hbm.at[pl.ds(n_own, width)], low_dst, sem.at[0])
        low_rc = pltpu.make_async_copy(rc_hbm, low_dst, sem.at[0])
        high_r1 = pltpu.make_async_copy(r1_hbm.at[pl.ds(n_own, width)], high_dst, sem.at[2])
        high_r3 = pltpu.make_async_copy(r3_hbm.at[pl.ds(n_own, width)], high_dst, sem.at[2])
        high_rc = pltpu.make_async_copy(rc_hbm, high_dst, sem.at[2])

        @pl.when(z == 0)
        def _():
            low_rc.start()
            high_r1.start()

        @pl.when(z == 1)
        def _():
            low_r1.start()
            high_r3.start()

        @pl.when(z == 2)
        def _():
            low_r3.start()
            high_r1.start()

        @pl.when(z == 3)
        def _():
            low_r1.start()
            high_rc.start()

        low_wait, high_wait = low_rc, high_rc
    else:
        low_wait = pltpu.make_async_copy(low_hbm, low_dst, sem.at[0])
        high_wait = pltpu.make_async_copy(high_hbm, high_dst, sem.at[2])
        low_wait.start()
        high_wait.start()
    for b in range(1, blocks):
        band_copies[b].start()
    mid.wait()
    if with_rims:
        low_wait.wait()
        high_wait.wait()
    outs = []
    for i, g in enumerate(chosen):
        b = i
        band_copies[b].wait()
        acc = jnp.zeros((rows, stage.shape[1]), jnp.float32)

        def near(k):
            n = g + BW + off_ref[g * k_band + k]
            return ext[pl.ds(pl.multiple_of(n * rows, rows), rows), :]

        for k in range(0, k_band - 1, 2):
            lhs = jnp.concatenate([bt[b, k], bt[b, k + 1]], axis=1)
            rhs = jnp.concatenate([near(k), near(k + 1)], axis=0)
            acc = acc + jnp.dot(lhs, rhs, preferred_element_type=jnp.float32)
        if k_band % 2:
            acc = acc + jnp.dot(bt[b, k_band - 1], near(k_band - 1), preferred_element_type=jnp.float32)
        span = pl.ds(b * rows, rows)
        stage[span, :] = acc
        outs.append(pltpu.make_async_copy(stage.at[span], out_hbm.at[span], sem.at[3 + blocks + b]))
        outs[-1].start()
    for c in outs:
        c.wait()


def band_call(z, band_offsets, current, rim_sources, band_tiles, fast, n_own, width, inner):
    all_blocks, k_band, rows, _ = band_tiles.shape
    middle = inner_blocks(all_blocks)
    chosen = middle if inner else [b for b in range(all_blocks) if b not in middle]
    blocks = len(chosen)
    classes = current.shape[1]
    flops = 2 * blocks * k_band * rows * rows * classes
    bytes_accessed = band_tiles.size * 2 + current.size * 2 * 2 + current.size * 4
    return pl.pallas_call(
        functools.partial(band_kernel, fast, n_own, (tuple(chosen), not inner)),
        cost_estimate=pl.CostEstimate(flops=flops, transcendentals=0, bytes_accessed=bytes_accessed),
        in_specs=[SMEM, SMEM] + [ANY] * (1 + len(rim_sources) + 1),
        out_specs=ANY,
        out_shape=jax.ShapeDtypeStruct((blocks * rows, classes), jnp.float32),
        scratch_shapes=[
            pltpu.VMEM((current.shape[0] + 2 * width, classes), current.dtype),
            pltpu.VMEM((blocks,) + band_tiles.shape[1:], band_tiles.dtype),
            pltpu.VMEM((blocks * rows, classes), jnp.float32),
            pltpu.SemaphoreType.DMA((3 + 2 * blocks,)),
        ],
    )(z, band_offsets.reshape(-1), current, *(() if inner else rim_sources), band_tiles)


def hub_kernel(n_hub, width, final, z_ref, hidx_ref, *rest):
    hub_hbm = rest[:n_hub]
    if final:
        (ht_hbm, band_in, band_edge, deg_ref, seeds_hbm, out_hbm, hub, ht, band, seeds, stage, sem) = rest[n_hub:]
    else:
        (ht_hbm, band_in, band_edge, deg_ref, seeds_hbm, pick_ref,
         cur_ref, owned_ref, p1_ref, p3_ref, pc_ref,
         hub, ht, band, seeds, sem) = rest[n_hub:]
    blocks, k_hub, rows = ht.shape[0], ht.shape[1], ht.shape[2]
    middle = inner_blocks(blocks)
    edge = [b for b in range(blocks) if b not in middle]
    per_block = []
    for b in range(blocks):
        span = pl.ds(b * rows, rows)
        per_block.append([
            pltpu.make_async_copy(ht_hbm.at[b], ht.at[b], sem.at[n_hub + 4 * b]),
            pltpu.make_async_copy(
                band_in.at[pl.ds(middle.index(b) * rows, rows)] if b in middle
                else band_edge.at[pl.ds(edge.index(b) * rows, rows)],
                band.at[span],
                sem.at[n_hub + 4 * b + 1],
            ),
            pltpu.make_async_copy(seeds_hbm.at[span], seeds.at[span], sem.at[n_hub + 4 * b + 3]),
        ])
    copies = []
    at = 0
    for i, piece in enumerate(hub_hbm):
        n = piece.shape[0]
        copies.append(pltpu.make_async_copy(piece, hub.at[pl.ds(at, n)], sem.at[i]))
        at += n
    for c in copies:
        c.start()
    for c in per_block[0]:
        c.start()
    for b in range(1, blocks):
        for c in per_block[b]:
            c.start()
    by_row = jnp.transpose(deg_ref[...])
    outs = []
    for c in copies:
        c.wait()
    for b in range(blocks):
        for c in per_block[b]:
            c.wait()
        span = pl.ds(b * rows, rows)
        acc = jnp.zeros((rows, hub.shape[2]), jnp.float32)
        blk = lambda h: hub[hidx_ref[b * k_hub + h]]
        for h in range(0, k_hub - 1, 2):
            lhs = jnp.concatenate([ht[b, h], ht[b, h + 1]], axis=1)
            rhs = jnp.concatenate([blk(h), blk(h + 1)], axis=0)
            acc = acc + jnp.dot(lhs, rhs, preferred_element_type=jnp.float32)
        if k_hub % 2:
            acc = acc + jnp.dot(ht[b, k_hub - 1], blk(k_hub - 1), preferred_element_type=jnp.float32)
        gathered = (band[span] + acc) / by_row[:, b:b + 1]
        labels = spread_weight * gathered + (1.0 - spread_weight) * seeds[span].astype(jnp.float32)
        if final:
            stage[span, :] = labels
            outs.append(pltpu.make_async_copy(stage.at[span], out_hbm.at[span], sem.at[n_hub + 4 * blocks + b]))
            outs[-1].start()
        else:
            cur_ref[span, :] = labels.astype(cur_ref.dtype)
    if final:
        for c in outs:
            c.wait()
        return
    own = cur_ref.shape[0]
    n_own = owned_ref.shape[0]
    owned = jnp.dot(pick_ref[...], cur_ref[...], preferred_element_type=jnp.float32).astype(owned_ref.dtype)
    owned_ref[...] = owned
    p1_ref[pl.ds(0, n_own), :] = owned
    p3_ref[pl.ds(0, n_own), :] = owned
    z = z_ref[0]
    top = cur_ref[pl.ds(own - width, width), :]
    bottom = cur_ref[pl.ds(0, width), :]
    p1_ref[pl.ds(n_own, width), :] = jnp.where(z % 2 == 0, top, bottom)
    p3_ref[pl.ds(n_own, width), :] = jnp.where(z == 1, top, bottom)
    pc_ref[...] = jnp.where(z == 3, top, bottom)


def hub_call(z, hub_index, pick, hub_pieces, hub_tiles, band, degree, seeds, width, final):
    blocks, k_hub, rows, _ = hub_tiles.shape
    classes = seeds.shape[1]
    n_hub = len(hub_pieces)
    n_hub_blocks = sum(p.shape[0] for p in hub_pieces)
    n_own = pick.shape[0]
    bf = jnp.bfloat16
    flops = 2 * blocks * k_hub * rows * rows * classes
    bytes_accessed = hub_tiles.size * 2 + n_hub_blocks * rows * classes * 2 + seeds.size * 4 * 4
    if final:
        outs = [jax.ShapeDtypeStruct(seeds.shape, jnp.float32)]
    else:
        outs = [
            jax.ShapeDtypeStruct(seeds.shape, bf),
            jax.ShapeDtypeStruct((n_own, classes), bf),
            jax.ShapeDtypeStruct((n_own + width, classes), bf),
            jax.ShapeDtypeStruct((n_own + width, classes), bf),
            jax.ShapeDtypeStruct((width, classes), bf),
        ]
    return pl.pallas_call(
        functools.partial(hub_kernel, n_hub, width, final),
        cost_estimate=pl.CostEstimate(flops=flops, transcendentals=0, bytes_accessed=bytes_accessed),
        in_specs=[SMEM, SMEM] + [ANY] * (n_hub + 3) + [VMEM, ANY] + ([] if final else [VMEM]),
        out_specs=[ANY] if final else [VMEM] * len(outs),
        out_shape=outs,
        scratch_shapes=[
            pltpu.VMEM((n_hub_blocks, rows, classes), bf),
            pltpu.VMEM(hub_tiles.shape, hub_tiles.dtype),
            pltpu.VMEM(seeds.shape, jnp.float32),
            pltpu.VMEM(seeds.shape, seeds.dtype),
            *([pltpu.VMEM(seeds.shape, jnp.float32)] if final else []),
            pltpu.SemaphoreType.DMA((n_hub + 5 * blocks,)),
        ],
    )(z, hub_index, *hub_pieces, hub_tiles, *band, degree, seeds, *([] if final else [pick]))


def positions_of(hub_blocks, owned, block_rows):
    count = lax.axis_size(AXES)
    if not fast_path(owned, block_rows):
        return hub_blocks
    offs = [0]
    for group in ROUNDS_32:
        offs = offs + [o ^ m for m in group for o in offs]
    where = np.zeros(count, np.int32)
    for p, o in enumerate(offs):
        where[o] = p
    return jnp.asarray(where)[hub_blocks ^ lax.axis_index(AXES)]


def body(seed_scores, seed_mask, band_offsets, band_tiles, hub_blocks, hub_tiles, hub_rows):
    block_rows = band_tiles.shape[2]
    seeds = seed_mask.astype(jnp.float32)[:, None] * seed_scores.astype(jnp.float32)
    degree = jnp.sum(band_tiles, axis=(1, 3), dtype=jnp.float32) + jnp.sum(
        hub_tiles, axis=(1, 3), dtype=jnp.float32
    )
    lanes = degree.shape[1]
    degree = jnp.zeros((lanes, lanes), jnp.float32).at[: degree.shape[0]].set(degree)
    width = BW * block_rows
    z = lax.axis_index("hub").astype(jnp.int32).reshape(1)
    current = seeds.astype(jnp.bfloat16)
    seeds16 = current
    owned = current[hub_rows]
    p1, p3, pc = payloads(current, owned, z[0], width)
    fast = fast_path(owned, block_rows)
    pick = (hub_rows[:, None] == jnp.arange(current.shape[0], dtype=hub_rows.dtype)[None, :]).astype(jnp.bfloat16)
    prep = (pick, degree, positions_of(hub_blocks, owned, block_rows).reshape(-1))
    for step in range(ITERS):
        middle = functools.partial(
            band_call, z, band_offsets, current, band_tiles=band_tiles, fast=fast, n_own=owned.shape[0], width=width
        )
        band, hub_pieces, prep_out = exchange(
            current, owned, p1, p3, pc, hub_blocks, width, block_rows,
            lambda: middle((), inner=True), lambda rims: middle(rims, inner=False), prep,
        )
        if prep is not None:
            pick, degree, hub_index = prep_out
            prep = None
        final = step + 1 == ITERS
        outs = hub_call(z, hub_index, pick, hub_pieces, hub_tiles, band, degree, seeds16, width, final)
        if final:
            labels = outs[0]
        else:
            current, owned, p1, p3, pc = outs
    return labels


def solution(mesh):
    placed = (
        P(AXES, None),
        P(AXES),
        P(AXES, None),
        P(AXES, None, None, None),
        P(AXES, None),
        P(AXES, None, None, None),
        P(AXES),
    )
    return jax.shard_map(
        body, mesh=mesh, in_specs=placed, out_specs=P(AXES, None), check_vma=False
    )
```

```python
import functools

import jax
import jax.numpy as jnp
import numpy as np
from jax import lax
from jax.experimental import pallas as pl
from jax.experimental.pallas import tpu as pltpu
from jax.sharding import PartitionSpec as P

BW = 2
ITERS = 3
AXES = ("node", "hub")
ROUNDS_32 = ((1, 2, 3), (8, 16, 24), (4,))


spread_weight = 0.8

SMEM = pl.BlockSpec(memory_space=pltpu.SMEM)
ANY = pl.BlockSpec(memory_space=pl.ANY)
VMEM = pl.BlockSpec(memory_space=pltpu.VMEM)


def fast_path(owned, block_rows):
    count = lax.axis_size(AXES)
    return count == 32 and owned.shape[0] == block_rows and lax.axis_size("hub") == 4


def payloads(current, owned, z, width):
    top = current[current.shape[0] - width:]
    bottom = current[:width]
    p1 = jnp.concatenate([owned, jnp.where(z % 2 == 0, top, bottom)], 0)
    p3 = jnp.concatenate([owned, jnp.where(z == 1, top, bottom)], 0)
    pc = jnp.where((z == 3) | (z == 1), top, bottom)
    return p1, p3, pc


def exchange(current, owned, p1, p3, pc, hub_blocks, width, block_rows, middle, prep):
    count = lax.axis_size(AXES)
    if not fast_path(owned, block_rows):
        forward = [(i, i + 1) for i in range(count - 1)]
        backward = [(target, source) for source, target in forward]
        low = lax.ppermute(current[current.shape[0] - width:], AXES, forward)
        high = lax.ppermute(current[:width], AXES, backward)
        hub_all = lax.all_gather(owned, AXES, axis=0, tiled=True)
        return middle((low, high)), [hub_all.reshape(-1, block_rows, owned.shape[1])], prep
    me = lax.axis_index(AXES)
    pairs = lambda m: [(i, i ^ m) for i in range(count)]
    r3 = lax.ppermute(owned, AXES, pairs(3))
    r2 = lax.ppermute(owned, AXES, pairs(2))
    r1 = lax.ppermute(p1, AXES, pairs(1))
    groups = count // 4
    cross = [(4 * g + 3, 4 * g + 4) for g in range(groups - 1)]
    cross += [(4 * g + 4, 4 * g + 3) for g in range(groups - 1)]
    cross += [(4 * g + 1, 4 * g + 2) for g in range(groups)] + [(4 * g + 2, 4 * g + 1) for g in range(groups)]
    rc = lax.ppermute(pc, AXES, cross)
    if prep is not None:
        (r1, r2, r3, rc), prep = lax.optimization_barrier(((r1, r2, r3, rc), prep))
    rows = block_rows
    buf = jnp.concatenate([owned[None], r1[None, :rows], r2[None], r3[None]], 0)
    offs = [0, 1, 2, 3]
    rounds = ROUNDS_32
    pieces = [buf]
    done = None
    for r, group in enumerate(rounds[1:]):
        sent = {m: lax.ppermute(buf, AXES, pairs(m)) for m in sorted(group, key=lambda m: -m)}
        recvs = [sent[m] for m in group]
        if done is None:
            done, recvs = lax.optimization_barrier((middle((r1, r3, rc)), recvs))
        offs = offs + [o ^ m for m in group for o in offs]
        pieces = [buf] + recvs
        if r + 2 < len(rounds):
            buf = jnp.concatenate(pieces, 0)
    assert sorted(offs) == list(range(count))
    where = np.zeros(count, np.int32)
    for p, o in enumerate(offs):
        where[o] = p
    return done, pieces, prep


def band_kernel(fast, n_own, z_ref, off_ref, cur_hbm, *rest):
    if fast:
        r1_hbm, r3_hbm, rc_hbm, bt_hbm, out_ref, ext, bt, sem = rest
    else:
        low_hbm, high_hbm, bt_hbm, out_ref, ext, bt, sem = rest
    blocks, k_band, rows = bt.shape[0], bt.shape[1], bt.shape[2]
    own = cur_hbm.shape[0]
    width = (ext.shape[0] - own) // 2
    low_dst = ext.at[pl.ds(0, width)]
    high_dst = ext.at[pl.ds(width + own, width)]
    mid = pltpu.make_async_copy(cur_hbm, ext.at[pl.ds(width, own)], sem.at[1])
    band_copies = [pltpu.make_async_copy(bt_hbm.at[b], bt.at[b], sem.at[3 + b]) for b in range(blocks)]
    band_copies[0].start()
    mid.start()
    if fast:
        z = z_ref[0]
        low_r1 = pltpu.make_async_copy(r1_hbm.at[pl.ds(n_own, width)], low_dst, sem.at[0])
        low_rc = pltpu.make_async_copy(rc_hbm, low_dst, sem.at[0])
        high_r1 = pltpu.make_async_copy(r1_hbm.at[pl.ds(n_own, width)], high_dst, sem.at[2])
        high_rc = pltpu.make_async_copy(rc_hbm, high_dst, sem.at[2])

        @pl.when(z == 0)
        def _():
            low_rc.start()
            high_r1.start()

        @pl.when(z == 1)
        def _():
            low_r1.start()
            high_rc.start()

        @pl.when(z == 2)
        def _():
            low_rc.start()
            high_r1.start()

        @pl.when(z == 3)
        def _():
            low_r1.start()
            high_rc.start()

        low_wait, high_wait = low_rc, high_rc
    else:
        low_wait = pltpu.make_async_copy(low_hbm, low_dst, sem.at[0])
        high_wait = pltpu.make_async_copy(high_hbm, high_dst, sem.at[2])
        low_wait.start()
        high_wait.start()
    for b in range(1, blocks):
        band_copies[b].start()
    mid.wait()
    low_wait.wait()
    high_wait.wait()
    for b in range(blocks):
        band_copies[b].wait()
        acc = jnp.zeros((rows, out_ref.shape[1]), jnp.float32)

        def near(k):
            n = b + BW + off_ref[b * k_band + k]
            return ext[pl.ds(pl.multiple_of(n * rows, rows), rows), :]

        for k in range(0, k_band - 1, 2):
            lhs = jnp.concatenate([bt[b, k], bt[b, k + 1]], axis=1)
            rhs = jnp.concatenate([near(k), near(k + 1)], axis=0)
            acc = acc + jnp.dot(lhs, rhs, preferred_element_type=jnp.float32)
        if k_band % 2:
            acc = acc + jnp.dot(bt[b, k_band - 1], near(k_band - 1), preferred_element_type=jnp.float32)
        out_ref[pl.ds(b * rows, rows), :] = acc


def band_call(z, band_offsets, current, rim_sources, band_tiles, fast, n_own, width):
    blocks, k_band, rows, _ = band_tiles.shape
    classes = current.shape[1]
    flops = 2 * blocks * k_band * rows * rows * classes
    bytes_accessed = band_tiles.size * 2 + current.size * 2 * 2 + current.size * 4
    return pl.pallas_call(
        functools.partial(band_kernel, fast, n_own),
        cost_estimate=pl.CostEstimate(flops=flops, transcendentals=0, bytes_accessed=bytes_accessed),
        in_specs=[SMEM, SMEM] + [ANY] * (1 + len(rim_sources) + 1),
        out_specs=VMEM,
        out_shape=jax.ShapeDtypeStruct(current.shape, jnp.float32),
        scratch_shapes=[
            pltpu.VMEM((current.shape[0] + 2 * width, classes), current.dtype),
            pltpu.VMEM(band_tiles.shape, band_tiles.dtype),
            pltpu.SemaphoreType.DMA((3 + blocks,)),
        ],
    )(z, band_offsets.reshape(-1), current, *rim_sources, band_tiles)


def hub_kernel(n_hub, width, final, z_ref, hidx_ref, *rest):
    hub_hbm = rest[:n_hub]
    if final:
        (ht_hbm, band_hbm, deg_ref, seeds_hbm, out_ref, hub, ht, band, seeds, sem) = rest[n_hub:]
    else:
        (ht_hbm, band_hbm, deg_ref, seeds_hbm, pick_ref,
         cur_ref, owned_ref, p1_ref, p3_ref, pc_ref,
         hub, ht, band, seeds, sem) = rest[n_hub:]
    blocks, k_hub, rows = ht.shape[0], ht.shape[1], ht.shape[2]
    per_block = []
    for b in range(blocks):
        span = pl.ds(b * rows, rows)
        per_block.append([
            pltpu.make_async_copy(ht_hbm.at[b], ht.at[b], sem.at[n_hub + 4 * b]),
            pltpu.make_async_copy(band_hbm.at[span], band.at[span], sem.at[n_hub + 4 * b + 1]),
            pltpu.make_async_copy(seeds_hbm.at[span], seeds.at[span], sem.at[n_hub + 4 * b + 3]),
        ])
    copies = []
    at = 0
    for i, piece in enumerate(hub_hbm):
        n = piece.shape[0]
        copies.append(pltpu.make_async_copy(piece, hub.at[pl.ds(at, n)], sem.at[i]))
        at += n
    for c in copies:
        c.start()
    for c in per_block[0]:
        c.start()
    for b in range(1, blocks):
        for c in per_block[b]:
            c.start()
    by_row = jnp.transpose(deg_ref[...])
    for c in copies:
        c.wait()
    for b in range(blocks):
        for c in per_block[b]:
            c.wait()
        span = pl.ds(b * rows, rows)
        acc = jnp.zeros((rows, hub.shape[2]), jnp.float32)
        blk = lambda h: hub[hidx_ref[b * k_hub + h]]
        for h in range(0, k_hub - 1, 2):
            lhs = jnp.concatenate([ht[b, h], ht[b, h + 1]], axis=1)
            rhs = jnp.concatenate([blk(h), blk(h + 1)], axis=0)
            acc = acc + jnp.dot(lhs, rhs, preferred_element_type=jnp.float32)
        if k_hub % 2:
            acc = acc + jnp.dot(ht[b, k_hub - 1], blk(k_hub - 1), preferred_element_type=jnp.float32)
        gathered = (band[span] + acc) / by_row[:, b:b + 1]
        labels = spread_weight * gathered + (1.0 - spread_weight) * seeds[span].astype(jnp.float32)
        if final:
            out_ref[span, :] = labels
        else:
            cur_ref[span, :] = labels.astype(cur_ref.dtype)
    if final:
        return
    own = cur_ref.shape[0]
    n_own = owned_ref.shape[0]
    owned = jnp.dot(pick_ref[...], cur_ref[...], preferred_element_type=jnp.float32).astype(owned_ref.dtype)
    owned_ref[...] = owned
    p1_ref[pl.ds(0, n_own), :] = owned
    p3_ref[pl.ds(0, n_own), :] = owned
    z = z_ref[0]
    top = cur_ref[pl.ds(own - width, width), :]
    bottom = cur_ref[pl.ds(0, width), :]
    p1_ref[pl.ds(n_own, width), :] = jnp.where(z % 2 == 0, top, bottom)
    p3_ref[pl.ds(n_own, width), :] = jnp.where(z == 1, top, bottom)
    pc_ref[...] = jnp.where((z == 3) | (z == 1), top, bottom)


def hub_call(z, hub_index, pick, hub_pieces, hub_tiles, band, degree, seeds, width, final):
    blocks, k_hub, rows, _ = hub_tiles.shape
    classes = seeds.shape[1]
    n_hub = len(hub_pieces)
    n_hub_blocks = sum(p.shape[0] for p in hub_pieces)
    n_own = pick.shape[0]
    bf = jnp.bfloat16
    flops = 2 * blocks * k_hub * rows * rows * classes
    bytes_accessed = hub_tiles.size * 2 + n_hub_blocks * rows * classes * 2 + seeds.size * 4 * 4
    if final:
        outs = [jax.ShapeDtypeStruct(seeds.shape, jnp.float32)]
    else:
        outs = [
            jax.ShapeDtypeStruct(seeds.shape, bf),
            jax.ShapeDtypeStruct((n_own, classes), bf),
            jax.ShapeDtypeStruct((n_own + width, classes), bf),
            jax.ShapeDtypeStruct((n_own + width, classes), bf),
            jax.ShapeDtypeStruct((width, classes), bf),
        ]
    return pl.pallas_call(
        functools.partial(hub_kernel, n_hub, width, final),
        cost_estimate=pl.CostEstimate(flops=flops, transcendentals=0, bytes_accessed=bytes_accessed),
        in_specs=[SMEM, SMEM] + [ANY] * (n_hub + 2) + [VMEM, ANY] + ([] if final else [VMEM]),
        out_specs=[VMEM] * len(outs),
        out_shape=outs,
        scratch_shapes=[
            pltpu.VMEM((n_hub_blocks, rows, classes), bf),
            pltpu.VMEM(hub_tiles.shape, hub_tiles.dtype),
            pltpu.VMEM(seeds.shape, jnp.float32),
            pltpu.VMEM(seeds.shape, seeds.dtype),
            pltpu.SemaphoreType.DMA((n_hub + 4 * blocks,)),
        ],
    )(z, hub_index, *hub_pieces, hub_tiles, band, degree, seeds, *([] if final else [pick]))


def positions_of(hub_blocks, owned, block_rows):
    count = lax.axis_size(AXES)
    if not fast_path(owned, block_rows):
        return hub_blocks
    offs = [0]
    for group in ROUNDS_32:
        offs = offs + [o ^ m for m in group for o in offs]
    where = np.zeros(count, np.int32)
    for p, o in enumerate(offs):
        where[o] = p
    return jnp.asarray(where)[hub_blocks ^ lax.axis_index(AXES)]


def body(seed_scores, seed_mask, band_offsets, band_tiles, hub_blocks, hub_tiles, hub_rows):
    block_rows = band_tiles.shape[2]
    seeds = seed_mask.astype(jnp.float32)[:, None] * seed_scores.astype(jnp.float32)
    degree = jnp.sum(band_tiles, axis=(1, 3), dtype=jnp.float32) + jnp.sum(
        hub_tiles, axis=(1, 3), dtype=jnp.float32
    )
    lanes = degree.shape[1]
    degree = jnp.zeros((lanes, lanes), jnp.float32).at[: degree.shape[0]].set(degree)
    width = BW * block_rows
    z = lax.axis_index("hub").astype(jnp.int32).reshape(1)
    current = seeds.astype(jnp.bfloat16)
    seeds16 = current
    owned = current[hub_rows]
    p1, p3, pc = payloads(current, owned, z[0], width)
    fast = fast_path(owned, block_rows)
    pick = (hub_rows[:, None] == jnp.arange(current.shape[0], dtype=hub_rows.dtype)[None, :]).astype(jnp.bfloat16)
    prep = (pick, degree, positions_of(hub_blocks, owned, block_rows).reshape(-1))
    for step in range(ITERS):
        middle = functools.partial(
            band_call, z, band_offsets, current, band_tiles=band_tiles, fast=fast, n_own=owned.shape[0], width=width
        )
        band, hub_pieces, prep_out = exchange(
            current, owned, p1, p3, pc, hub_blocks, width, block_rows, lambda rims: middle(rims), prep
        )
        if prep is not None:
            pick, degree, hub_index = prep_out
            prep = None
        final = step + 1 == ITERS
        outs = hub_call(z, hub_index, pick, hub_pieces, hub_tiles, band, degree, seeds16, width, final)
        if final:
            labels = outs[0]
        else:
            current, owned, p1, p3, pc = outs
    return labels


def solution(mesh):
    placed = (
        P(AXES, None),
        P(AXES),
        P(AXES, None),
        P(AXES, None, None, None),
        P(AXES, None),
        P(AXES, None, None, None),
        P(AXES),
    )
    return jax.shard_map(
        body, mesh=mesh, in_specs=placed, out_specs=P(AXES, None), check_vma=False
    )
```

```python
import functools

import jax
import jax.numpy as jnp
import numpy as np
from jax import lax
from jax.experimental import pallas as pl
from jax.experimental.pallas import tpu as pltpu
from jax.sharding import PartitionSpec as P

BW = 2
ITERS = 3
AXES = ("node", "hub")
ROUNDS_32 = ((1, 2, 3), (8, 16, 24), (4,))


spread_weight = 0.8

SMEM = pl.BlockSpec(memory_space=pltpu.SMEM)
ANY = pl.BlockSpec(memory_space=pl.ANY)
VMEM = pl.BlockSpec(memory_space=pltpu.VMEM)


def fast_path(owned, block_rows):
    count = lax.axis_size(AXES)
    return count == 32 and owned.shape[0] == block_rows and lax.axis_size("hub") == 4


def payloads(current, owned, z, width):
    top = current[current.shape[0] - width:]
    bottom = current[:width]
    p1 = jnp.concatenate([owned, jnp.where(z % 2 == 0, top, bottom)], 0)
    pc = jnp.where((z == 3) | (z == 1), top, bottom)
    return p1, pc


def exchange(current, owned, p1, pc, hub_blocks, width, block_rows, middle, prep):
    count = lax.axis_size(AXES)
    if not fast_path(owned, block_rows):
        forward = [(i, i + 1) for i in range(count - 1)]
        backward = [(target, source) for source, target in forward]
        low = lax.ppermute(current[current.shape[0] - width:], AXES, forward)
        high = lax.ppermute(current[:width], AXES, backward)
        hub_all = lax.all_gather(owned, AXES, axis=0, tiled=True)
        return middle((low, high)), [hub_all.reshape(-1, block_rows, owned.shape[1])], prep
    me = lax.axis_index(AXES)
    pairs = lambda m: [(i, i ^ m) for i in range(count)]
    r3 = lax.ppermute(owned, AXES, pairs(3))
    r2 = lax.ppermute(owned, AXES, pairs(2))
    r1 = lax.ppermute(p1, AXES, pairs(1))
    groups = count // 4
    cross = [(4 * g + 3, 4 * g + 4) for g in range(groups - 1)]
    cross += [(4 * g + 4, 4 * g + 3) for g in range(groups - 1)]
    cross += [(4 * g + 1, 4 * g + 2) for g in range(groups)] + [(4 * g + 2, 4 * g + 1) for g in range(groups)]
    rc = lax.ppermute(pc, AXES, cross)
    if prep is not None:
        (r1, r2, r3, rc), prep = lax.optimization_barrier(((r1, r2, r3, rc), prep))
    rows = block_rows
    buf = jnp.concatenate([owned[None], r1[None, :rows], r2[None], r3[None]], 0)
    offs = [0, 1, 2, 3]
    rounds = ROUNDS_32
    pieces = [buf]
    done = None
    for r, group in enumerate(rounds[1:]):
        sent = {m: lax.ppermute(buf, AXES, pairs(m)) for m in sorted(group, key=lambda m: -m)}
        recvs = [sent[m] for m in group]
        if done is None:
            done, recvs = lax.optimization_barrier((middle((r1, r3, rc)), recvs))
        offs = offs + [o ^ m for m in group for o in offs]
        pieces = [buf] + recvs
        if r + 2 < len(rounds):
            buf = jnp.concatenate(pieces, 0)
    assert sorted(offs) == list(range(count))
    where = np.zeros(count, np.int32)
    for p, o in enumerate(offs):
        where[o] = p
    return done, pieces, prep


def band_kernel(fast, n_own, z_ref, off_ref, cur_hbm, *rest):
    if fast:
        r1_hbm, r3_hbm, rc_hbm, bt_hbm, out_ref, ext, bt, sem = rest
    else:
        low_hbm, high_hbm, bt_hbm, out_ref, ext, bt, sem = rest
    blocks, k_band, rows = bt.shape[0], bt.shape[1], bt.shape[2]
    own = cur_hbm.shape[0]
    width = (ext.shape[0] - own) // 2
    low_dst = ext.at[pl.ds(0, width)]
    high_dst = ext.at[pl.ds(width + own, width)]
    mid = pltpu.make_async_copy(cur_hbm, ext.at[pl.ds(width, own)], sem.at[1])
    band_copies = [pltpu.make_async_copy(bt_hbm.at[b], bt.at[b], sem.at[3 + b]) for b in range(blocks)]
    band_copies[0].start()
    mid.start()
    if fast:
        z = z_ref[0]
        low_r1 = pltpu.make_async_copy(r1_hbm.at[pl.ds(n_own, width)], low_dst, sem.at[0])
        low_rc = pltpu.make_async_copy(rc_hbm, low_dst, sem.at[0])
        high_r1 = pltpu.make_async_copy(r1_hbm.at[pl.ds(n_own, width)], high_dst, sem.at[2])
        high_rc = pltpu.make_async_copy(rc_hbm, high_dst, sem.at[2])

        @pl.when(z == 0)
        def _():
            low_rc.start()
            high_r1.start()

        @pl.when(z == 1)
        def _():
            low_r1.start()
            high_rc.start()

        @pl.when(z == 2)
        def _():
            low_rc.start()
            high_r1.start()

        @pl.when(z == 3)
        def _():
            low_r1.start()
            high_rc.start()

        low_wait, high_wait = low_rc, high_rc
    else:
        low_wait = pltpu.make_async_copy(low_hbm, low_dst, sem.at[0])
        high_wait = pltpu.make_async_copy(high_hbm, high_dst, sem.at[2])
        low_wait.start()
        high_wait.start()
    for b in range(1, blocks):
        band_copies[b].start()
    mid.wait()
    low_wait.wait()
    high_wait.wait()
    for b in range(blocks):
        band_copies[b].wait()
        acc = jnp.zeros((rows, out_ref.shape[1]), jnp.float32)

        def near(k):
            n = b + BW + off_ref[b * k_band + k]
            return ext[pl.ds(pl.multiple_of(n * rows, rows), rows), :]

        for k in range(0, k_band - 1, 2):
            lhs = jnp.concatenate([bt[b, k], bt[b, k + 1]], axis=1)
            rhs = jnp.concatenate([near(k), near(k + 1)], axis=0)
            acc = acc + jnp.dot(lhs, rhs, preferred_element_type=jnp.float32)
        if k_band % 2:
            acc = acc + jnp.dot(bt[b, k_band - 1], near(k_band - 1), preferred_element_type=jnp.float32)
        out_ref[pl.ds(b * rows, rows), :] = acc


def band_call(z, band_offsets, current, rim_sources, band_tiles, fast, n_own, width):
    blocks, k_band, rows, _ = band_tiles.shape
    classes = current.shape[1]
    flops = 2 * blocks * k_band * rows * rows * classes
    bytes_accessed = band_tiles.size * 2 + current.size * 2 * 2 + current.size * 4
    return pl.pallas_call(
        functools.partial(band_kernel, fast, n_own),
        cost_estimate=pl.CostEstimate(flops=flops, transcendentals=0, bytes_accessed=bytes_accessed),
        in_specs=[SMEM, SMEM] + [ANY] * (1 + len(rim_sources) + 1),
        out_specs=VMEM,
        out_shape=jax.ShapeDtypeStruct(current.shape, jnp.float32),
        scratch_shapes=[
            pltpu.VMEM((current.shape[0] + 2 * width, classes), current.dtype),
            pltpu.VMEM(band_tiles.shape, band_tiles.dtype),
            pltpu.SemaphoreType.DMA((3 + blocks,)),
        ],
    )(z, band_offsets.reshape(-1), current, *rim_sources, band_tiles)


def hub_kernel(n_hub, width, final, z_ref, hidx_ref, *rest):
    hub_hbm = rest[:n_hub]
    if final:
        (ht_hbm, band_hbm, deg_ref, seeds_hbm, out_ref, hub, ht, band, seeds, sem) = rest[n_hub:]
    else:
        (ht_hbm, band_hbm, deg_ref, seeds_hbm, pick_ref,
         cur_ref, owned_ref, p1_ref, pc_ref,
         hub, ht, band, seeds, sem) = rest[n_hub:]
    blocks, k_hub, rows = ht.shape[0], ht.shape[1], ht.shape[2]
    per_block = []
    for b in range(blocks):
        span = pl.ds(b * rows, rows)
        per_block.append([
            pltpu.make_async_copy(ht_hbm.at[b], ht.at[b], sem.at[n_hub + 4 * b]),
            pltpu.make_async_copy(band_hbm.at[span], band.at[span], sem.at[n_hub + 4 * b + 1]),
            pltpu.make_async_copy(seeds_hbm.at[span], seeds.at[span], sem.at[n_hub + 4 * b + 3]),
        ])
    copies = []
    at = 0
    for i, piece in enumerate(hub_hbm):
        n = piece.shape[0]
        copies.append(pltpu.make_async_copy(piece, hub.at[pl.ds(at, n)], sem.at[i]))
        at += n
    for c in copies:
        c.start()
    for c in per_block[0]:
        c.start()
    for b in range(1, blocks):
        for c in per_block[b]:
            c.start()
    by_row = jnp.transpose(deg_ref[...])
    for c in copies:
        c.wait()
    for b in range(blocks):
        for c in per_block[b]:
            c.wait()
        span = pl.ds(b * rows, rows)
        acc = jnp.zeros((rows, hub.shape[2]), jnp.float32)
        blk = lambda h: hub[hidx_ref[b * k_hub + h]]
        for h in range(0, k_hub - 1, 2):
            lhs = jnp.concatenate([ht[b, h], ht[b, h + 1]], axis=1)
            rhs = jnp.concatenate([blk(h), blk(h + 1)], axis=0)
            acc = acc + jnp.dot(lhs, rhs, preferred_element_type=jnp.float32)
        if k_hub % 2:
            acc = acc + jnp.dot(ht[b, k_hub - 1], blk(k_hub - 1), preferred_element_type=jnp.float32)
        gathered = (band[span] + acc) / by_row[:, b:b + 1]
        labels = spread_weight * gathered + (1.0 - spread_weight) * seeds[span].astype(jnp.float32)
        if final:
            out_ref[span, :] = labels
        else:
            cur_ref[span, :] = labels.astype(cur_ref.dtype)
    if final:
        return
    own = cur_ref.shape[0]
    n_own = owned_ref.shape[0]
    owned = jnp.dot(pick_ref[...], cur_ref[...], preferred_element_type=jnp.float32).astype(owned_ref.dtype)
    owned_ref[...] = owned
    p1_ref[pl.ds(0, n_own), :] = owned
    z = z_ref[0]
    top = cur_ref[pl.ds(own - width, width), :]
    bottom = cur_ref[pl.ds(0, width), :]
    p1_ref[pl.ds(n_own, width), :] = jnp.where(z % 2 == 0, top, bottom)
    pc_ref[...] = jnp.where((z == 3) | (z == 1), top, bottom)


def hub_call(z, hub_index, pick, hub_pieces, hub_tiles, band, degree, seeds, width, final):
    blocks, k_hub, rows, _ = hub_tiles.shape
    classes = seeds.shape[1]
    n_hub = len(hub_pieces)
    n_hub_blocks = sum(p.shape[0] for p in hub_pieces)
    n_own = pick.shape[0]
    bf = jnp.bfloat16
    flops = 2 * blocks * k_hub * rows * rows * classes
    bytes_accessed = hub_tiles.size * 2 + n_hub_blocks * rows * classes * 2 + seeds.size * 4 * 4
    if final:
        outs = [jax.ShapeDtypeStruct(seeds.shape, jnp.float32)]
    else:
        outs = [
            jax.ShapeDtypeStruct(seeds.shape, bf),
            jax.ShapeDtypeStruct((n_own, classes), bf),
            jax.ShapeDtypeStruct((n_own + width, classes), bf),
            jax.ShapeDtypeStruct((width, classes), bf),
        ]
    return pl.pallas_call(
        functools.partial(hub_kernel, n_hub, width, final),
        cost_estimate=pl.CostEstimate(flops=flops, transcendentals=0, bytes_accessed=bytes_accessed),
        in_specs=[SMEM, SMEM] + [ANY] * (n_hub + 2) + [VMEM, ANY] + ([] if final else [VMEM]),
        out_specs=[VMEM] * len(outs),
        out_shape=outs,
        scratch_shapes=[
            pltpu.VMEM((n_hub_blocks, rows, classes), bf),
            pltpu.VMEM(hub_tiles.shape, hub_tiles.dtype),
            pltpu.VMEM(seeds.shape, jnp.float32),
            pltpu.VMEM(seeds.shape, seeds.dtype),
            pltpu.SemaphoreType.DMA((n_hub + 4 * blocks,)),
        ],
    )(z, hub_index, *hub_pieces, hub_tiles, band, degree, seeds, *([] if final else [pick]))


def positions_of(hub_blocks, owned, block_rows):
    count = lax.axis_size(AXES)
    if not fast_path(owned, block_rows):
        return hub_blocks
    offs = [0]
    for group in ROUNDS_32:
        offs = offs + [o ^ m for m in group for o in offs]
    where = np.zeros(count, np.int32)
    for p, o in enumerate(offs):
        where[o] = p
    return jnp.asarray(where)[hub_blocks ^ lax.axis_index(AXES)]


def body(seed_scores, seed_mask, band_offsets, band_tiles, hub_blocks, hub_tiles, hub_rows):
    block_rows = band_tiles.shape[2]
    seeds = seed_mask.astype(jnp.float32)[:, None] * seed_scores.astype(jnp.float32)
    degree = jnp.sum(band_tiles, axis=(1, 3), dtype=jnp.float32) + jnp.sum(
        hub_tiles, axis=(1, 3), dtype=jnp.float32
    )
    lanes = degree.shape[1]
    degree = jnp.zeros((lanes, lanes), jnp.float32).at[: degree.shape[0]].set(degree)
    width = BW * block_rows
    z = lax.axis_index("hub").astype(jnp.int32).reshape(1)
    current = seeds.astype(jnp.bfloat16)
    seeds16 = current
    owned = current[hub_rows]
    p1, pc = payloads(current, owned, z[0], width)
    fast = fast_path(owned, block_rows)
    pick = (hub_rows[:, None] == jnp.arange(current.shape[0], dtype=hub_rows.dtype)[None, :]).astype(jnp.bfloat16)
    prep = (pick, degree, positions_of(hub_blocks, owned, block_rows).reshape(-1))
    for step in range(ITERS):
        middle = functools.partial(
            band_call, z, band_offsets, current, band_tiles=band_tiles, fast=fast, n_own=owned.shape[0], width=width
        )
        band, hub_pieces, prep_out = exchange(
            current, owned, p1, pc, hub_blocks, width, block_rows, lambda rims: middle(rims), prep
        )
        if prep is not None:
            pick, degree, hub_index = prep_out
            prep = None
        final = step + 1 == ITERS
        outs = hub_call(z, hub_index, pick, hub_pieces, hub_tiles, band, degree, seeds16, width, final)
        if final:
            labels = outs[0]
        else:
            current, owned, p1, pc = outs
    return labels


def solution(mesh):
    placed = (
        P(AXES, None),
        P(AXES),
        P(AXES, None),
        P(AXES, None, None, None),
        P(AXES, None),
        P(AXES, None, None, None),
        P(AXES),
    )
    return jax.shard_map(
        body, mesh=mesh, in_specs=placed, out_specs=P(AXES, None), check_vma=False
    )
```

```python
import functools

import jax
import jax.numpy as jnp
import numpy as np
from jax import lax
from jax.experimental import pallas as pl
from jax.experimental.pallas import tpu as pltpu
from jax.sharding import PartitionSpec as P

BW = 2
ITERS = 3
AXES = ("node", "hub")
ROUNDS_32 = ((1, 2, 3), (8, 16, 24), (4,))


spread_weight = 0.8

SMEM = pl.BlockSpec(memory_space=pltpu.SMEM)
ANY = pl.BlockSpec(memory_space=pl.ANY)
VMEM = pl.BlockSpec(memory_space=pltpu.VMEM)


def fast_path(owned, block_rows):
    count = lax.axis_size(AXES)
    return count == 32 and owned.shape[0] == block_rows and lax.axis_size("hub") == 4


def payloads(current, owned, z, width):
    top = current[current.shape[0] - width:]
    bottom = current[:width]
    p1 = jnp.concatenate([owned, jnp.where(z % 2 == 0, top, bottom)], 0)
    pc = jnp.where((z == 3) | (z == 1), top, bottom)
    return p1, pc


def exchange(current, owned, p1, pc, hub_blocks, width, block_rows, middle, prep):
    count = lax.axis_size(AXES)
    if not fast_path(owned, block_rows):
        forward = [(i, i + 1) for i in range(count - 1)]
        backward = [(target, source) for source, target in forward]
        low = lax.ppermute(current[current.shape[0] - width:], AXES, forward)
        high = lax.ppermute(current[:width], AXES, backward)
        hub_all = lax.all_gather(owned, AXES, axis=0, tiled=True)
        return middle((low, high)), [hub_all.reshape(-1, block_rows, owned.shape[1])], prep
    me = lax.axis_index(AXES)
    pairs = lambda m: [(i, i ^ m) for i in range(count)]
    r3 = lax.ppermute(owned, AXES, pairs(3))
    r2 = lax.ppermute(owned, AXES, pairs(2))
    r1 = lax.ppermute(p1, AXES, pairs(1))
    groups = count // 4
    cross = [(4 * g + 3, 4 * g + 4) for g in range(groups - 1)]
    cross += [(4 * g + 4, 4 * g + 3) for g in range(groups - 1)]
    cross += [(4 * g + 1, 4 * g + 2) for g in range(groups)] + [(4 * g + 2, 4 * g + 1) for g in range(groups)]
    rc = lax.ppermute(pc, AXES, cross)
    if prep is not None:
        (r1, r2, r3, rc), prep = lax.optimization_barrier(((r1, r2, r3, rc), prep))
    rows = block_rows
    buf = jnp.concatenate([owned[None], r1[None, :rows], r2[None], r3[None]], 0)
    offs = [0, 1, 2, 3]
    rounds = ROUNDS_32
    pieces = [buf]
    done = None
    for r, group in enumerate(rounds[1:]):
        sent = {m: lax.ppermute(buf, AXES, pairs(m)) for m in sorted(group, key=lambda m: -m)}
        recvs = [sent[m] for m in group]
        if done is None:
            done, recvs = lax.optimization_barrier((middle((r1, rc)), recvs))
        offs = offs + [o ^ m for m in group for o in offs]
        pieces = [buf] + recvs
        if r + 2 < len(rounds):
            buf = jnp.concatenate(pieces, 0)
    assert sorted(offs) == list(range(count))
    where = np.zeros(count, np.int32)
    for p, o in enumerate(offs):
        where[o] = p
    return done, pieces, prep


def band_kernel(fast, n_own, z_ref, off_ref, cur_hbm, *rest):
    if fast:
        r1_hbm, rc_hbm, bt_hbm, out_ref, ext, bt, sem = rest
    else:
        low_hbm, high_hbm, bt_hbm, out_ref, ext, bt, sem = rest
    blocks, k_band, rows = bt.shape[0], bt.shape[1], bt.shape[2]
    own = cur_hbm.shape[0]
    width = (ext.shape[0] - own) // 2
    low_dst = ext.at[pl.ds(0, width)]
    high_dst = ext.at[pl.ds(width + own, width)]
    mid = pltpu.make_async_copy(cur_hbm, ext.at[pl.ds(width, own)], sem.at[1])
    band_copies = [pltpu.make_async_copy(bt_hbm.at[b], bt.at[b], sem.at[3 + b]) for b in range(blocks)]
    band_copies[0].start()
    mid.start()
    if fast:
        z = z_ref[0]
        low_r1 = pltpu.make_async_copy(r1_hbm.at[pl.ds(n_own, width)], low_dst, sem.at[0])
        low_rc = pltpu.make_async_copy(rc_hbm, low_dst, sem.at[0])
        high_r1 = pltpu.make_async_copy(r1_hbm.at[pl.ds(n_own, width)], high_dst, sem.at[2])
        high_rc = pltpu.make_async_copy(rc_hbm, high_dst, sem.at[2])

        @pl.when(z == 0)
        def _():
            low_rc.start()
            high_r1.start()

        @pl.when(z == 1)
        def _():
            low_r1.start()
            high_rc.start()

        @pl.when(z == 2)
        def _():
            low_rc.start()
            high_r1.start()

        @pl.when(z == 3)
        def _():
            low_r1.start()
            high_rc.start()

        low_wait, high_wait = low_rc, high_rc
    else:
        low_wait = pltpu.make_async_copy(low_hbm, low_dst, sem.at[0])
        high_wait = pltpu.make_async_copy(high_hbm, high_dst, sem.at[2])
        low_wait.start()
        high_wait.start()
    for b in range(1, blocks):
        band_copies[b].start()
    mid.wait()
    low_wait.wait()
    high_wait.wait()
    for b in range(blocks):
        band_copies[b].wait()
        acc = jnp.zeros((rows, out_ref.shape[1]), jnp.float32)

        def near(k):
            n = b + BW + off_ref[b * k_band + k]
            return ext[pl.ds(pl.multiple_of(n * rows, rows), rows), :]

        for k in range(0, k_band - 1, 2):
            lhs = jnp.concatenate([bt[b, k], bt[b, k + 1]], axis=1)
            rhs = jnp.concatenate([near(k), near(k + 1)], axis=0)
            acc = acc + jnp.dot(lhs, rhs, preferred_element_type=jnp.float32)
        if k_band % 2:
            acc = acc + jnp.dot(bt[b, k_band - 1], near(k_band - 1), preferred_element_type=jnp.float32)
        out_ref[pl.ds(b * rows, rows), :] = acc


def band_call(z, band_offsets, current, rim_sources, band_tiles, fast, n_own, width):
    blocks, k_band, rows, _ = band_tiles.shape
    classes = current.shape[1]
    flops = 2 * blocks * k_band * rows * rows * classes
    bytes_accessed = band_tiles.size * 2 + current.size * 2 * 2 + current.size * 4
    return pl.pallas_call(
        functools.partial(band_kernel, fast, n_own),
        cost_estimate=pl.CostEstimate(flops=flops, transcendentals=0, bytes_accessed=bytes_accessed),
        in_specs=[SMEM, SMEM] + [ANY] * (1 + len(rim_sources) + 1),
        out_specs=VMEM,
        out_shape=jax.ShapeDtypeStruct(current.shape, jnp.float32),
        scratch_shapes=[
            pltpu.VMEM((current.shape[0] + 2 * width, classes), current.dtype),
            pltpu.VMEM(band_tiles.shape, band_tiles.dtype),
            pltpu.SemaphoreType.DMA((3 + blocks,)),
        ],
    )(z, band_offsets.reshape(-1), current, *rim_sources, band_tiles)


def hub_kernel(n_hub, width, final, z_ref, hidx_ref, *rest):
    hub_hbm = rest[:n_hub]
    if final:
        (ht_hbm, band_hbm, deg_ref, seeds_hbm, out_ref, hub, ht, band, seeds, sem) = rest[n_hub:]
    else:
        (ht_hbm, band_hbm, deg_ref, seeds_hbm, pick_ref,
         cur_ref, owned_ref, p1_ref, pc_ref,
         hub, ht, band, seeds, sem) = rest[n_hub:]
    blocks, k_hub, rows = ht.shape[0], ht.shape[1], ht.shape[2]
    per_block = []
    for b in range(blocks):
        span = pl.ds(b * rows, rows)
        per_block.append([
            pltpu.make_async_copy(ht_hbm.at[b], ht.at[b], sem.at[n_hub + 4 * b]),
            pltpu.make_async_copy(band_hbm.at[span], band.at[span], sem.at[n_hub + 4 * b + 1]),
            pltpu.make_async_copy(seeds_hbm.at[span], seeds.at[span], sem.at[n_hub + 4 * b + 3]),
        ])
    copies = []
    at = 0
    for i, piece in enumerate(hub_hbm):
        n = piece.shape[0]
        copies.append(pltpu.make_async_copy(piece, hub.at[pl.ds(at, n)], sem.at[i]))
        at += n
    for c in copies:
        c.start()
    for c in per_block[0]:
        c.start()
    for b in range(1, blocks):
        for c in per_block[b]:
            c.start()
    by_row = jnp.transpose(deg_ref[...])
    for c in copies:
        c.wait()
    for b in range(blocks):
        for c in per_block[b]:
            c.wait()
        span = pl.ds(b * rows, rows)
        acc = jnp.zeros((rows, hub.shape[2]), jnp.float32)
        blk = lambda h: hub[hidx_ref[b * k_hub + h]]
        for h in range(0, k_hub - 1, 2):
            lhs = jnp.concatenate([ht[b, h], ht[b, h + 1]], axis=1)
            rhs = jnp.concatenate([blk(h), blk(h + 1)], axis=0)
            acc = acc + jnp.dot(lhs, rhs, preferred_element_type=jnp.float32)
        if k_hub % 2:
            acc = acc + jnp.dot(ht[b, k_hub - 1], blk(k_hub - 1), preferred_element_type=jnp.float32)
        gathered = (band[span] + acc) / by_row[:, b:b + 1]
        labels = spread_weight * gathered + (1.0 - spread_weight) * seeds[span].astype(jnp.float32)
        if final:
            out_ref[span, :] = labels
        else:
            cur_ref[span, :] = labels.astype(cur_ref.dtype)
    if final:
        return
    own = cur_ref.shape[0]
    n_own = owned_ref.shape[0]
    owned = jnp.dot(pick_ref[...], cur_ref[...], preferred_element_type=jnp.float32).astype(owned_ref.dtype)
    owned_ref[...] = owned
    p1_ref[pl.ds(0, n_own), :] = owned
    z = z_ref[0]
    top = cur_ref[pl.ds(own - width, width), :]
    bottom = cur_ref[pl.ds(0, width), :]
    p1_ref[pl.ds(n_own, width), :] = jnp.where(z % 2 == 0, top, bottom)
    pc_ref[...] = jnp.where((z == 3) | (z == 1), top, bottom)


def hub_call(z, hub_index, pick, hub_pieces, hub_tiles, band, degree, seeds, width, final):
    blocks, k_hub, rows, _ = hub_tiles.shape
    classes = seeds.shape[1]
    n_hub = len(hub_pieces)
    n_hub_blocks = sum(p.shape[0] for p in hub_pieces)
    n_own = pick.shape[0]
    bf = jnp.bfloat16
    flops = 2 * blocks * k_hub * rows * rows * classes
    bytes_accessed = hub_tiles.size * 2 + n_hub_blocks * rows * classes * 2 + seeds.size * 4 * 4
    if final:
        outs = [jax.ShapeDtypeStruct(seeds.shape, jnp.float32)]
    else:
        outs = [
            jax.ShapeDtypeStruct(seeds.shape, bf),
            jax.ShapeDtypeStruct((n_own, classes), bf),
            jax.ShapeDtypeStruct((n_own + width, classes), bf),
            jax.ShapeDtypeStruct((width, classes), bf),
        ]
    return pl.pallas_call(
        functools.partial(hub_kernel, n_hub, width, final),
        cost_estimate=pl.CostEstimate(flops=flops, transcendentals=0, bytes_accessed=bytes_accessed),
        in_specs=[SMEM, SMEM] + [ANY] * (n_hub + 2) + [VMEM, ANY] + ([] if final else [VMEM]),
        out_specs=[VMEM] * len(outs),
        out_shape=outs,
        scratch_shapes=[
            pltpu.VMEM((n_hub_blocks, rows, classes), bf),
            pltpu.VMEM(hub_tiles.shape, hub_tiles.dtype),
            pltpu.VMEM(seeds.shape, jnp.float32),
            pltpu.VMEM(seeds.shape, seeds.dtype),
            pltpu.SemaphoreType.DMA((n_hub + 4 * blocks,)),
        ],
    )(z, hub_index, *hub_pieces, hub_tiles, band, degree, seeds, *([] if final else [pick]))


def positions_of(hub_blocks, owned, block_rows):
    count = lax.axis_size(AXES)
    if not fast_path(owned, block_rows):
        return hub_blocks
    offs = [0]
    for group in ROUNDS_32:
        offs = offs + [o ^ m for m in group for o in offs]
    where = np.zeros(count, np.int32)
    for p, o in enumerate(offs):
        where[o] = p
    return jnp.asarray(where)[hub_blocks ^ lax.axis_index(AXES)]


def body(seed_scores, seed_mask, band_offsets, band_tiles, hub_blocks, hub_tiles, hub_rows):
    block_rows = band_tiles.shape[2]
    seeds = seed_mask.astype(jnp.float32)[:, None] * seed_scores.astype(jnp.float32)
    degree = jnp.sum(band_tiles, axis=(1, 3), dtype=jnp.float32) + jnp.sum(
        hub_tiles, axis=(1, 3), dtype=jnp.float32
    )
    lanes = degree.shape[1]
    degree = jnp.zeros((lanes, lanes), jnp.float32).at[: degree.shape[0]].set(degree)
    width = BW * block_rows
    z = lax.axis_index("hub").astype(jnp.int32).reshape(1)
    current = seeds.astype(jnp.bfloat16)
    seeds16 = current
    owned = current[hub_rows]
    p1, pc = payloads(current, owned, z[0], width)
    fast = fast_path(owned, block_rows)
    pick = (hub_rows[:, None] == jnp.arange(current.shape[0], dtype=hub_rows.dtype)[None, :]).astype(jnp.bfloat16)
    prep = (pick, degree, positions_of(hub_blocks, owned, block_rows).reshape(-1))
    for step in range(ITERS):
        middle = functools.partial(
            band_call, z, band_offsets, current, band_tiles=band_tiles, fast=fast, n_own=owned.shape[0], width=width
        )
        band, hub_pieces, prep_out = exchange(
            current, owned, p1, pc, hub_blocks, width, block_rows, lambda rims: middle(rims), prep
        )
        if prep is not None:
            pick, degree, hub_index = prep_out
            prep = None
        final = step + 1 == ITERS
        outs = hub_call(z, hub_index, pick, hub_pieces, hub_tiles, band, degree, seeds16, width, final)
        if final:
            labels = outs[0]
        else:
            current, owned, p1, pc = outs
    return labels


def solution(mesh):
    placed = (
        P(AXES, None),
        P(AXES),
        P(AXES, None),
        P(AXES, None, None, None),
        P(AXES, None),
        P(AXES, None, None, None),
        P(AXES),
    )
    return jax.shard_map(
        body, mesh=mesh, in_specs=placed, out_specs=P(AXES, None), check_vma=False
    )
```
